256 devices in a mesh: head: 8 (over z), ctx: 32 (over x, y, core).
Axes of the slice: x: 4, y: 4, z: 8, core: 2. Of those that a mesh axis runs over, the one named last changes fastest.
Arguments:
- queries: bfloat16 [16384, 4096], P('ctx', 'head'), may hold values from -100 to 100
- keys: bfloat16 [16384, 4096], P('ctx', 'head'), may hold values from -100 to 100
- values: bfloat16 [16384, 4096], P('ctx', 'head'), may hold values from -4 to 4
- out_grad: bfloat16 [16384, 4096], P('ctx', 'head'), may hold values from -6 to 6
- q_gain: float32 [4096], P('head'), may hold values from 0.1 to 1.9
- k_gain: float32 [4096], P('head'), may hold values from 0.1 to 1.9
- signs: int32 [2, 128, 16], replicated, may hold values from 0 to 1
Outputs:
- attended: bfloat16 [16384, 4096], P('ctx', 'head')
- q_grad: bfloat16 [16384, 4096], P('ctx', 'head')
- k_grad: bfloat16 [16384, 4096], P('ctx', 'head')
- v_grad: bfloat16 [16384, 4096], P('ctx', 'head')
The draws below stay inside these ranges and needn't reach their ends.
All inputs are finite; a program needn't handle non-finite values.
Results may differ from the reference program's by a relative error of at most 0.012.
The reference program's roundings to bfloat16 on the way (of `sign_pair`, `weights`, `state_half`, `score_grad` and `later_half`) count: a program that leaves them out, or rounds other values in their place, can miss the bound.
Values sent between devices are 32-bit elements; how exact they have to be, the bound alone decides.
No kernel may reach another device: no remote copies, remote signals or barrier semaphores. Data moves between devices by JAX's collectives and lax.ppermute only.
A program may use at most 128 MiB of HBM per device.

```python
import math
import jax
import jax.numpy as jnp
from jax import lax

HEADS = 32
DH = 128
RS = 16
BLOCK = 256
TOKENS = 16384


def shared_field(key):
    key_freq, key_phase = jax.random.split(jax.random.fold_in(key, 5))
    col_count = HEADS * DH
    frequency = jax.random.uniform(key_freq, (1, col_count), dtype=jnp.float32, minval=0.2 / BLOCK, maxval=2.0 / BLOCK)
    phase_shift = jax.random.uniform(key_phase, (1, col_count), dtype=jnp.float32, minval=-math.pi, maxval=math.pi)
    position = jnp.arange(TOKENS, dtype=jnp.float32)[:, None]
    return math.sqrt(2.0) * jnp.sin(2.0 * math.pi * frequency * position + phase_shift)


def scaled_field(key, shared):
    key_base, key_rows = jax.random.split(key, 2)
    col_count = HEADS * DH
    col_scale = 0.6 * jnp.exp(math.log(3.0) * jnp.arange(col_count, dtype=jnp.float32) / (col_count - 1))
    row_scale = jnp.exp(math.log(10.0) * jax.random.uniform(key_rows, (TOKENS, 1), dtype=jnp.float32))
    own_draw = jnp.clip(jax.random.normal(key_base, (TOKENS, col_count), dtype=jnp.float32), -5.0, 5.0)
    base_draw = 0.85 * shared + 0.5 * own_draw
    return base_draw * col_scale[None, :] * row_scale


def draw_queries(key, part):
    return scaled_field(jax.random.fold_in(key, 11), shared_field(key)).astype(jnp.bfloat16)


def draw_keys(key, part):
    return scaled_field(jax.random.fold_in(key, 23), shared_field(key)).astype(jnp.bfloat16)


def draw_values(key, part):
    key_noise, key_amp, key_freq, key_shift, key_local = jax.random.split(jax.random.fold_in(key, 37), 5)
    key_lamp, key_lfreq, key_lshift = jax.random.split(key_local, 3)
    col_count = HEADS * DH
    position = jnp.arange(TOKENS, dtype=jnp.float32)[:, None]
    amplitude = jax.random.uniform(key_amp, (1, col_count), dtype=jnp.float32, minval=0.4, maxval=1.2)
    frequency = jax.random.uniform(key_freq, (1, col_count), dtype=jnp.float32, minval=0.5, maxval=3.0)
    phase_shift = jax.random.uniform(key_shift, (1, col_count), dtype=jnp.float32, minval=-math.pi, maxval=math.pi)
    trend = amplitude * jnp.sin(2.0 * math.pi * frequency * position / TOKENS + phase_shift)
    local_amp = jax.random.uniform(key_lamp, (1, col_count), dtype=jnp.float32, minval=0.3, maxval=0.8)
    local_freq = jax.random.uniform(key_lfreq, (1, col_count), dtype=jnp.float32, minval=0.25 / BLOCK, maxval=1.0 / BLOCK)
    local_shift = jax.random.uniform(key_lshift, (1, col_count), dtype=jnp.float32, minval=-math.pi, maxval=math.pi)
    local_wave = local_amp * jnp.sin(2.0 * math.pi * local_freq * position + local_shift)
    noise = 0.6 * jnp.clip(jax.random.normal(key_noise, (TOKENS, col_count), dtype=jnp.float32), -3.0, 3.0)
    return (trend + local_wave + noise).astype(jnp.bfloat16)


def plant(result, stream_key, least, largest):
    longest = result.shape.index(max(result.shape))
    spots = []
    for shift in (0, 1):
        where = [jax.random.randint(jax.random.fold_in(stream_key, axis), (), 0, length) for axis, length in enumerate(result.shape)]
        where[longest] = (where[longest] + shift) % result.shape[longest]
        spots.append(tuple(where))
    return result.at[spots[0]].set(least).at[spots[1]].set(largest)


def block_levels(rng, dims, cuts, least, high):
    def one(dim, parts):
        draws = jax.random.uniform(jax.random.fold_in(jax.random.fold_in(rng, 6), dim), (parts,), jnp.float32, least / len(cuts), high / len(cuts))
        return jnp.repeat(jnp.exp(draws), dims[dim] // parts).reshape((-1,) + (1,) * (len(dims) - dim - 1))

    level = one(*cuts[0])
    for cut in cuts[1:]:
        level = level * one(*cut)
    return level


def bell_draw(key, extent, scale, reach, pieces=(), held_as=jnp.bfloat16):
    factor_of = block_levels(key, extent, pieces, -0.22, 0.18) if pieces else 1.0
    entries = jax.random.normal(key, extent, jnp.float32) * scale * factor_of
    return jnp.minimum(jnp.maximum(entries, -reach), reach).astype(held_as)


def setup_inputs(seed: int = 0) -> dict:
    key_list = jax.random.split(jax.random.key(seed), 8)
    return {
        "queries": draw_queries(jax.random.fold_in(key_list[7], 71), 0),
        "keys": draw_keys(jax.random.fold_in(key_list[7], 71), 0),
        "values": draw_values(jax.random.fold_in(key_list[7], 71), 0),
        "out_grad": bell_draw(key_list[3], (TOKENS, HEADS * DH), 1.0, 6.0, ((0, 32), (1, 8))),
        "q_gain": jnp.clip(1.0 + 0.18 * jax.random.normal(key_list[4], (HEADS * DH,), jnp.float32), 0.1, 1.9),
        "k_gain": jnp.clip(1.0 + 0.18 * jax.random.normal(key_list[5], (HEADS * DH,), jnp.float32), 0.1, 1.9),
        "signs": plant(jax.random.randint(key_list[6], (2, DH, RS), 0, 2), jax.random.fold_in(key_list[6], 1), 0, 1).astype(jnp.int32),
    }


EPSILON = 1e-06
HIGHEST_PREC = lax.Precision.HIGHEST

def product_of(spec, lhs, rhs):
    return jnp.einsum(spec, lhs.astype(jnp.float32), rhs.astype(jnp.float32))

def precise_product(spec, lhs, rhs):
    return jnp.einsum(spec, lhs.astype(jnp.float32), rhs.astype(jnp.float32), precision=HIGHEST_PREC)

def causal_mask():
    row_ids = lax.broadcasted_iota(jnp.int32, (BLOCK, BLOCK), 0)
    col_ids = lax.broadcasted_iota(jnp.int32, (BLOCK, BLOCK), 1)
    return row_ids >= col_ids

def sketch(inputs, sign_pair):
    projected = product_of('...d,dr->...r', inputs, sign_pair)
    left_part = projected[..., :RS]
    right_part = projected[..., RS:]
    sketched = left_part * right_part * (RS * DH) ** (-0.5)
    outer_prod = sketched[..., :, None] * sketched[..., None, :]
    sketch_feats = outer_prod.reshape(sketched.shape[:-1] + (RS * RS,)).astype(jnp.bfloat16)
    return (sketch_feats, sketched, left_part, right_part)

def sketch_back(feat_grad, sketched, left_part, right_part, sign_pair):
    grid = feat_grad.reshape(feat_grad.shape[:-1] + (RS, RS))
    symmetric = grid + jnp.swapaxes(grid, -1, -2)
    sketch_grad = lax.optimization_barrier(jnp.sum(symmetric * sketched[..., None, :], axis=-1))
    both_grad = jnp.concatenate([sketch_grad * right_part, sketch_grad * left_part], axis=-1) * (RS * DH) ** (-0.5)
    return precise_product('...r,dr->...d', both_grad, sign_pair)

def forward_blocks(q_normed, k_normed, values, sign_pair):
    scores = product_of('...id,...jd->...ij', q_normed, k_normed) * DH ** (-0.5)
    weights = jnp.where(causal_mask(), scores ** 4, 0.0).astype(jnp.bfloat16)
    q_parts = sketch(q_normed, sign_pair)
    k_parts = sketch(k_normed, sign_pair)
    block_kv = product_of('...jr,...jd->...rd', k_parts[0], values)
    block_keys = lax.optimization_barrier(jnp.sum(k_parts[0].astype(jnp.float32), axis=-2))
    return (scores, weights, q_parts, k_parts, block_kv, block_keys)

def before_blocks(block_kv, block_keys, prior_kv, prior_keys):
    key_state = prior_kv[..., None, :, :] + jnp.cumsum(block_kv, axis=-3) - block_kv
    key_total = prior_keys[..., None, :] + jnp.cumsum(block_keys, axis=-2) - block_keys
    return (key_state, key_total)

def after_blocks(block_u, block_w, later_u, later_w):
    rev_u = jnp.flip(jnp.cumsum(jnp.flip(block_u, -3), axis=-3), -3)
    rev_w = jnp.flip(jnp.cumsum(jnp.flip(block_w, -2), axis=-2), -2)
    return (later_u[..., None, :, :] + rev_u - block_u, later_w[..., None, :] + rev_w - block_w)

def finish_forward(weights, values, q_feats, key_state, key_total):
    state_half = key_state.astype(jnp.bfloat16)
    numerator = product_of('...ij,...jd->...id', weights, values) + product_of('...ir,...rd->...id', q_feats, state_half)
    denominator = 1.0 + lax.optimization_barrier(jnp.sum(weights.astype(jnp.float32), axis=-1)) + precise_product('...ir,...r->...i', q_feats, key_total)
    attended = (numerator / denominator[..., None]).astype(jnp.bfloat16)
    return (state_half, numerator, denominator, attended)

def backward_blocks(grad_in, numerator, denominator, scores, weights, values, q_normed, k_normed, q_feats, state_half, key_total):
    grad_float = grad_in.astype(jnp.float32)
    scaled_grad = (grad_float / denominator[..., None]).astype(jnp.bfloat16)
    den_grad = -lax.optimization_barrier(jnp.sum(grad_float * numerator, axis=-1)) / (denominator * denominator)
    weight_grad = product_of('...id,...jd->...ij', scaled_grad, values) + den_grad[..., None]
    score_grad = jnp.where(causal_mask(), 4.0 * scores ** 3 * weight_grad * DH ** (-0.5), 0.0).astype(jnp.bfloat16)
    q_diag = product_of('...ij,...jd->...id', score_grad, k_normed)
    k_diag = product_of('...ij,...id->...jd', score_grad, q_normed)
    v_diag = product_of('...ij,...id->...jd', weights, scaled_grad)
    qf_grad = product_of('...id,...rd->...ir', scaled_grad, state_half) + den_grad[..., None] * key_total[..., None, :]
    block_u = product_of('...ir,...id->...rd', q_feats, scaled_grad)
    block_w = precise_product('...ir,...i->...r', q_feats, den_grad)
    return (q_diag, k_diag, v_diag, qf_grad, block_u, block_w)

def finish_backward(values, k_feats, later_state, later_total, v_diag):
    later_half = later_state.astype(jnp.bfloat16)
    kf_grad = product_of('...jd,...rd->...jr', values, later_half) + later_total[..., None, :]
    v_grad = v_diag + product_of('...jr,...rd->...jd', k_feats, later_half)
    return (kf_grad, v_grad)

def normalize(raw, gain, total):
    scale = lax.rsqrt(total / (HEADS * DH) + EPSILON)[:, None]
    return (scale, (raw.astype(jnp.float32) * scale * gain).astype(jnp.bfloat16))

def norm_back(raw, gain, scale, normed_grad, dot_total):
    raw_float = raw.astype(jnp.float32)
    return (scale * gain * normed_grad - raw_float * scale ** 3 * dot_total[:, None] / (HEADS * DH)).astype(jnp.bfloat16)

def reference(queries, keys, values, out_grad, q_gain, k_gain, signs):
    sign_pair = jnp.concatenate([2 * signs[0] - 1, 2 * signs[1] - 1], axis=1).astype(jnp.bfloat16)
    q_float = queries.astype(jnp.float32)
    k_float = keys.astype(jnp.float32)
    q_scale, q_normed = normalize(queries, q_gain, lax.optimization_barrier(jnp.sum(q_float * q_float, axis=-1)))
    k_scale, k_normed = normalize(keys, k_gain, lax.optimization_barrier(jnp.sum(k_float * k_float, axis=-1)))

    def split_heads(array):
        return array.reshape(TOKENS, HEADS, DH).transpose(1, 0, 2).reshape(HEADS, TOKENS // BLOCK, BLOCK, DH)

    def join_heads(array):
        return array.reshape(HEADS, TOKENS, DH).transpose(1, 0, 2).reshape(TOKENS, HEADS * DH)

    def one_head(inputs):
        q_head, k_head, v_head, g_head = inputs
        scores, weights, q_parts, k_parts, block_kv, block_keys = forward_blocks(q_head, k_head, v_head, sign_pair)
        zero_kv = jnp.zeros((RS * RS, DH), jnp.float32)
        zero_keys = jnp.zeros((RS * RS,), jnp.float32)
        key_state, key_total = before_blocks(block_kv, block_keys, zero_kv, zero_keys)
        state_half, numerator, denominator, attended = finish_forward(weights, v_head, q_parts[0], key_state, key_total)
        q_diag, k_diag, v_diag, qf_grad, block_u, block_w = backward_blocks(g_head, numerator, denominator, scores, weights, v_head, q_head, k_head, q_parts[0], state_half, key_total)
        later_state, later_total = after_blocks(block_u, block_w, zero_kv, zero_keys)
        kf_grad, v_grad = finish_backward(v_head, k_parts[0], later_state, later_total, v_diag)
        qn_grad = q_diag + sketch_back(qf_grad, q_parts[1], q_parts[2], q_parts[3], sign_pair)
        kn_grad = k_diag + sketch_back(kf_grad, k_parts[1], k_parts[2], k_parts[3], sign_pair)
        return (attended, qn_grad, kn_grad, v_grad.astype(jnp.bfloat16))
    stacked = (split_heads(q_normed), split_heads(k_normed), split_heads(values), split_heads(out_grad))
    attended, qn_grad, kn_grad, v_grad = lax.map(one_head, stacked)
    qn_grad = join_heads(qn_grad)
    kn_grad = join_heads(kn_grad)
    q_dot = lax.optimization_barrier(jnp.sum(q_float * q_gain * qn_grad, axis=-1))
    k_dot = lax.optimization_barrier(jnp.sum(k_float * k_gain * kn_grad, axis=-1))
    q_grad = norm_back(queries, q_gain, q_scale, qn_grad, q_dot)
    k_grad = norm_back(keys, k_gain, k_scale, kn_grad, k_dot)
    return (join_heads(attended), q_grad, k_grad, join_heads(v_grad))
```

```python
import jax
import jax.numpy as jnp
from jax import lax
from jax.sharding import PartitionSpec as P

HEADS = 32
DH = 128
RS = 16
BLOCK = 256


EPSILON = 1e-06
HIGHEST_PREC = lax.Precision.HIGHEST


def carried_in(part, axis, reverse):
    count = lax.axis_size(axis)
    leaves = jax.tree.leaves(part)
    flat = jnp.concatenate([leaf.reshape(-1) for leaf in leaves])
    total = flat.shape[0]
    chunk = -(-total // (count * 128)) * 128
    rows = jnp.pad(flat, (0, chunk * count - total)).reshape(count, chunk)
    mine = lax.all_to_all(rows, axis, 0, 0, tiled=True)
    if reverse:
        mine = jnp.flip(mine, 0)
    running = jnp.cumsum(mine[:-1], axis=0)
    shifted = jnp.concatenate([jnp.zeros_like(mine[:1]), running], axis=0)
    if reverse:
        shifted = jnp.flip(shifted, 0)
    back = lax.all_to_all(shifted, axis, 0, 0, tiled=True).reshape(-1)[:total]
    pieces = []
    offset = 0
    for leaf in leaves:
        pieces.append(back[offset : offset + leaf.size].reshape(leaf.shape))
        offset += leaf.size
    return jax.tree.unflatten(jax.tree.structure(part), pieces)


def product_of(spec, lhs, rhs):
    return jnp.einsum(spec, lhs, rhs, preferred_element_type=jnp.float32)


def precise_product(spec, lhs, rhs):
    return jnp.einsum(
        spec, lhs.astype(jnp.float32), rhs.astype(jnp.float32), precision=HIGHEST_PREC
    )


def causal_mask():
    row_ids = lax.broadcasted_iota(jnp.int32, (BLOCK, BLOCK), 0)
    col_ids = lax.broadcasted_iota(jnp.int32, (BLOCK, BLOCK), 1)
    return row_ids >= col_ids


def sketch(inputs, sign_pair):
    projected = product_of("...d,dr->...r", inputs, sign_pair)
    left_part = projected[..., :RS]
    right_part = projected[..., RS:]
    sketched = left_part * right_part * (RS * DH) ** (-0.5)
    outer_prod = sketched[..., :, None] * sketched[..., None, :]
    sketch_feats = outer_prod.reshape(sketched.shape[:-1] + (RS * RS,)).astype(jnp.bfloat16)
    return (sketch_feats, sketched, left_part, right_part)


def sketch_back(feat_grad, sketched, left_part, right_part, sign_pair):
    grid = feat_grad.reshape(feat_grad.shape[:-1] + (RS, RS))
    symmetric = grid + jnp.swapaxes(grid, -1, -2)
    sketch_grad = jnp.sum(symmetric * sketched[..., None, :], axis=-1)
    both_grad = jnp.concatenate([sketch_grad * right_part, sketch_grad * left_part], axis=-1) * (
        RS * DH
    ) ** (-0.5)
    return precise_product("...r,dr->...d", both_grad, sign_pair)


def forward_blocks(q_normed, k_normed, values, sign_pair):
    scores = product_of("...id,...jd->...ij", q_normed, k_normed) * DH ** (-0.5)
    weights = jnp.where(causal_mask(), scores**4, 0.0).astype(jnp.bfloat16)
    q_parts = sketch(q_normed, sign_pair)
    k_parts = sketch(k_normed, sign_pair)
    block_kv = product_of("...jr,...jd->...rd", k_parts[0], values)
    block_keys = jnp.sum(k_parts[0].astype(jnp.float32), axis=-2)
    return (scores, weights, q_parts, k_parts, block_kv, block_keys)


def before_blocks(block_kv, block_keys, prior_kv, prior_keys):
    key_state = prior_kv[..., None, :, :] + jnp.cumsum(block_kv, axis=-3) - block_kv
    key_total = prior_keys[..., None, :] + jnp.cumsum(block_keys, axis=-2) - block_keys
    return (key_state, key_total)


def after_blocks(block_u, block_w, later_u, later_w):
    rev_u = jnp.flip(jnp.cumsum(jnp.flip(block_u, -3), axis=-3), -3)
    rev_w = jnp.flip(jnp.cumsum(jnp.flip(block_w, -2), axis=-2), -2)
    return (later_u[..., None, :, :] + rev_u - block_u, later_w[..., None, :] + rev_w - block_w)


def finish_forward(weights, values, q_feats, key_state, key_total):
    state_half = key_state.astype(jnp.bfloat16)
    numerator = product_of("...ij,...jd->...id", weights, values) + product_of(
        "...ir,...rd->...id", q_feats, state_half
    )
    denominator = (
        1.0
        + jnp.sum(weights.astype(jnp.float32), axis=-1)
        + precise_product("...ir,...r->...i", q_feats, key_total)
    )
    attended = (numerator / denominator[..., None]).astype(jnp.bfloat16)
    return (state_half, numerator, denominator, attended)


def backward_blocks(
    grad_in,
    numerator,
    denominator,
    scores,
    weights,
    values,
    q_normed,
    k_normed,
    q_feats,
    state_half,
    key_total,
):
    grad_float = grad_in.astype(jnp.float32)
    scaled_grad = (grad_float / denominator[..., None]).astype(jnp.bfloat16)
    den_grad = -jnp.sum(grad_float * numerator, axis=-1) / (denominator * denominator)
    weight_grad = product_of("...id,...jd->...ij", scaled_grad, values) + den_grad[..., None]
    score_grad = jnp.where(
        causal_mask(), 4.0 * scores**3 * weight_grad * DH ** (-0.5), 0.0
    ).astype(jnp.bfloat16)
    q_diag = product_of("...ij,...jd->...id", score_grad, k_normed)
    k_diag = product_of("...ij,...id->...jd", score_grad, q_normed)
    v_diag = product_of("...ij,...id->...jd", weights, scaled_grad)
    qf_grad = (
        product_of("...id,...rd->...ir", scaled_grad, state_half)
        + den_grad[..., None] * key_total[..., None, :]
    )
    block_u = product_of("...ir,...id->...rd", q_feats, scaled_grad)
    block_w = precise_product("...ir,...i->...r", q_feats, den_grad)
    return (q_diag, k_diag, v_diag, qf_grad, block_u, block_w)


def finish_backward(values, k_feats, later_state, later_total, v_diag):
    later_half = later_state.astype(jnp.bfloat16)
    kf_grad = product_of("...jd,...rd->...jr", values, later_half) + later_total[..., None, :]
    v_grad = v_diag + product_of("...jr,...rd->...jd", k_feats, later_half)
    return (kf_grad, v_grad)


def normalize(raw, gain, total):
    scale = lax.rsqrt(total / (HEADS * DH) + EPSILON)[:, None]
    return (scale, (raw.astype(jnp.float32) * scale * gain).astype(jnp.bfloat16))


def norm_back(raw, gain, scale, normed_grad, dot_total):
    raw_float = raw.astype(jnp.float32)
    return (
        scale * gain * normed_grad - raw_float * scale**3 * dot_total[:, None] / (HEADS * DH)
    ).astype(jnp.bfloat16)


def on_device(queries, keys, values, out_grad, q_gain, k_gain, signs):
    tok_rows = queries.shape[0]
    heads_here = queries.shape[1] // DH
    block_count = tok_rows // BLOCK
    sign_pair = jnp.concatenate([2 * signs[0] - 1, 2 * signs[1] - 1], axis=1).astype(jnp.bfloat16)
    q_float = queries.astype(jnp.float32)
    k_float = keys.astype(jnp.float32)
    q_total, k_total = lax.psum(
        (jnp.sum(q_float * q_float, axis=-1), jnp.sum(k_float * k_float, axis=-1)), "head"
    )
    q_scale, q_normed = normalize(queries, q_gain, q_total)
    k_scale, k_normed = normalize(keys, k_gain, k_total)

    def split_heads(array):
        return (
            array.reshape(tok_rows, heads_here, DH)
            .transpose(1, 0, 2)
            .reshape(heads_here, block_count, BLOCK, DH)
        )

    def join_heads(array):
        return (
            array.reshape(heads_here, tok_rows, DH)
            .transpose(1, 0, 2)
            .reshape(tok_rows, heads_here * DH)
        )

    q_heads = split_heads(q_normed)
    k_heads = split_heads(k_normed)
    v_heads = split_heads(values)
    g_heads = split_heads(out_grad)
    scores, weights, q_parts, k_parts, block_kv, block_keys = forward_blocks(
        q_heads, k_heads, v_heads, sign_pair
    )
    sum_kv = jnp.sum(block_kv, axis=1)
    sum_keys = jnp.sum(block_keys, axis=1)
    prior_kv, prior_keys = carried_in((sum_kv, sum_keys), "ctx", False)
    key_state, key_total = before_blocks(block_kv, block_keys, prior_kv, prior_keys)
    state_half, numerator, denominator, attended = finish_forward(
        weights, v_heads, q_parts[0], key_state, key_total
    )
    q_diag, k_diag, v_diag, qf_grad, block_u, block_w = backward_blocks(
        g_heads,
        numerator,
        denominator,
        scores,
        weights,
        v_heads,
        q_heads,
        k_heads,
        q_parts[0],
        state_half,
        key_total,
    )
    later_u, later_w = carried_in(
        (jnp.sum(block_u, axis=1), jnp.sum(block_w, axis=1)),
        "ctx",
        True,
    )
    later_state, later_total = after_blocks(block_u, block_w, later_u, later_w)
    kf_grad, v_grad = finish_backward(v_heads, k_parts[0], later_state, later_total, v_diag)
    qn_grad = join_heads(
        q_diag + sketch_back(qf_grad, q_parts[1], q_parts[2], q_parts[3], sign_pair)
    )
    kn_grad = join_heads(
        k_diag + sketch_back(kf_grad, k_parts[1], k_parts[2], k_parts[3], sign_pair)
    )
    q_dot, k_dot = lax.psum(
        (
            jnp.sum(q_float * q_gain * qn_grad, axis=-1),
            jnp.sum(k_float * k_gain * kn_grad, axis=-1),
        ),
        "head",
    )
    q_grad = norm_back(queries, q_gain, q_scale, qn_grad, q_dot)
    k_grad = norm_back(keys, k_gain, k_scale, kn_grad, k_dot)
    return (join_heads(attended), q_grad, k_grad, join_heads(v_grad).astype(jnp.bfloat16))


def solution(mesh):
    in_specs = (
        P("ctx", "head"),
        P("ctx", "head"),
        P("ctx", "head"),
        P("ctx", "head"),
        P("head"),
        P("head"),
        P(),
    )
    out_specs = (P("ctx", "head"), P("ctx", "head"), P("ctx", "head"), P("ctx", "head"))
    return jax.shard_map(
        on_device, mesh=mesh, in_specs=in_specs, out_specs=out_specs, check_vma=False
    )
```

```python
import jax
import jax.numpy as jnp
from jax import lax
from jax.sharding import PartitionSpec as P

HEADS = 32
DH = 128
RS = 16
BLOCK = 256


EPSILON = 1e-06
HIGHEST_PREC = lax.Precision.HIGHEST


def carried_in(part, axis, reverse):
    count = lax.axis_size(axis)
    leaves = jax.tree.leaves(part)
    flat = jnp.concatenate([leaf.reshape(-1) for leaf in leaves])
    total = flat.shape[0]
    chunk = -(-total // (count * 128)) * 128
    rows = jnp.pad(flat, (0, chunk * count - total)).reshape(count, chunk)
    mine = lax.all_to_all(rows, axis, 0, 0, tiled=True)
    dest = lax.broadcasted_iota(jnp.int32, (count, count), 0)
    source = lax.broadcasted_iota(jnp.int32, (count, count), 1)
    taken = (source > dest) if reverse else (source < dest)
    shifted = jnp.einsum(
        "ij,jc->ic", taken.astype(jnp.float32), mine, precision=HIGHEST_PREC
    )
    back = lax.all_to_all(shifted, axis, 0, 0, tiled=True).reshape(-1)[:total]
    pieces = []
    offset = 0
    for leaf in leaves:
        pieces.append(back[offset : offset + leaf.size].reshape(leaf.shape))
        offset += leaf.size
    return jax.tree.unflatten(jax.tree.structure(part), pieces)


def product_of(spec, lhs, rhs):
    return jnp.einsum(spec, lhs, rhs, preferred_element_type=jnp.float32)


def precise_product(spec, lhs, rhs):
    return jnp.einsum(
        spec, lhs.astype(jnp.float32), rhs.astype(jnp.float32), precision=HIGHEST_PREC
    )


def causal_mask():
    row_ids = lax.broadcasted_iota(jnp.int32, (BLOCK, BLOCK), 0)
    col_ids = lax.broadcasted_iota(jnp.int32, (BLOCK, BLOCK), 1)
    return row_ids >= col_ids


def sketch(inputs, sign_pair):
    projected = product_of("...d,dr->...r", inputs, sign_pair)
    left_part = projected[..., :RS]
    right_part = projected[..., RS:]
    sketched = left_part * right_part * (RS * DH) ** (-0.5)
    outer_prod = sketched[..., :, None] * sketched[..., None, :]
    sketch_feats = outer_prod.reshape(sketched.shape[:-1] + (RS * RS,)).astype(jnp.bfloat16)
    return (sketch_feats, sketched, left_part, right_part)


def sketch_back(feat_grad, sketched, left_part, right_part, sign_pair):
    grid = feat_grad.reshape(feat_grad.shape[:-1] + (RS, RS))
    symmetric = grid + jnp.swapaxes(grid, -1, -2)
    sketch_grad = jnp.sum(symmetric * sketched[..., None, :], axis=-1)
    both_grad = jnp.concatenate([sketch_grad * right_part, sketch_grad * left_part], axis=-1) * (
        RS * DH
    ) ** (-0.5)
    return precise_product("...r,dr->...d", both_grad, sign_pair)


def forward_blocks(q_normed, k_normed, values, sign_pair):
    scores = product_of("...id,...jd->...ij", q_normed, k_normed) * DH ** (-0.5)
    weights = jnp.where(causal_mask(), scores**4, 0.0).astype(jnp.bfloat16)
    q_parts = sketch(q_normed, sign_pair)
    k_parts = sketch(k_normed, sign_pair)
    block_kv = product_of("...jr,...jd->...rd", k_parts[0], values)
    block_keys = jnp.sum(k_parts[0].astype(jnp.float32), axis=-2)
    return (scores, weights, q_parts, k_parts, block_kv, block_keys)


def before_blocks(block_kv, block_keys, prior_kv, prior_keys):
    key_state = prior_kv[..., None, :, :] + jnp.cumsum(block_kv, axis=-3) - block_kv
    key_total = prior_keys[..., None, :] + jnp.cumsum(block_keys, axis=-2) - block_keys
    return (key_state, key_total)


def after_blocks(block_u, block_w, later_u, later_w):
    rev_u = jnp.flip(jnp.cumsum(jnp.flip(block_u, -3), axis=-3), -3)
    rev_w = jnp.flip(jnp.cumsum(jnp.flip(block_w, -2), axis=-2), -2)
    return (later_u[..., None, :, :] + rev_u - block_u, later_w[..., None, :] + rev_w - block_w)


def finish_forward(weights, values, q_feats, key_state, key_total):
    state_half = key_state.astype(jnp.bfloat16)
    numerator = product_of("...ij,...jd->...id", weights, values) + product_of(
        "...ir,...rd->...id", q_feats, state_half
    )
    denominator = (
        1.0
        + jnp.sum(weights.astype(jnp.float32), axis=-1)
        + precise_product("...ir,...r->...i", q_feats, key_total)
    )
    attended = (numerator / denominator[..., None]).astype(jnp.bfloat16)
    return (state_half, numerator, denominator, attended)


def backward_blocks(
    grad_in,
    numerator,
    denominator,
    scores,
    weights,
    values,
    q_normed,
    k_normed,
    q_feats,
    state_half,
    key_total,
):
    grad_float = grad_in.astype(jnp.float32)
    scaled_grad = (grad_float / denominator[..., None]).astype(jnp.bfloat16)
    den_grad = -jnp.sum(grad_float * numerator, axis=-1) / (denominator * denominator)
    weight_grad = product_of("...id,...jd->...ij", scaled_grad, values) + den_grad[..., None]
    score_grad = jnp.where(
        causal_mask(), 4.0 * scores**3 * weight_grad * DH ** (-0.5), 0.0
    ).astype(jnp.bfloat16)
    q_diag = product_of("...ij,...jd->...id", score_grad, k_normed)
    k_diag = product_of("...ij,...id->...jd", score_grad, q_normed)
    v_diag = product_of("...ij,...id->...jd", weights, scaled_grad)
    qf_grad = (
        product_of("...id,...rd->...ir", scaled_grad, state_half)
        + den_grad[..., None] * key_total[..., None, :]
    )
    block_u = product_of("...ir,...id->...rd", q_feats, scaled_grad)
    block_w = precise_product("...ir,...i->...r", q_feats, den_grad)
    return (q_diag, k_diag, v_diag, qf_grad, block_u, block_w)


def finish_backward(values, k_feats, later_state, later_total, v_diag):
    later_half = later_state.astype(jnp.bfloat16)
    kf_grad = product_of("...jd,...rd->...jr", values, later_half) + later_total[..., None, :]
    v_grad = v_diag + product_of("...jr,...rd->...jd", k_feats, later_half)
    return (kf_grad, v_grad)


def normalize(raw, gain, total):
    scale = lax.rsqrt(total / (HEADS * DH) + EPSILON)[:, None]
    return (scale, (raw.astype(jnp.float32) * scale * gain).astype(jnp.bfloat16))


def norm_back(raw, gain, scale, normed_grad, dot_total):
    raw_float = raw.astype(jnp.float32)
    return (
        scale * gain * normed_grad - raw_float * scale**3 * dot_total[:, None] / (HEADS * DH)
    ).astype(jnp.bfloat16)


def on_device(queries, keys, values, out_grad, q_gain, k_gain, signs):
    tok_rows = queries.shape[0]
    heads_here = queries.shape[1] // DH
    block_count = tok_rows // BLOCK
    sign_pair = jnp.concatenate([2 * signs[0] - 1, 2 * signs[1] - 1], axis=1).astype(jnp.bfloat16)
    q_float = queries.astype(jnp.float32)
    k_float = keys.astype(jnp.float32)
    q_total, k_total = lax.psum(
        (jnp.sum(q_float * q_float, axis=-1), jnp.sum(k_float * k_float, axis=-1)), "head"
    )
    q_scale, q_normed = normalize(queries, q_gain, q_total)
    k_scale, k_normed = normalize(keys, k_gain, k_total)

    def split_heads(array):
        return (
            array.reshape(tok_rows, heads_here, DH)
            .transpose(1, 0, 2)
            .reshape(heads_here, block_count, BLOCK, DH)
        )

    def join_heads(array):
        return (
            array.reshape(heads_here, tok_rows, DH)
            .transpose(1, 0, 2)
            .reshape(tok_rows, heads_here * DH)
        )

    q_heads = split_heads(q_normed)
    k_heads = split_heads(k_normed)
    v_heads = split_heads(values)
    g_heads = split_heads(out_grad)
    scores, weights, q_parts, k_parts, block_kv, block_keys = forward_blocks(
        q_heads, k_heads, v_heads, sign_pair
    )
    sum_kv = jnp.sum(block_kv, axis=1)
    sum_keys = jnp.sum(block_keys, axis=1)
    prior_kv, prior_keys = carried_in((sum_kv, sum_keys), "ctx", False)
    key_state, key_total = before_blocks(block_kv, block_keys, prior_kv, prior_keys)
    state_half, numerator, denominator, attended = finish_forward(
        weights, v_heads, q_parts[0], key_state, key_total
    )
    q_diag, k_diag, v_diag, qf_grad, block_u, block_w = backward_blocks(
        g_heads,
        numerator,
        denominator,
        scores,
        weights,
        v_heads,
        q_heads,
        k_heads,
        q_parts[0],
        state_half,
        key_total,
    )
    later_u, later_w = carried_in(
        (jnp.sum(block_u, axis=1), jnp.sum(block_w, axis=1)),
        "ctx",
        True,
    )
    later_state, later_total = after_blocks(block_u, block_w, later_u, later_w)
    kf_grad, v_grad = finish_backward(v_heads, k_parts[0], later_state, later_total, v_diag)
    qn_grad = join_heads(
        q_diag + sketch_back(qf_grad, q_parts[1], q_parts[2], q_parts[3], sign_pair)
    )
    kn_grad = join_heads(
        k_diag + sketch_back(kf_grad, k_parts[1], k_parts[2], k_parts[3], sign_pair)
    )
    q_dot, k_dot = lax.psum(
        (
            jnp.sum(q_float * q_gain * qn_grad, axis=-1),
            jnp.sum(k_float * k_gain * kn_grad, axis=-1),
        ),
        "head",
    )
    q_grad = norm_back(queries, q_gain, q_scale, qn_grad, q_dot)
    k_grad = norm_back(keys, k_gain, k_scale, kn_grad, k_dot)
    return (join_heads(attended), q_grad, k_grad, join_heads(v_grad).astype(jnp.bfloat16))


def solution(mesh):
    in_specs = (
        P("ctx", "head"),
        P("ctx", "head"),
        P("ctx", "head"),
        P("ctx", "head"),
        P("head"),
        P("head"),
        P(),
    )
    out_specs = (P("ctx", "head"), P("ctx", "head"), P("ctx", "head"), P("ctx", "head"))
    return jax.shard_map(
        on_device, mesh=mesh, in_specs=in_specs, out_specs=out_specs, check_vma=False
    )
```

```python
import jax
import jax.numpy as jnp
from jax import lax
from jax.sharding import PartitionSpec as P

HEADS = 32
DH = 128
RS = 16
BLOCK = 256


EPSILON = 1e-06
HIGHEST_PREC = lax.Precision.HIGHEST


def carried_in(state, totals, axis, reverse):
    count = lax.axis_size(axis)
    heads_here, rows, lanes = state.shape
    total_rows = totals.shape[1] // lanes
    room = -(-(rows + total_rows) * heads_here // (count * 8)) * 8
    padded = room * count // heads_here
    stacked = jnp.concatenate(
        [
            state,
            totals.reshape(heads_here, total_rows, lanes),
            jnp.zeros((heads_here, padded - rows - total_rows, lanes), state.dtype),
        ],
        axis=1,
    ).reshape(count, room, lanes)
    mine = lax.all_to_all(stacked, axis, 0, 0, tiled=True)
    dest = lax.broadcasted_iota(jnp.int32, (count, count), 0)
    source = lax.broadcasted_iota(jnp.int32, (count, count), 1)
    taken = (source > dest) if reverse else (source < dest)
    shifted = jnp.einsum(
        "ij,jrc->irc", taken.astype(jnp.float32), mine, precision=HIGHEST_PREC
    )
    back = lax.all_to_all(shifted, axis, 0, 0, tiled=True).reshape(heads_here, padded, lanes)
    return (back[:, :rows], back[:, rows : rows + total_rows].reshape(totals.shape))


def head_sum(parts, axis):
    count = lax.axis_size(axis)
    stacked = jnp.stack(parts)
    spread = jnp.broadcast_to(stacked[None], (count,) + stacked.shape)
    gathered = lax.all_to_all(spread, axis, 0, 0, tiled=True)
    summed = jnp.sum(gathered, axis=0)
    return tuple(summed[i] for i in range(len(parts)))


def product_of(spec, lhs, rhs):
    return jnp.einsum(spec, lhs, rhs, preferred_element_type=jnp.float32)


def precise_product(spec, lhs, rhs):
    return jnp.einsum(
        spec, lhs.astype(jnp.float32), rhs.astype(jnp.float32), precision=HIGHEST_PREC
    )


def causal_mask():
    row_ids = lax.broadcasted_iota(jnp.int32, (BLOCK, BLOCK), 0)
    col_ids = lax.broadcasted_iota(jnp.int32, (BLOCK, BLOCK), 1)
    return row_ids >= col_ids


def sketch(inputs, sign_pair):
    projected = product_of("...d,dr->...r", inputs, sign_pair)
    left_part = projected[..., :RS]
    right_part = projected[..., RS:]
    sketched = left_part * right_part * (RS * DH) ** (-0.5)
    outer_prod = sketched[..., :, None] * sketched[..., None, :]
    sketch_feats = outer_prod.reshape(sketched.shape[:-1] + (RS * RS,)).astype(jnp.bfloat16)
    return (sketch_feats, sketched, left_part, right_part)


def sketch_back(feat_grad, sketched, left_part, right_part, sign_pair):
    grid = feat_grad.reshape(feat_grad.shape[:-1] + (RS, RS))
    symmetric = grid + jnp.swapaxes(grid, -1, -2)
    sketch_grad = jnp.sum(symmetric * sketched[..., None, :], axis=-1)
    both_grad = jnp.concatenate([sketch_grad * right_part, sketch_grad * left_part], axis=-1) * (
        RS * DH
    ) ** (-0.5)
    return precise_product("...r,dr->...d", both_grad, sign_pair)


def forward_blocks(q_normed, k_normed, values, sign_pair):
    scores = product_of("...id,...jd->...ij", q_normed, k_normed) * DH ** (-0.5)
    weights = jnp.where(causal_mask(), scores**4, 0.0).astype(jnp.bfloat16)
    q_parts = sketch(q_normed, sign_pair)
    k_parts = sketch(k_normed, sign_pair)
    block_kv = product_of("...jr,...jd->...rd", k_parts[0], values)
    block_keys = jnp.sum(k_parts[0].astype(jnp.float32), axis=-2)
    return (scores, weights, q_parts, k_parts, block_kv, block_keys)


def before_blocks(block_kv, block_keys, prior_kv, prior_keys):
    key_state = prior_kv[..., None, :, :] + jnp.cumsum(block_kv, axis=-3) - block_kv
    key_total = prior_keys[..., None, :] + jnp.cumsum(block_keys, axis=-2) - block_keys
    return (key_state, key_total)


def after_blocks(block_u, block_w, later_u, later_w):
    rev_u = jnp.flip(jnp.cumsum(jnp.flip(block_u, -3), axis=-3), -3)
    rev_w = jnp.flip(jnp.cumsum(jnp.flip(block_w, -2), axis=-2), -2)
    return (later_u[..., None, :, :] + rev_u - block_u, later_w[..., None, :] + rev_w - block_w)


def finish_forward(weights, values, q_feats, key_state, key_total):
    state_half = key_state.astype(jnp.bfloat16)
    numerator = product_of("...ij,...jd->...id", weights, values) + product_of(
        "...ir,...rd->...id", q_feats, state_half
    )
    denominator = (
        1.0
        + jnp.sum(weights.astype(jnp.float32), axis=-1)
        + precise_product("...ir,...r->...i", q_feats, key_total)
    )
    attended = (numerator / denominator[..., None]).astype(jnp.bfloat16)
    return (state_half, numerator, denominator, attended)


def backward_blocks(
    grad_in,
    numerator,
    denominator,
    scores,
    weights,
    values,
    q_normed,
    k_normed,
    q_feats,
    state_half,
    key_total,
):
    grad_float = grad_in.astype(jnp.float32)
    scaled_grad = (grad_float / denominator[..., None]).astype(jnp.bfloat16)
    den_grad = -jnp.sum(grad_float * numerator, axis=-1) / (denominator * denominator)
    weight_grad = product_of("...id,...jd->...ij", scaled_grad, values) + den_grad[..., None]
    score_grad = jnp.where(
        causal_mask(), 4.0 * scores**3 * weight_grad * DH ** (-0.5), 0.0
    ).astype(jnp.bfloat16)
    q_diag = product_of("...ij,...jd->...id", score_grad, k_normed)
    k_diag = product_of("...ij,...id->...jd", score_grad, q_normed)
    v_diag = product_of("...ij,...id->...jd", weights, scaled_grad)
    qf_grad = (
        product_of("...id,...rd->...ir", scaled_grad, state_half)
        + den_grad[..., None] * key_total[..., None, :]
    )
    block_u = product_of("...ir,...id->...rd", q_feats, scaled_grad)
    block_w = precise_product("...ir,...i->...r", q_feats, den_grad)
    return (q_diag, k_diag, v_diag, qf_grad, block_u, block_w)


def finish_backward(values, k_feats, later_state, later_total, v_diag):
    later_half = later_state.astype(jnp.bfloat16)
    kf_grad = product_of("...jd,...rd->...jr", values, later_half) + later_total[..., None, :]
    v_grad = v_diag + product_of("...jr,...rd->...jd", k_feats, later_half)
    return (kf_grad, v_grad)


def normalize(raw, gain, total):
    scale = lax.rsqrt(total / (HEADS * DH) + EPSILON)[:, None]
    return (scale, (raw.astype(jnp.float32) * scale * gain).astype(jnp.bfloat16))


def norm_back(raw, gain, scale, normed_grad, dot_total):
    raw_float = raw.astype(jnp.float32)
    return (
        scale * gain * normed_grad - raw_float * scale**3 * dot_total[:, None] / (HEADS * DH)
    ).astype(jnp.bfloat16)


def on_device(queries, keys, values, out_grad, q_gain, k_gain, signs):
    tok_rows = queries.shape[0]
    heads_here = queries.shape[1] // DH
    block_count = tok_rows // BLOCK
    sign_pair = jnp.concatenate([2 * signs[0] - 1, 2 * signs[1] - 1], axis=1).astype(jnp.bfloat16)
    q_float = queries.astype(jnp.float32)
    k_float = keys.astype(jnp.float32)
    q_total, k_total = head_sum(
        (jnp.sum(q_float * q_float, axis=-1), jnp.sum(k_float * k_float, axis=-1)), "head"
    )
    q_scale, q_normed = normalize(queries, q_gain, q_total)
    k_scale, k_normed = normalize(keys, k_gain, k_total)

    def split_heads(array):
        return (
            array.reshape(tok_rows, heads_here, DH)
            .transpose(1, 0, 2)
            .reshape(heads_here, block_count, BLOCK, DH)
        )

    def join_heads(array):
        return (
            array.reshape(heads_here, tok_rows, DH)
            .transpose(1, 0, 2)
            .reshape(tok_rows, heads_here * DH)
        )

    q_heads = split_heads(q_normed)
    k_heads = split_heads(k_normed)
    v_heads = split_heads(values)
    g_heads = split_heads(out_grad)
    scores, weights, q_parts, k_parts, block_kv, block_keys = forward_blocks(
        q_heads, k_heads, v_heads, sign_pair
    )
    sum_kv = jnp.sum(block_kv, axis=1)
    sum_keys = jnp.sum(block_keys, axis=1)
    prior_kv, prior_keys = carried_in(sum_kv, sum_keys, "ctx", False)
    key_state, key_total = before_blocks(block_kv, block_keys, prior_kv, prior_keys)
    state_half, numerator, denominator, attended = finish_forward(
        weights, v_heads, q_parts[0], key_state, key_total
    )
    q_diag, k_diag, v_diag, qf_grad, block_u, block_w = backward_blocks(
        g_heads,
        numerator,
        denominator,
        scores,
        weights,
        v_heads,
        q_heads,
        k_heads,
        q_parts[0],
        state_half,
        key_total,
    )
    later_u, later_w = carried_in(
        jnp.sum(block_u, axis=1), jnp.sum(block_w, axis=1), "ctx", True
    )
    later_state, later_total = after_blocks(block_u, block_w, later_u, later_w)
    kf_grad, v_grad = finish_backward(v_heads, k_parts[0], later_state, later_total, v_diag)
    qn_grad = join_heads(
        q_diag + sketch_back(qf_grad, q_parts[1], q_parts[2], q_parts[3], sign_pair)
    )
    kn_grad = join_heads(
        k_diag + sketch_back(kf_grad, k_parts[1], k_parts[2], k_parts[3], sign_pair)
    )
    q_dot, k_dot = head_sum(
        (
            jnp.sum(q_float * q_gain * qn_grad, axis=-1),
            jnp.sum(k_float * k_gain * kn_grad, axis=-1),
        ),
        "head",
    )
    q_grad = norm_back(queries, q_gain, q_scale, qn_grad, q_dot)
    k_grad = norm_back(keys, k_gain, k_scale, kn_grad, k_dot)
    return (join_heads(attended), q_grad, k_grad, join_heads(v_grad).astype(jnp.bfloat16))


def solution(mesh):
    in_specs = (
        P("ctx", "head"),
        P("ctx", "head"),
        P("ctx", "head"),
        P("ctx", "head"),
        P("head"),
        P("head"),
        P(),
    )
    out_specs = (P("ctx", "head"), P("ctx", "head"), P("ctx", "head"), P("ctx", "head"))
    return jax.shard_map(
        on_device, mesh=mesh, in_specs=in_specs, out_specs=out_specs, check_vma=False
    )
```

```python
import numpy as np
import jax
import jax.numpy as jnp
from jax import lax
from jax.sharding import PartitionSpec as P

HEADS = 32
DH = 128
RS = 16
BLOCK = 256


EPSILON = 1e-06
HIGHEST_PREC = lax.Precision.HIGHEST


def shift_rows(rows, step, reverse):
    widths = [(0, 0)] * rows.ndim
    if reverse:
        widths[0] = (0, step)
        return jnp.pad(rows[step:], widths)
    widths[0] = (step, 0)
    return jnp.pad(rows[:-step], widths)


def carried_in(state, totals, axis, reverse):
    count = lax.axis_size(axis)
    heads_here, rows, lanes = state.shape
    total_rows = totals.shape[1] // lanes
    room = -(-(rows + total_rows) * heads_here // (count * 8)) * 8
    padded = room * count // heads_here
    stacked = jnp.concatenate(
        [
            state,
            totals.reshape(heads_here, total_rows, lanes),
            jnp.zeros((heads_here, padded - rows - total_rows, lanes), state.dtype),
        ],
        axis=1,
    ).reshape(count, room, lanes)
    mine = lax.all_to_all(stacked, axis, 0, 0, tiled=True)
    shifted = shift_rows(mine, 1, reverse)
    step = 1
    while step < count:
        shifted = shifted + shift_rows(shifted, step, reverse)
        step *= 2
    back = lax.all_to_all(shifted, axis, 0, 0, tiled=True).reshape(heads_here, padded, lanes)
    return (back[:, :rows], back[:, rows : rows + total_rows].reshape(totals.shape))


def head_sum(parts, axis):
    count = lax.axis_size(axis)
    stacked = jnp.stack(parts)
    spread = jnp.broadcast_to(stacked[None], (count,) + stacked.shape)
    gathered = lax.all_to_all(spread, axis, 0, 0, tiled=True)
    summed = jnp.sum(gathered, axis=0)
    return tuple(summed[i] for i in range(len(parts)))


def product_of(spec, lhs, rhs):
    return jnp.einsum(spec, lhs, rhs, preferred_element_type=jnp.float32)


def precise_product(spec, lhs, rhs):
    return jnp.einsum(
        spec, lhs.astype(jnp.float32), rhs.astype(jnp.float32), precision=HIGHEST_PREC
    )


def causal_mask():
    row_ids = lax.broadcasted_iota(jnp.int32, (BLOCK, BLOCK), 0)
    col_ids = lax.broadcasted_iota(jnp.int32, (BLOCK, BLOCK), 1)
    return row_ids >= col_ids


def sketch(inputs, sign_pair):
    projected = product_of("...d,dr->...r", inputs, sign_pair)
    left_part = projected[..., :RS]
    right_part = projected[..., RS:]
    sketched = left_part * right_part * (RS * DH) ** (-0.5)
    outer_prod = sketched[..., :, None] * sketched[..., None, :]
    sketch_feats = outer_prod.reshape(sketched.shape[:-1] + (RS * RS,)).astype(jnp.bfloat16)
    return (sketch_feats, sketched, left_part, right_part)


def lane_select(rule):
    lanes = np.arange(RS * RS)
    return jnp.asarray((rule(lanes)[:, None] == np.arange(RS)[None, :]).astype(np.float32))


def sketch_back(feat_grad, sketched, left_part, right_part, sign_pair):
    by_row = lane_select(lambda f: f // RS)
    by_col = lane_select(lambda f: f % RS)
    row_copy = precise_product("...r,fr->...f", sketched, by_row)
    col_copy = precise_product("...s,fs->...f", sketched, by_col)
    sketch_grad = precise_product(
        "...f,fr->...r",
        jnp.concatenate([feat_grad * col_copy, feat_grad * row_copy], axis=-1),
        jnp.concatenate([by_row, by_col], axis=0),
    )
    both_grad = jnp.concatenate([sketch_grad * right_part, sketch_grad * left_part], axis=-1) * (
        RS * DH
    ) ** (-0.5)
    return precise_product("...r,dr->...d", both_grad, sign_pair)


def forward_blocks(q_normed, k_normed, values, sign_pair):
    scores = product_of("...id,...jd->...ij", q_normed, k_normed) * DH ** (-0.5)
    weights = jnp.where(causal_mask(), scores**4, 0.0).astype(jnp.bfloat16)
    q_parts = sketch(q_normed, sign_pair)
    k_parts = sketch(k_normed, sign_pair)
    block_kv = product_of("...jr,...jd->...rd", k_parts[0], values)
    block_keys = jnp.sum(k_parts[0].astype(jnp.float32), axis=-2)
    return (scores, weights, q_parts, k_parts, block_kv, block_keys)


def exclusive_blocks(blocks, prior, axis, reverse):
    count = blocks.shape[axis]
    running = prior
    outs = [None] * count
    for b in reversed(range(count)) if reverse else range(count):
        outs[b] = running
        running = running + lax.index_in_dim(blocks, b, axis, keepdims=False)
    return jnp.stack(outs, axis=axis)


def before_blocks(block_kv, block_keys, prior_kv, prior_keys):
    key_state = exclusive_blocks(block_kv, prior_kv, -3, False)
    key_total = exclusive_blocks(block_keys, prior_keys, -2, False)
    return (key_state, key_total)


def after_blocks(block_u, block_w, later_u, later_w):
    return (
        exclusive_blocks(block_u, later_u, -3, True),
        exclusive_blocks(block_w, later_w, -2, True),
    )


def finish_forward(weights, values, q_feats, key_state, key_total):
    state_half = key_state.astype(jnp.bfloat16)
    numerator = product_of("...ij,...jd->...id", weights, values) + product_of(
        "...ir,...rd->...id", q_feats, state_half
    )
    denominator = (
        1.0
        + jnp.sum(weights.astype(jnp.float32), axis=-1)
        + precise_product("...ir,...r->...i", q_feats, key_total)
    )
    attended = (numerator / denominator[..., None]).astype(jnp.bfloat16)
    return (state_half, numerator, denominator, attended)


def backward_blocks(
    grad_in,
    numerator,
    denominator,
    scores,
    weights,
    values,
    q_normed,
    k_normed,
    q_feats,
    state_half,
    key_total,
):
    grad_float = grad_in.astype(jnp.float32)
    scaled_grad = (grad_float / denominator[..., None]).astype(jnp.bfloat16)
    den_grad = -jnp.sum(grad_float * numerator, axis=-1) / (denominator * denominator)
    weight_grad = product_of("...id,...jd->...ij", scaled_grad, values) + den_grad[..., None]
    score_grad = jnp.where(
        causal_mask(), 4.0 * scores**3 * weight_grad * DH ** (-0.5), 0.0
    ).astype(jnp.bfloat16)
    q_diag = product_of("...ij,...jd->...id", score_grad, k_normed)
    k_diag = product_of("...ij,...id->...jd", score_grad, q_normed)
    v_diag = product_of("...ij,...id->...jd", weights, scaled_grad)
    qf_grad = (
        product_of("...id,...rd->...ir", scaled_grad, state_half)
        + den_grad[..., None] * key_total[..., None, :]
    )
    block_u = product_of("...ir,...id->...rd", q_feats, scaled_grad)
    block_w = precise_product("...ir,...i->...r", q_feats, den_grad)
    return (q_diag, k_diag, v_diag, qf_grad, block_u, block_w)


def finish_backward(values, k_feats, later_state, later_total, v_diag):
    later_half = later_state.astype(jnp.bfloat16)
    kf_grad = product_of("...jd,...rd->...jr", values, later_half) + later_total[..., None, :]
    v_grad = v_diag + product_of("...jr,...rd->...jd", k_feats, later_half)
    return (kf_grad, v_grad)


def normalize(raw, gain, total):
    scale = lax.rsqrt(total / (HEADS * DH) + EPSILON)[:, None]
    return (scale, (raw.astype(jnp.float32) * scale * gain).astype(jnp.bfloat16))


def norm_back(raw, gain, scale, normed_grad, dot_total):
    raw_float = raw.astype(jnp.float32)
    return (
        scale * gain * normed_grad - raw_float * scale**3 * dot_total[:, None] / (HEADS * DH)
    ).astype(jnp.bfloat16)


def on_device(queries, keys, values, out_grad, q_gain, k_gain, signs):
    tok_rows = queries.shape[0]
    heads_here = queries.shape[1] // DH
    block_count = tok_rows // BLOCK
    sign_pair = jnp.concatenate([2 * signs[0] - 1, 2 * signs[1] - 1], axis=1).astype(jnp.bfloat16)
    q_float = queries.astype(jnp.float32)
    k_float = keys.astype(jnp.float32)
    q_total, k_total = head_sum(
        (jnp.sum(q_float * q_float, axis=-1), jnp.sum(k_float * k_float, axis=-1)), "head"
    )
    q_scale, q_normed = normalize(queries, q_gain, q_total)
    k_scale, k_normed = normalize(keys, k_gain, k_total)

    def split_heads(array):
        return (
            array.reshape(tok_rows, heads_here, DH)
            .transpose(1, 0, 2)
            .reshape(heads_here, block_count, BLOCK, DH)
        )

    def join_heads(array):
        return (
            array.reshape(heads_here, tok_rows, DH)
            .transpose(1, 0, 2)
            .reshape(tok_rows, heads_here * DH)
        )

    q_heads = split_heads(q_normed)
    k_heads = split_heads(k_normed)
    v_heads = split_heads(values)
    g_heads = split_heads(out_grad)
    scores, weights, q_parts, k_parts, block_kv, block_keys = forward_blocks(
        q_heads, k_heads, v_heads, sign_pair
    )
    sum_kv = jnp.sum(block_kv, axis=1)
    sum_keys = jnp.sum(block_keys, axis=1)
    prior_kv, prior_keys = carried_in(sum_kv, sum_keys, "ctx", False)
    key_state, key_total = before_blocks(block_kv, block_keys, prior_kv, prior_keys)
    state_half, numerator, denominator, attended = finish_forward(
        weights, v_heads, q_parts[0], key_state, key_total
    )
    q_diag, k_diag, v_diag, qf_grad, block_u, block_w = backward_blocks(
        g_heads,
        numerator,
        denominator,
        scores,
        weights,
        v_heads,
        q_heads,
        k_heads,
        q_parts[0],
        state_half,
        key_total,
    )
    later_u, later_w = carried_in(
        jnp.sum(block_u, axis=1), jnp.sum(block_w, axis=1), "ctx", True
    )
    later_state, later_total = after_blocks(block_u, block_w, later_u, later_w)
    kf_grad, v_grad = finish_backward(v_heads, k_parts[0], later_state, later_total, v_diag)
    qn_grad = join_heads(
        q_diag + sketch_back(qf_grad, q_parts[1], q_parts[2], q_parts[3], sign_pair)
    )
    kn_grad = join_heads(
        k_diag + sketch_back(kf_grad, k_parts[1], k_parts[2], k_parts[3], sign_pair)
    )
    q_dot, k_dot = head_sum(
        (
            jnp.sum(q_float * q_gain * qn_grad, axis=-1),
            jnp.sum(k_float * k_gain * kn_grad, axis=-1),
        ),
        "head",
    )
    q_grad = norm_back(queries, q_gain, q_scale, qn_grad, q_dot)
    k_grad = norm_back(keys, k_gain, k_scale, kn_grad, k_dot)
    return (join_heads(attended), q_grad, k_grad, join_heads(v_grad).astype(jnp.bfloat16))


def solution(mesh):
    in_specs = (
        P("ctx", "head"),
        P("ctx", "head"),
        P("ctx", "head"),
        P("ctx", "head"),
        P("head"),
        P("head"),
        P(),
    )
    out_specs = (P("ctx", "head"), P("ctx", "head"), P("ctx", "head"), P("ctx", "head"))
    return jax.shard_map(
        on_device, mesh=mesh, in_specs=in_specs, out_specs=out_specs, check_vma=False
    )
```

```python
import numpy as np
import jax
import jax.numpy as jnp
from jax import lax
from jax.sharding import PartitionSpec as P

HEADS = 32
DH = 128
RS = 16
BLOCK = 256


EPSILON = 1e-06
HIGHEST_PREC = lax.Precision.HIGHEST


def shift_rows(rows, step, reverse):
    widths = [(0, 0)] * rows.ndim
    if reverse:
        widths[0] = (0, step)
        return jnp.pad(rows[step:], widths)
    widths[0] = (step, 0)
    return jnp.pad(rows[:-step], widths)


def carried_in(state, totals, axis, reverse):
    count = lax.axis_size(axis)
    heads_here, rows, lanes = state.shape
    total_rows = totals.shape[1] // lanes
    room = -(-(rows + total_rows) * heads_here // (count * 8)) * 8
    padded = room * count // heads_here
    stacked = jnp.concatenate(
        [
            state,
            totals.reshape(heads_here, total_rows, lanes),
            jnp.zeros((heads_here, padded - rows - total_rows, lanes), state.dtype),
        ],
        axis=1,
    ).reshape(count, room, lanes)
    mine = lax.all_to_all(stacked, axis, 0, 0, tiled=True)
    shifted = shift_rows(mine, 1, reverse)
    step = 1
    while step < count:
        shifted = shifted + shift_rows(shifted, step, reverse)
        step *= 2
    back = lax.all_to_all(shifted, axis, 0, 0, tiled=True).reshape(heads_here, padded, lanes)
    return (back[:, :rows], back[:, rows : rows + total_rows].reshape(totals.shape))


def head_sum(parts, axis):
    count = lax.axis_size(axis)
    stacked = jnp.stack(parts)
    spread = jnp.broadcast_to(stacked[None], (count,) + stacked.shape)
    gathered = lax.all_to_all(spread, axis, 0, 0, tiled=True)
    summed = jnp.sum(gathered, axis=0)
    return tuple(summed[i] for i in range(len(parts)))


def product_of(spec, lhs, rhs):
    return jnp.einsum(spec, lhs, rhs, preferred_element_type=jnp.float32)


def precise_product(spec, lhs, rhs):
    return jnp.einsum(
        spec, lhs.astype(jnp.float32), rhs.astype(jnp.float32), precision=HIGHEST_PREC
    )


def causal_mask():
    row_ids = lax.broadcasted_iota(jnp.int32, (BLOCK, BLOCK), 0)
    col_ids = lax.broadcasted_iota(jnp.int32, (BLOCK, BLOCK), 1)
    return row_ids >= col_ids


def sketch(inputs, sign_pair):
    projected = product_of("...d,dr->...r", inputs, sign_pair)
    left_part = projected[..., :RS]
    right_part = projected[..., RS:]
    sketched = left_part * right_part * (RS * DH) ** (-0.5)
    outer_prod = sketched[..., :, None] * sketched[..., None, :]
    sketch_feats = outer_prod.reshape(sketched.shape[:-1] + (RS * RS,)).astype(jnp.bfloat16)
    return (sketch_feats, sketched, left_part, right_part)


def sketch_back(feat_grad, sketched, left_part, right_part, sign_pair):
    grid = feat_grad.reshape(feat_grad.shape[:-1] + (RS, RS))
    symmetric = grid + jnp.swapaxes(grid, -1, -2)
    sketch_grad = jnp.sum(symmetric * sketched[..., None, :], axis=-1)
    both_grad = jnp.concatenate([sketch_grad * right_part, sketch_grad * left_part], axis=-1) * (
        RS * DH
    ) ** (-0.5)
    return precise_product("...r,dr->...d", both_grad, sign_pair)


def forward_blocks(q_normed, k_normed, values, sign_pair):
    scores = product_of("...id,...jd->...ij", q_normed, k_normed) * DH ** (-0.5)
    weights = jnp.where(causal_mask(), scores**4, 0.0).astype(jnp.bfloat16)
    q_parts = sketch(q_normed, sign_pair)
    k_parts = sketch(k_normed, sign_pair)
    block_kv = product_of("...jr,...jd->...rd", k_parts[0], values)
    block_keys = jnp.sum(k_parts[0].astype(jnp.float32), axis=-2)
    return (scores, weights, q_parts, k_parts, block_kv, block_keys)


def exclusive_blocks(blocks, prior, axis, reverse):
    count = blocks.shape[axis]
    running = prior
    outs = [None] * count
    for b in reversed(range(count)) if reverse else range(count):
        outs[b] = running
        running = running + lax.index_in_dim(blocks, b, axis, keepdims=False)
    return jnp.stack(outs, axis=axis)


def before_blocks(block_kv, block_keys, prior_kv, prior_keys):
    key_state = exclusive_blocks(block_kv, prior_kv, -3, False)
    key_total = exclusive_blocks(block_keys, prior_keys, -2, False)
    return (key_state, key_total)


def after_blocks(block_u, block_w, later_u, later_w):
    return (
        exclusive_blocks(block_u, later_u, -3, True),
        exclusive_blocks(block_w, later_w, -2, True),
    )


def finish_forward(weights, values, q_feats, key_state, key_total):
    state_half = key_state.astype(jnp.bfloat16)
    numerator = product_of("...ij,...jd->...id", weights, values) + product_of(
        "...ir,...rd->...id", q_feats, state_half
    )
    denominator = (
        1.0
        + jnp.sum(weights.astype(jnp.float32), axis=-1)
        + precise_product("...ir,...r->...i", q_feats, key_total)
    )
    attended = (numerator / denominator[..., None]).astype(jnp.bfloat16)
    return (state_half, numerator, denominator, attended)


def backward_blocks(
    grad_in,
    numerator,
    denominator,
    scores,
    weights,
    values,
    q_normed,
    k_normed,
    q_feats,
    state_half,
    key_total,
):
    grad_float = grad_in.astype(jnp.float32)
    scaled_grad = (grad_float / denominator[..., None]).astype(jnp.bfloat16)
    den_grad = -jnp.sum(grad_float * numerator, axis=-1) / (denominator * denominator)
    weight_grad = product_of("...id,...jd->...ij", scaled_grad, values) + den_grad[..., None]
    score_grad = jnp.where(
        causal_mask(), 4.0 * scores**3 * weight_grad * DH ** (-0.5), 0.0
    ).astype(jnp.bfloat16)
    q_diag = product_of("...ij,...jd->...id", score_grad, k_normed)
    k_diag = product_of("...ij,...id->...jd", score_grad, q_normed)
    v_diag = product_of("...ij,...id->...jd", weights, scaled_grad)
    qf_grad = (
        product_of("...id,...rd->...ir", scaled_grad, state_half)
        + den_grad[..., None] * key_total[..., None, :]
    )
    block_u = product_of("...ir,...id->...rd", q_feats, scaled_grad)
    block_w = precise_product("...ir,...i->...r", q_feats, den_grad)
    return (q_diag, k_diag, v_diag, qf_grad, block_u, block_w)


def finish_backward(values, k_feats, later_state, later_total, v_diag):
    later_half = later_state.astype(jnp.bfloat16)
    kf_grad = product_of("...jd,...rd->...jr", values, later_half) + later_total[..., None, :]
    v_grad = v_diag + product_of("...jr,...rd->...jd", k_feats, later_half)
    return (kf_grad, v_grad)


def normalize(raw, gain, total):
    scale = lax.rsqrt(total / (HEADS * DH) + EPSILON)[:, None]
    return (scale, (raw.astype(jnp.float32) * scale * gain).astype(jnp.bfloat16))


def norm_back(raw, gain, scale, normed_grad, dot_total):
    raw_float = raw.astype(jnp.float32)
    return (
        scale * gain * normed_grad - raw_float * scale**3 * dot_total[:, None] / (HEADS * DH)
    ).astype(jnp.bfloat16)


def on_device(queries, keys, values, out_grad, q_gain, k_gain, signs):
    tok_rows = queries.shape[0]
    heads_here = queries.shape[1] // DH
    block_count = tok_rows // BLOCK
    sign_pair = jnp.concatenate([2 * signs[0] - 1, 2 * signs[1] - 1], axis=1).astype(jnp.bfloat16)
    q_float = queries.astype(jnp.float32)
    k_float = keys.astype(jnp.float32)
    q_total, k_total = head_sum(
        (jnp.sum(q_float * q_float, axis=-1), jnp.sum(k_float * k_float, axis=-1)), "head"
    )
    q_scale, q_normed = normalize(queries, q_gain, q_total)
    k_scale, k_normed = normalize(keys, k_gain, k_total)

    def split_heads(array):
        return (
            array.reshape(tok_rows, heads_here, DH)
            .transpose(1, 0, 2)
            .reshape(heads_here, block_count, BLOCK, DH)
        )

    def join_heads(array):
        return (
            array.reshape(heads_here, tok_rows, DH)
            .transpose(1, 0, 2)
            .reshape(tok_rows, heads_here * DH)
        )

    q_heads = split_heads(q_normed)
    k_heads = split_heads(k_normed)
    v_heads = split_heads(values)
    g_heads = split_heads(out_grad)
    scores, weights, q_parts, k_parts, block_kv, block_keys = forward_blocks(
        q_heads, k_heads, v_heads, sign_pair
    )
    sum_kv = jnp.sum(block_kv, axis=1)
    sum_keys = jnp.sum(block_keys, axis=1)
    prior_kv, prior_keys = carried_in(sum_kv, sum_keys, "ctx", False)
    key_state, key_total = before_blocks(block_kv, block_keys, prior_kv, prior_keys)
    state_half, numerator, denominator, attended = finish_forward(
        weights, v_heads, q_parts[0], key_state, key_total
    )
    q_diag, k_diag, v_diag, qf_grad, block_u, block_w = backward_blocks(
        g_heads,
        numerator,
        denominator,
        scores,
        weights,
        v_heads,
        q_heads,
        k_heads,
        q_parts[0],
        state_half,
        key_total,
    )
    later_u, later_w = carried_in(
        jnp.sum(block_u, axis=1), jnp.sum(block_w, axis=1), "ctx", True
    )
    later_state, later_total = after_blocks(block_u, block_w, later_u, later_w)
    kf_grad, v_grad = finish_backward(v_heads, k_parts[0], later_state, later_total, v_diag)
    qn_grad = join_heads(
        q_diag + sketch_back(qf_grad, q_parts[1], q_parts[2], q_parts[3], sign_pair)
    )
    kn_grad = join_heads(
        k_diag + sketch_back(kf_grad, k_parts[1], k_parts[2], k_parts[3], sign_pair)
    )
    q_dot, k_dot = head_sum(
        (
            jnp.sum(q_float * q_gain * qn_grad, axis=-1),
            jnp.sum(k_float * k_gain * kn_grad, axis=-1),
        ),
        "head",
    )
    q_grad = norm_back(queries, q_gain, q_scale, qn_grad, q_dot)
    k_grad = norm_back(keys, k_gain, k_scale, kn_grad, k_dot)
    return (join_heads(attended), q_grad, k_grad, join_heads(v_grad).astype(jnp.bfloat16))


def solution(mesh):
    in_specs = (
        P("ctx", "head"),
        P("ctx", "head"),
        P("ctx", "head"),
        P("ctx", "head"),
        P("head"),
        P("head"),
        P(),
    )
    out_specs = (P("ctx", "head"), P("ctx", "head"), P("ctx", "head"), P("ctx", "head"))
    return jax.shard_map(
        on_device, mesh=mesh, in_specs=in_specs, out_specs=out_specs, check_vma=False
    )
```

```python
import jax
import jax.numpy as jnp
from jax import lax
from jax.sharding import PartitionSpec as P

HEADS = 32
DH = 128
RS = 16
BLOCK = 256


EPSILON = 1e-06
HIGHEST_PREC = lax.Precision.HIGHEST


def shift_rows(rows, step, reverse):
    widths = [(0, 0)] * rows.ndim
    if reverse:
        widths[0] = (0, step)
        return jnp.pad(rows[step:], widths)
    widths[0] = (step, 0)
    return jnp.pad(rows[:-step], widths)


def carried_in(state, totals, axis, reverse):
    count = lax.axis_size(axis)
    heads_here, rows, lanes = state.shape
    total_rows = totals.shape[1] // lanes
    room = -(-(rows + total_rows) * heads_here // (count * 8)) * 8
    padded = room * count // heads_here
    stacked = jnp.concatenate(
        [
            state,
            totals.reshape(heads_here, total_rows, lanes),
            jnp.zeros((heads_here, padded - rows - total_rows, lanes), state.dtype),
        ],
        axis=1,
    ).reshape(count, room, lanes)
    mine = lax.all_to_all(stacked, axis, 0, 0, tiled=True)
    shifted = shift_rows(mine, 1, reverse)
    step = 1
    while step < count:
        shifted = shifted + shift_rows(shifted, step, reverse)
        step *= 2
    back = lax.all_to_all(shifted, axis, 0, 0, tiled=True).reshape(heads_here, padded, lanes)
    return (back[:, :rows], back[:, rows : rows + total_rows].reshape(totals.shape))


def head_sum(parts, axis):
    count = lax.axis_size(axis)
    stacked = jnp.stack(parts)
    spread = jnp.broadcast_to(stacked[None], (count,) + stacked.shape)
    gathered = lax.all_to_all(spread, axis, 0, 0, tiled=True)
    summed = jnp.sum(gathered, axis=0)
    return tuple(summed[i] for i in range(len(parts)))


def product_of(spec, lhs, rhs):
    return jnp.einsum(spec, lhs, rhs, preferred_element_type=jnp.float32)


def precise_product(spec, lhs, rhs):
    return jnp.einsum(
        spec, lhs.astype(jnp.float32), rhs.astype(jnp.float32), precision=HIGHEST_PREC
    )


def causal_mask():
    row_ids = lax.broadcasted_iota(jnp.int32, (BLOCK, BLOCK), 0)
    col_ids = lax.broadcasted_iota(jnp.int32, (BLOCK, BLOCK), 1)
    return row_ids >= col_ids


def sketch(inputs, sign_pair):
    projected = product_of("...d,dr->...r", inputs, sign_pair)
    left_part = projected[..., :RS]
    right_part = projected[..., RS:]
    sketched = left_part * right_part * (RS * DH) ** (-0.5)
    outer_prod = sketched[..., :, None] * sketched[..., None, :]
    sketch_feats = outer_prod.reshape(sketched.shape[:-1] + (RS * RS,)).astype(jnp.bfloat16)
    return (sketch_feats, sketched, left_part, right_part)


def sketch_back(feat_grad, sketched, left_part, right_part, sign_pair):
    grid = feat_grad.reshape(feat_grad.shape[:-1] + (RS, RS))
    symmetric = grid + jnp.swapaxes(grid, -1, -2)
    sketch_grad = jnp.sum(symmetric * sketched[..., None, :], axis=-1)
    both_grad = jnp.concatenate([sketch_grad * right_part, sketch_grad * left_part], axis=-1) * (
        RS * DH
    ) ** (-0.5)
    return precise_product("...r,dr->...d", both_grad, sign_pair)


def forward_blocks(q_normed, k_normed, values, sign_pair):
    scores = product_of("...id,...jd->...ij", q_normed, k_normed) * DH ** (-0.5)
    weights = jnp.where(causal_mask(), scores**4, 0.0).astype(jnp.bfloat16)
    q_parts = sketch(q_normed, sign_pair)
    k_parts = sketch(k_normed, sign_pair)
    block_kv = product_of("...jr,...jd->...rd", k_parts[0], values)
    block_keys = jnp.sum(k_parts[0].astype(jnp.float32), axis=-2)
    return (scores, weights, q_parts, k_parts, block_kv, block_keys)


def before_blocks(block_kv, block_keys, prior_kv, prior_keys):
    key_state = prior_kv[..., None, :, :] + jnp.cumsum(block_kv, axis=-3) - block_kv
    key_total = prior_keys[..., None, :] + jnp.cumsum(block_keys, axis=-2) - block_keys
    return (key_state, key_total)


def after_blocks(block_u, block_w, later_u, later_w):
    rev_u = jnp.flip(jnp.cumsum(jnp.flip(block_u, -3), axis=-3), -3)
    rev_w = jnp.flip(jnp.cumsum(jnp.flip(block_w, -2), axis=-2), -2)
    return (later_u[..., None, :, :] + rev_u - block_u, later_w[..., None, :] + rev_w - block_w)


def finish_forward(weights, values, q_feats, key_state, key_total):
    state_half = key_state.astype(jnp.bfloat16)
    numerator = product_of("...ij,...jd->...id", weights, values) + product_of(
        "...ir,...rd->...id", q_feats, state_half
    )
    denominator = (
        1.0
        + jnp.sum(weights.astype(jnp.float32), axis=-1)
        + precise_product("...ir,...r->...i", q_feats, key_total)
    )
    attended = (numerator / denominator[..., None]).astype(jnp.bfloat16)
    return (state_half, numerator, denominator, attended)


def backward_blocks(
    grad_in,
    numerator,
    denominator,
    scores,
    weights,
    values,
    q_normed,
    k_normed,
    q_feats,
    state_half,
    key_total,
):
    grad_float = grad_in.astype(jnp.float32)
    scaled_grad = (grad_float / denominator[..., None]).astype(jnp.bfloat16)
    den_grad = -jnp.sum(grad_float * numerator, axis=-1) / (denominator * denominator)
    weight_grad = product_of("...id,...jd->...ij", scaled_grad, values) + den_grad[..., None]
    score_grad = jnp.where(
        causal_mask(), 4.0 * scores**3 * weight_grad * DH ** (-0.5), 0.0
    ).astype(jnp.bfloat16)
    q_diag = product_of("...ij,...jd->...id", score_grad, k_normed)
    k_diag = product_of("...ij,...id->...jd", score_grad, q_normed)
    v_diag = product_of("...ij,...id->...jd", weights, scaled_grad)
    qf_grad = (
        product_of("...id,...rd->...ir", scaled_grad, state_half)
        + den_grad[..., None] * key_total[..., None, :]
    )
    block_u = product_of("...ir,...id->...rd", q_feats, scaled_grad)
    block_w = precise_product("...ir,...i->...r", q_feats, den_grad)
    return (q_diag, k_diag, v_diag, qf_grad, block_u, block_w)


def finish_backward(values, k_feats, later_state, later_total, v_diag):
    later_half = later_state.astype(jnp.bfloat16)
    kf_grad = product_of("...jd,...rd->...jr", values, later_half) + later_total[..., None, :]
    v_grad = v_diag + product_of("...jr,...rd->...jd", k_feats, later_half)
    return (kf_grad, v_grad)


def normalize(raw, gain, total):
    scale = lax.rsqrt(total / (HEADS * DH) + EPSILON)[:, None]
    return (scale, (raw.astype(jnp.float32) * scale * gain).astype(jnp.bfloat16))


def norm_back(raw, gain, scale, normed_grad, dot_total):
    raw_float = raw.astype(jnp.float32)
    return (
        scale * gain * normed_grad - raw_float * scale**3 * dot_total[:, None] / (HEADS * DH)
    ).astype(jnp.bfloat16)


def on_device(queries, keys, values, out_grad, q_gain, k_gain, signs):
    tok_rows = queries.shape[0]
    heads_here = queries.shape[1] // DH
    block_count = tok_rows // BLOCK
    sign_pair = jnp.concatenate([2 * signs[0] - 1, 2 * signs[1] - 1], axis=1).astype(jnp.bfloat16)
    q_float = queries.astype(jnp.float32)
    k_float = keys.astype(jnp.float32)
    q_total, k_total = head_sum(
        (jnp.sum(q_float * q_float, axis=-1), jnp.sum(k_float * k_float, axis=-1)), "head"
    )
    q_scale, q_normed = normalize(queries, q_gain, q_total)
    k_scale, k_normed = normalize(keys, k_gain, k_total)

    def split_heads(array):
        return (
            array.reshape(tok_rows, heads_here, DH)
            .transpose(1, 0, 2)
            .reshape(heads_here, block_count, BLOCK, DH)
        )

    def join_heads(array):
        return (
            array.reshape(heads_here, tok_rows, DH)
            .transpose(1, 0, 2)
            .reshape(tok_rows, heads_here * DH)
        )

    q_heads = split_heads(q_normed)
    k_heads = split_heads(k_normed)
    v_heads = split_heads(values)
    g_heads = split_heads(out_grad)
    scores, weights, q_parts, k_parts, block_kv, block_keys = forward_blocks(
        q_heads, k_heads, v_heads, sign_pair
    )
    sum_kv = jnp.sum(block_kv, axis=1)
    sum_keys = jnp.sum(block_keys, axis=1)
    prior_kv, prior_keys = carried_in(sum_kv, sum_keys, "ctx", False)
    key_state, key_total = before_blocks(block_kv, block_keys, prior_kv, prior_keys)
    state_half, numerator, denominator, attended = finish_forward(
        weights, v_heads, q_parts[0], key_state, key_total
    )
    q_diag, k_diag, v_diag, qf_grad, block_u, block_w = backward_blocks(
        g_heads,
        numerator,
        denominator,
        scores,
        weights,
        v_heads,
        q_heads,
        k_heads,
        q_parts[0],
        state_half,
        key_total,
    )
    later_u, later_w = carried_in(
        jnp.sum(block_u, axis=1), jnp.sum(block_w, axis=1), "ctx", True
    )
    later_state, later_total = after_blocks(block_u, block_w, later_u, later_w)
    kf_grad, v_grad = finish_backward(v_heads, k_parts[0], later_state, later_total, v_diag)
    qn_grad = join_heads(
        q_diag + sketch_back(qf_grad, q_parts[1], q_parts[2], q_parts[3], sign_pair)
    )
    kn_grad = join_heads(
        k_diag + sketch_back(kf_grad, k_parts[1], k_parts[2], k_parts[3], sign_pair)
    )
    q_dot, k_dot = head_sum(
        (
            jnp.sum(q_float * q_gain * qn_grad, axis=-1),
            jnp.sum(k_float * k_gain * kn_grad, axis=-1),
        ),
        "head",
    )
    q_grad = norm_back(queries, q_gain, q_scale, qn_grad, q_dot)
    k_grad = norm_back(keys, k_gain, k_scale, kn_grad, k_dot)
    return (join_heads(attended), q_grad, k_grad, join_heads(v_grad).astype(jnp.bfloat16))


def solution(mesh):
    in_specs = (
        P("ctx", "head"),
        P("ctx", "head"),
        P("ctx", "head"),
        P("ctx", "head"),
        P("head"),
        P("head"),
        P(),
    )
    out_specs = (P("ctx", "head"), P("ctx", "head"), P("ctx", "head"), P("ctx", "head"))
    return jax.shard_map(
        on_device, mesh=mesh, in_specs=in_specs, out_specs=out_specs, check_vma=False
    )
```

```python
import numpy as np
import jax
import jax.numpy as jnp
from jax import lax
from jax.sharding import PartitionSpec as P

HEADS = 32
DH = 128
RS = 16
BLOCK = 256


EPSILON = 1e-06
HIGHEST_PREC = lax.Precision.HIGHEST


def shift_rows(rows, step, reverse):
    widths = [(0, 0)] * rows.ndim
    if reverse:
        widths[0] = (0, step)
        return jnp.pad(rows[step:], widths)
    widths[0] = (step, 0)
    return jnp.pad(rows[:-step], widths)


def carried_in(state, totals, axis, reverse):
    count = lax.axis_size(axis)
    heads_here, rows, lanes = state.shape
    total_rows = totals.shape[1] // lanes
    room = -(-(rows + total_rows) * heads_here // (count * 8)) * 8
    padded = room * count // heads_here
    stacked = jnp.concatenate(
        [
            state,
            totals.reshape(heads_here, total_rows, lanes),
            jnp.zeros((heads_here, padded - rows - total_rows, lanes), state.dtype),
        ],
        axis=1,
    ).reshape(count, room, lanes)
    mine = lax.all_to_all(stacked, axis, 0, 0, tiled=True)
    shifted = shift_rows(mine, 1, reverse)
    step = 1
    while step < count:
        shifted = shifted + shift_rows(shifted, step, reverse)
        step *= 2
    back = lax.all_to_all(shifted, axis, 0, 0, tiled=True).reshape(heads_here, padded, lanes)
    return (back[:, :rows], back[:, rows : rows + total_rows].reshape(totals.shape))


def head_sum(parts, axis):
    count = lax.axis_size(axis)
    stacked = jnp.stack(parts)
    spread = jnp.broadcast_to(stacked[None], (count,) + stacked.shape)
    gathered = lax.all_to_all(spread, axis, 0, 0, tiled=True)
    summed = jnp.sum(gathered, axis=0)
    return tuple(summed[i] for i in range(len(parts)))


def product_of(spec, lhs, rhs):
    return jnp.einsum(spec, lhs, rhs, preferred_element_type=jnp.float32)


def precise_product(spec, lhs, rhs):
    return jnp.einsum(
        spec, lhs.astype(jnp.float32), rhs.astype(jnp.float32), precision=HIGHEST_PREC
    )


def causal_mask():
    row_ids = lax.broadcasted_iota(jnp.int32, (BLOCK, BLOCK), 0)
    col_ids = lax.broadcasted_iota(jnp.int32, (BLOCK, BLOCK), 1)
    return row_ids >= col_ids


def sketch(inputs, sign_pair):
    projected = product_of("...d,dr->...r", inputs, sign_pair)
    left_part = projected[..., :RS]
    right_part = projected[..., RS:]
    sketched = left_part * right_part * (RS * DH) ** (-0.5)
    outer_prod = sketched[..., :, None] * sketched[..., None, :]
    sketch_feats = outer_prod.reshape(sketched.shape[:-1] + (RS * RS,)).astype(jnp.bfloat16)
    return (sketch_feats, sketched, left_part, right_part)


def sketch_back(feat_grad, sketched, left_part, right_part, sign_pair):
    grid = feat_grad.reshape(feat_grad.shape[:-1] + (RS, RS))
    symmetric = grid + jnp.swapaxes(grid, -1, -2)
    sketch_grad = jnp.sum(symmetric * sketched[..., None, :], axis=-1)
    both_grad = jnp.concatenate([sketch_grad * right_part, sketch_grad * left_part], axis=-1) * (
        RS * DH
    ) ** (-0.5)
    return precise_product("...r,dr->...d", both_grad, sign_pair)


def pair_tables():
    upper = [r * RS + c for r in range(RS) for c in range(r, RS)]
    low = np.minimum.outer(np.arange(RS), np.arange(RS)).reshape(-1)
    high = np.maximum.outer(np.arange(RS), np.arange(RS)).reshape(-1)
    owner = np.array([upper.index(a * RS + b) for a, b in zip(low, high)])
    pick = np.zeros((RS * RS, len(upper)), np.float32)
    pick[upper, np.arange(len(upper))] = 1.0
    spread = np.zeros((RS * RS, len(upper)), np.float32)
    spread[np.arange(RS * RS), owner] = 1.0
    return pick, spread


def pick_pairs(feats):
    pick = jnp.asarray(pair_tables()[0], jnp.bfloat16)
    return product_of("...f,fp->...p", feats, pick).astype(jnp.bfloat16)


def spread_pairs(half):
    spread = jnp.asarray(pair_tables()[1])
    return jnp.einsum("...pd,fp->...fd", half, spread, precision=HIGHEST_PREC)


def forward_blocks(q_normed, k_normed, values, sign_pair):
    scores = product_of("...id,...jd->...ij", q_normed, k_normed) * DH ** (-0.5)
    weights = jnp.where(causal_mask(), scores**4, 0.0).astype(jnp.bfloat16)
    q_parts = sketch(q_normed, sign_pair)
    k_parts = sketch(k_normed, sign_pair)
    block_kv = product_of("...jr,...jd->...rd", pick_pairs(k_parts[0]), values)
    block_keys = jnp.sum(k_parts[0].astype(jnp.float32), axis=-2)
    return (scores, weights, q_parts, k_parts, block_kv, block_keys)


def before_blocks(block_kv, block_keys, prior_kv, prior_keys):
    key_state = prior_kv[..., None, :, :] + jnp.cumsum(block_kv, axis=-3) - block_kv
    key_total = prior_keys[..., None, :] + jnp.cumsum(block_keys, axis=-2) - block_keys
    return (key_state, key_total)


def after_blocks(block_u, block_w, later_u, later_w):
    rev_u = jnp.flip(jnp.cumsum(jnp.flip(block_u, -3), axis=-3), -3)
    rev_w = jnp.flip(jnp.cumsum(jnp.flip(block_w, -2), axis=-2), -2)
    return (later_u[..., None, :, :] + rev_u - block_u, later_w[..., None, :] + rev_w - block_w)


def finish_forward(weights, values, q_feats, key_state, key_total):
    state_half = key_state.astype(jnp.bfloat16)
    numerator = product_of("...ij,...jd->...id", weights, values) + product_of(
        "...ir,...rd->...id", q_feats, state_half
    )
    denominator = (
        1.0
        + jnp.sum(weights.astype(jnp.float32), axis=-1)
        + precise_product("...ir,...r->...i", q_feats, key_total)
    )
    attended = (numerator / denominator[..., None]).astype(jnp.bfloat16)
    return (state_half, numerator, denominator, attended)


def backward_blocks(
    grad_in,
    numerator,
    denominator,
    scores,
    weights,
    values,
    q_normed,
    k_normed,
    q_feats,
    state_half,
    key_total,
):
    grad_float = grad_in.astype(jnp.float32)
    scaled_grad = (grad_float / denominator[..., None]).astype(jnp.bfloat16)
    den_grad = -jnp.sum(grad_float * numerator, axis=-1) / (denominator * denominator)
    weight_grad = product_of("...id,...jd->...ij", scaled_grad, values) + den_grad[..., None]
    score_grad = jnp.where(
        causal_mask(), 4.0 * scores**3 * weight_grad * DH ** (-0.5), 0.0
    ).astype(jnp.bfloat16)
    q_diag = product_of("...ij,...jd->...id", score_grad, k_normed)
    k_diag = product_of("...ij,...id->...jd", score_grad, q_normed)
    v_diag = product_of("...ij,...id->...jd", weights, scaled_grad)
    qf_grad = (
        product_of("...id,...rd->...ir", scaled_grad, state_half)
        + den_grad[..., None] * key_total[..., None, :]
    )
    block_u = product_of("...ir,...id->...rd", pick_pairs(q_feats), scaled_grad)
    block_w = precise_product("...ir,...i->...r", q_feats, den_grad)
    return (q_diag, k_diag, v_diag, qf_grad, block_u, block_w)


def finish_backward(values, k_feats, later_state, later_total, v_diag):
    later_half = later_state.astype(jnp.bfloat16)
    kf_grad = product_of("...jd,...rd->...jr", values, later_half) + later_total[..., None, :]
    v_grad = v_diag + product_of("...jr,...rd->...jd", k_feats, later_half)
    return (kf_grad, v_grad)


def normalize(raw, gain, total):
    scale = lax.rsqrt(total / (HEADS * DH) + EPSILON)[:, None]
    return (scale, (raw.astype(jnp.float32) * scale * gain).astype(jnp.bfloat16))


def norm_back(raw, gain, scale, normed_grad, dot_total):
    raw_float = raw.astype(jnp.float32)
    return (
        scale * gain * normed_grad - raw_float * scale**3 * dot_total[:, None] / (HEADS * DH)
    ).astype(jnp.bfloat16)


def on_device(queries, keys, values, out_grad, q_gain, k_gain, signs):
    tok_rows = queries.shape[0]
    heads_here = queries.shape[1] // DH
    block_count = tok_rows // BLOCK
    sign_pair = jnp.concatenate([2 * signs[0] - 1, 2 * signs[1] - 1], axis=1).astype(jnp.bfloat16)
    q_float = queries.astype(jnp.float32)
    k_float = keys.astype(jnp.float32)
    q_total, k_total = head_sum(
        (jnp.sum(q_float * q_float, axis=-1), jnp.sum(k_float * k_float, axis=-1)), "head"
    )
    q_scale, q_normed = normalize(queries, q_gain, q_total)
    k_scale, k_normed = normalize(keys, k_gain, k_total)

    def split_heads(array):
        return (
            array.reshape(tok_rows, heads_here, DH)
            .transpose(1, 0, 2)
            .reshape(heads_here, block_count, BLOCK, DH)
        )

    def join_heads(array):
        return (
            array.reshape(heads_here, tok_rows, DH)
            .transpose(1, 0, 2)
            .reshape(tok_rows, heads_here * DH)
        )

    q_heads = split_heads(q_normed)
    k_heads = split_heads(k_normed)
    v_heads = split_heads(values)
    g_heads = split_heads(out_grad)
    scores, weights, q_parts, k_parts, block_kv, block_keys = forward_blocks(
        q_heads, k_heads, v_heads, sign_pair
    )
    sum_kv = jnp.sum(block_kv, axis=1)
    sum_keys = jnp.sum(block_keys, axis=1)
    prior_kv, prior_keys = carried_in(sum_kv, sum_keys, "ctx", False)
    key_state, key_total = before_blocks(block_kv, block_keys, prior_kv, prior_keys)
    key_state = spread_pairs(key_state)
    state_half, numerator, denominator, attended = finish_forward(
        weights, v_heads, q_parts[0], key_state, key_total
    )
    q_diag, k_diag, v_diag, qf_grad, block_u, block_w = backward_blocks(
        g_heads,
        numerator,
        denominator,
        scores,
        weights,
        v_heads,
        q_heads,
        k_heads,
        q_parts[0],
        state_half,
        key_total,
    )
    later_u, later_w = carried_in(
        jnp.sum(block_u, axis=1), jnp.sum(block_w, axis=1), "ctx", True
    )
    later_state, later_total = after_blocks(block_u, block_w, later_u, later_w)
    later_state = spread_pairs(later_state)
    kf_grad, v_grad = finish_backward(v_heads, k_parts[0], later_state, later_total, v_diag)
    qn_grad = join_heads(
        q_diag + sketch_back(qf_grad, q_parts[1], q_parts[2], q_parts[3], sign_pair)
    )
    kn_grad = join_heads(
        k_diag + sketch_back(kf_grad, k_parts[1], k_parts[2], k_parts[3], sign_pair)
    )
    q_dot, k_dot = head_sum(
        (
            jnp.sum(q_float * q_gain * qn_grad, axis=-1),
            jnp.sum(k_float * k_gain * kn_grad, axis=-1),
        ),
        "head",
    )
    q_grad = norm_back(queries, q_gain, q_scale, qn_grad, q_dot)
    k_grad = norm_back(keys, k_gain, k_scale, kn_grad, k_dot)
    return (join_heads(attended), q_grad, k_grad, join_heads(v_grad).astype(jnp.bfloat16))


def solution(mesh):
    in_specs = (
        P("ctx", "head"),
        P("ctx", "head"),
        P("ctx", "head"),
        P("ctx", "head"),
        P("head"),
        P("head"),
        P(),
    )
    out_specs = (P("ctx", "head"), P("ctx", "head"), P("ctx", "head"), P("ctx", "head"))
    return jax.shard_map(
        on_device, mesh=mesh, in_specs=in_specs, out_specs=out_specs, check_vma=False
    )
```

```python
import numpy as np
import jax
import jax.numpy as jnp
from jax import lax
from jax.sharding import PartitionSpec as P

HEADS = 32
DH = 128
RS = 16
BLOCK = 256


EPSILON = 1e-06
HIGHEST_PREC = lax.Precision.HIGHEST


def shift_rows(rows, step, reverse):
    widths = [(0, 0)] * rows.ndim
    if reverse:
        widths[0] = (0, step)
        return jnp.pad(rows[step:], widths)
    widths[0] = (step, 0)
    return jnp.pad(rows[:-step], widths)


def carried_in(state, totals, axis, reverse):
    count = lax.axis_size(axis)
    heads_here, rows, lanes = state.shape
    total_rows = totals.shape[1] // lanes
    room = -(-(rows + total_rows) * heads_here // (count * 8)) * 8
    padded = room * count // heads_here
    stacked = jnp.concatenate(
        [
            state,
            totals.reshape(heads_here, total_rows, lanes),
            jnp.zeros((heads_here, padded - rows - total_rows, lanes), state.dtype),
        ],
        axis=1,
    ).reshape(count, room, lanes)
    mine = lax.all_to_all(stacked, axis, 0, 0, tiled=True)
    shifted = shift_rows(mine, 1, reverse)
    step = 1
    while step < count:
        shifted = shifted + shift_rows(shifted, step, reverse)
        step *= 2
    back = lax.all_to_all(shifted, axis, 0, 0, tiled=True).reshape(heads_here, padded, lanes)
    return (back[:, :rows], back[:, rows : rows + total_rows].reshape(totals.shape))


def head_sum(parts, axis):
    count = lax.axis_size(axis)
    stacked = jnp.stack(parts)
    spread = jnp.broadcast_to(stacked[None], (count,) + stacked.shape)
    gathered = lax.all_to_all(spread, axis, 0, 0, tiled=True)
    summed = jnp.sum(gathered, axis=0)
    return tuple(summed[i] for i in range(len(parts)))


def product_of(spec, lhs, rhs):
    return jnp.einsum(spec, lhs, rhs, preferred_element_type=jnp.float32)


def precise_product(spec, lhs, rhs):
    return jnp.einsum(
        spec, lhs.astype(jnp.float32), rhs.astype(jnp.float32), precision=HIGHEST_PREC
    )


def causal_mask():
    row_ids = lax.broadcasted_iota(jnp.int32, (BLOCK, BLOCK), 0)
    col_ids = lax.broadcasted_iota(jnp.int32, (BLOCK, BLOCK), 1)
    return row_ids >= col_ids


def sketch(inputs, sign_pair):
    projected = product_of("...d,dr->...r", inputs, sign_pair)
    left_part = projected[..., :RS]
    right_part = projected[..., RS:]
    sketched = left_part * right_part * (RS * DH) ** (-0.5)
    outer_prod = sketched[..., :, None] * sketched[..., None, :]
    sketch_feats = outer_prod.reshape(sketched.shape[:-1] + (RS * RS,)).astype(jnp.bfloat16)
    return (sketch_feats, sketched, left_part, right_part)


def sketch_back(feat_grad, sketched, left_part, right_part, sign_pair):
    grid = feat_grad.reshape(feat_grad.shape[:-1] + (RS, RS))
    symmetric = grid + jnp.swapaxes(grid, -1, -2)
    sketch_grad = jnp.sum(symmetric * sketched[..., None, :], axis=-1)
    both_grad = jnp.concatenate([sketch_grad * right_part, sketch_grad * left_part], axis=-1) * (
        RS * DH
    ) ** (-0.5)
    return precise_product("...r,dr->...d", both_grad, sign_pair)


def pair_tables():
    upper = [r * RS + c for r in range(RS) for c in range(r, RS)]
    low = np.minimum.outer(np.arange(RS), np.arange(RS)).reshape(-1)
    high = np.maximum.outer(np.arange(RS), np.arange(RS)).reshape(-1)
    owner = np.array([upper.index(a * RS + b) for a, b in zip(low, high)])
    pick = np.zeros((RS * RS, len(upper)), np.float32)
    pick[upper, np.arange(len(upper))] = 1.0
    spread = np.zeros((RS * RS, len(upper)), np.float32)
    spread[np.arange(RS * RS), owner] = 1.0
    return pick, spread


def pick_pairs(feats):
    pick = jnp.asarray(pair_tables()[0], jnp.bfloat16)
    return product_of("...f,fp->...p", feats, pick).astype(jnp.bfloat16)


def spread_pairs(half):
    spread = jnp.asarray(pair_tables()[1], jnp.bfloat16)
    return product_of("...pd,fp->...fd", half.astype(jnp.bfloat16), spread).astype(jnp.bfloat16)


def forward_blocks(q_normed, k_normed, values, sign_pair):
    scores = product_of("...id,...jd->...ij", q_normed, k_normed) * DH ** (-0.5)
    weights = jnp.where(causal_mask(), scores**4, 0.0).astype(jnp.bfloat16)
    q_parts = sketch(q_normed, sign_pair)
    k_parts = sketch(k_normed, sign_pair)
    block_kv = product_of("...jr,...jd->...rd", pick_pairs(k_parts[0]), values)
    block_keys = jnp.sum(k_parts[0].astype(jnp.float32), axis=-2)
    return (scores, weights, q_parts, k_parts, block_kv, block_keys)


def before_blocks(block_kv, block_keys, prior_kv, prior_keys):
    key_state = prior_kv[..., None, :, :] + jnp.cumsum(block_kv, axis=-3) - block_kv
    key_total = prior_keys[..., None, :] + jnp.cumsum(block_keys, axis=-2) - block_keys
    return (key_state, key_total)


def after_blocks(block_u, block_w, later_u, later_w):
    rev_u = jnp.flip(jnp.cumsum(jnp.flip(block_u, -3), axis=-3), -3)
    rev_w = jnp.flip(jnp.cumsum(jnp.flip(block_w, -2), axis=-2), -2)
    return (later_u[..., None, :, :] + rev_u - block_u, later_w[..., None, :] + rev_w - block_w)


def finish_forward(weights, values, q_feats, key_state, key_total):
    state_half = key_state
    numerator = product_of("...ij,...jd->...id", weights, values) + product_of(
        "...ir,...rd->...id", q_feats, state_half
    )
    denominator = (
        1.0
        + jnp.sum(weights.astype(jnp.float32), axis=-1)
        + precise_product("...ir,...r->...i", q_feats, key_total)
    )
    attended = (numerator / denominator[..., None]).astype(jnp.bfloat16)
    return (state_half, numerator, denominator, attended)


def backward_blocks(
    grad_in,
    numerator,
    denominator,
    scores,
    weights,
    values,
    q_normed,
    k_normed,
    q_feats,
    state_half,
    key_total,
):
    grad_float = grad_in.astype(jnp.float32)
    scaled_grad = (grad_float / denominator[..., None]).astype(jnp.bfloat16)
    den_grad = -jnp.sum(grad_float * numerator, axis=-1) / (denominator * denominator)
    weight_grad = product_of("...id,...jd->...ij", scaled_grad, values) + den_grad[..., None]
    score_grad = jnp.where(
        causal_mask(), 4.0 * scores**3 * weight_grad * DH ** (-0.5), 0.0
    ).astype(jnp.bfloat16)
    q_diag = product_of("...ij,...jd->...id", score_grad, k_normed)
    k_diag = product_of("...ij,...id->...jd", score_grad, q_normed)
    v_diag = product_of("...ij,...id->...jd", weights, scaled_grad)
    qf_grad = (
        product_of("...id,...rd->...ir", scaled_grad, state_half)
        + den_grad[..., None] * key_total[..., None, :]
    )
    block_u = product_of("...ir,...id->...rd", pick_pairs(q_feats), scaled_grad)
    block_w = precise_product("...ir,...i->...r", q_feats, den_grad)
    return (q_diag, k_diag, v_diag, qf_grad, block_u, block_w)


def finish_backward(values, k_feats, later_state, later_total, v_diag):
    later_half = later_state
    kf_grad = product_of("...jd,...rd->...jr", values, later_half) + later_total[..., None, :]
    v_grad = v_diag + product_of("...jr,...rd->...jd", k_feats, later_half)
    return (kf_grad, v_grad)


def normalize(raw, gain, total):
    scale = lax.rsqrt(total / (HEADS * DH) + EPSILON)[:, None]
    return (scale, (raw.astype(jnp.float32) * scale * gain).astype(jnp.bfloat16))


def norm_back(raw, gain, scale, normed_grad, dot_total):
    raw_float = raw.astype(jnp.float32)
    return (
        scale * gain * normed_grad - raw_float * scale**3 * dot_total[:, None] / (HEADS * DH)
    ).astype(jnp.bfloat16)


def on_device(queries, keys, values, out_grad, q_gain, k_gain, signs):
    tok_rows = queries.shape[0]
    heads_here = queries.shape[1] // DH
    block_count = tok_rows // BLOCK
    sign_pair = jnp.concatenate([2 * signs[0] - 1, 2 * signs[1] - 1], axis=1).astype(jnp.bfloat16)
    q_float = queries.astype(jnp.float32)
    k_float = keys.astype(jnp.float32)
    q_total, k_total = head_sum(
        (jnp.sum(q_float * q_float, axis=-1), jnp.sum(k_float * k_float, axis=-1)), "head"
    )
    q_scale, q_normed = normalize(queries, q_gain, q_total)
    k_scale, k_normed = normalize(keys, k_gain, k_total)

    def split_heads(array):
        return (
            array.reshape(tok_rows, heads_here, DH)
            .transpose(1, 0, 2)
            .reshape(heads_here, block_count, BLOCK, DH)
        )

    def join_heads(array):
        return (
            array.reshape(heads_here, tok_rows, DH)
            .transpose(1, 0, 2)
            .reshape(tok_rows, heads_here * DH)
        )

    q_heads = split_heads(q_normed)
    k_heads = split_heads(k_normed)
    v_heads = split_heads(values)
    g_heads = split_heads(out_grad)
    scores, weights, q_parts, k_parts, block_kv, block_keys = forward_blocks(
        q_heads, k_heads, v_heads, sign_pair
    )
    sum_kv = jnp.sum(block_kv, axis=1)
    sum_keys = jnp.sum(block_keys, axis=1)
    prior_kv, prior_keys = carried_in(sum_kv, sum_keys, "ctx", False)
    key_state, key_total = before_blocks(block_kv, block_keys, prior_kv, prior_keys)
    key_state = spread_pairs(key_state)
    state_half, numerator, denominator, attended = finish_forward(
        weights, v_heads, q_parts[0], key_state, key_total
    )
    q_diag, k_diag, v_diag, qf_grad, block_u, block_w = backward_blocks(
        g_heads,
        numerator,
        denominator,
        scores,
        weights,
        v_heads,
        q_heads,
        k_heads,
        q_parts[0],
        state_half,
        key_total,
    )
    later_u, later_w = carried_in(
        jnp.sum(block_u, axis=1), jnp.sum(block_w, axis=1), "ctx", True
    )
    later_state, later_total = after_blocks(block_u, block_w, later_u, later_w)
    later_state = spread_pairs(later_state)
    kf_grad, v_grad = finish_backward(v_heads, k_parts[0], later_state, later_total, v_diag)
    qn_grad = join_heads(
        q_diag + sketch_back(qf_grad, q_parts[1], q_parts[2], q_parts[3], sign_pair)
    )
    kn_grad = join_heads(
        k_diag + sketch_back(kf_grad, k_parts[1], k_parts[2], k_parts[3], sign_pair)
    )
    q_dot, k_dot = head_sum(
        (
            jnp.sum(q_float * q_gain * qn_grad, axis=-1),
            jnp.sum(k_float * k_gain * kn_grad, axis=-1),
        ),
        "head",
    )
    q_grad = norm_back(queries, q_gain, q_scale, qn_grad, q_dot)
    k_grad = norm_back(keys, k_gain, k_scale, kn_grad, k_dot)
    return (join_heads(attended), q_grad, k_grad, join_heads(v_grad).astype(jnp.bfloat16))


def solution(mesh):
    in_specs = (
        P("ctx", "head"),
        P("ctx", "head"),
        P("ctx", "head"),
        P("ctx", "head"),
        P("head"),
        P("head"),
        P(),
    )
    out_specs = (P("ctx", "head"), P("ctx", "head"), P("ctx", "head"), P("ctx", "head"))
    return jax.shard_map(
        on_device, mesh=mesh, in_specs=in_specs, out_specs=out_specs, check_vma=False
    )
```

```python
import numpy as np
import jax
import jax.numpy as jnp
from jax import lax
from jax.sharding import PartitionSpec as P

HEADS = 32
DH = 128
RS = 16
BLOCK = 256


EPSILON = 1e-06
HIGHEST_PREC = lax.Precision.HIGHEST


def shift_rows(rows, step, reverse):
    widths = [(0, 0)] * rows.ndim
    if reverse:
        widths[0] = (0, step)
        return jnp.pad(rows[step:], widths)
    widths[0] = (step, 0)
    return jnp.pad(rows[:-step], widths)


def carried_in(state, totals, axis, reverse):
    count = lax.axis_size(axis)
    heads_here, rows, lanes = state.shape
    total_rows = totals.shape[1] // lanes
    room = -(-(rows + total_rows) * heads_here // (count * 8)) * 8
    padded = room * count // heads_here
    stacked = jnp.concatenate(
        [
            state,
            totals.reshape(heads_here, total_rows, lanes),
            jnp.zeros((heads_here, padded - rows - total_rows, lanes), state.dtype),
        ],
        axis=1,
    ).reshape(count, room, lanes)
    mine = lax.all_to_all(stacked, axis, 0, 0, tiled=True)
    shifted = shift_rows(mine, 1, reverse)
    step = 1
    while step < count:
        shifted = shifted + shift_rows(shifted, step, reverse)
        step *= 2
    back = lax.all_to_all(shifted, axis, 0, 0, tiled=True).reshape(heads_here, padded, lanes)
    return (back[:, :rows], back[:, rows : rows + total_rows].reshape(totals.shape))


def head_sum(parts, axis):
    count = lax.axis_size(axis)
    stacked = jnp.stack(parts)
    spread = jnp.broadcast_to(stacked[None], (count,) + stacked.shape)
    gathered = lax.all_to_all(spread, axis, 0, 0, tiled=True)
    summed = jnp.sum(gathered, axis=0)
    return tuple(summed[i] for i in range(len(parts)))


def product_of(spec, lhs, rhs):
    return jnp.einsum(spec, lhs, rhs, preferred_element_type=jnp.float32)


def precise_product(spec, lhs, rhs):
    return jnp.einsum(
        spec, lhs.astype(jnp.float32), rhs.astype(jnp.float32), precision=HIGHEST_PREC
    )


def causal_mask():
    row_ids = lax.broadcasted_iota(jnp.int32, (BLOCK, BLOCK), 0)
    col_ids = lax.broadcasted_iota(jnp.int32, (BLOCK, BLOCK), 1)
    return row_ids >= col_ids


def sketch(inputs, sign_pair):
    projected = product_of("...d,dr->...r", inputs, sign_pair)
    left_part = projected[..., :RS]
    right_part = projected[..., RS:]
    sketched = left_part * right_part * (RS * DH) ** (-0.5)
    outer_prod = sketched[..., :, None] * sketched[..., None, :]
    sketch_feats = outer_prod.reshape(sketched.shape[:-1] + (RS * RS,)).astype(jnp.bfloat16)
    return (sketch_feats, sketched, left_part, right_part)


def sketch_back(feat_grad, sketched, left_part, right_part, sign_pair):
    grid = feat_grad.reshape(feat_grad.shape[:-1] + (RS, RS))
    symmetric = grid + jnp.swapaxes(grid, -1, -2)
    sketch_grad = jnp.sum(symmetric * sketched[..., None, :], axis=-1)
    both_grad = jnp.concatenate([sketch_grad * right_part, sketch_grad * left_part], axis=-1) * (
        RS * DH
    ) ** (-0.5)
    return precise_product("...r,dr->...d", both_grad, sign_pair)


def pair_tables():
    upper = [r * RS + c for r in range(RS) for c in range(r, RS)]
    low = np.minimum.outer(np.arange(RS), np.arange(RS)).reshape(-1)
    high = np.maximum.outer(np.arange(RS), np.arange(RS)).reshape(-1)
    owner = np.array([upper.index(a * RS + b) for a, b in zip(low, high)])
    pick = np.zeros((RS * RS, len(upper)), np.float32)
    pick[upper, np.arange(len(upper))] = 1.0
    spread = np.zeros((RS * RS, len(upper)), np.float32)
    spread[np.arange(RS * RS), owner] = 1.0
    return pick, spread


def pick_pairs(feats):
    pick = jnp.asarray(pair_tables()[0], jnp.bfloat16)
    return lax.optimization_barrier(product_of("...f,fp->...p", feats, pick).astype(jnp.bfloat16))


def spread_pairs(half):
    spread = jnp.asarray(pair_tables()[1], jnp.bfloat16)
    return lax.optimization_barrier(
        product_of("...pd,fp->...fd", half.astype(jnp.bfloat16), spread).astype(jnp.bfloat16)
    )


def forward_blocks(q_normed, k_normed, values, sign_pair):
    scores = product_of("...id,...jd->...ij", q_normed, k_normed) * DH ** (-0.5)
    weights = jnp.where(causal_mask(), scores**4, 0.0).astype(jnp.bfloat16)
    q_parts = sketch(q_normed, sign_pair)
    k_parts = sketch(k_normed, sign_pair)
    block_kv = product_of("...jr,...jd->...rd", pick_pairs(k_parts[0]), values)
    block_keys = jnp.sum(k_parts[0].astype(jnp.float32), axis=-2)
    return (scores, weights, q_parts, k_parts, block_kv, block_keys)


def before_blocks(block_kv, block_keys, prior_kv, prior_keys):
    key_state = prior_kv[..., None, :, :] + jnp.cumsum(block_kv, axis=-3) - block_kv
    key_total = prior_keys[..., None, :] + jnp.cumsum(block_keys, axis=-2) - block_keys
    return (key_state, key_total)


def after_blocks(block_u, block_w, later_u, later_w):
    rev_u = jnp.flip(jnp.cumsum(jnp.flip(block_u, -3), axis=-3), -3)
    rev_w = jnp.flip(jnp.cumsum(jnp.flip(block_w, -2), axis=-2), -2)
    return (later_u[..., None, :, :] + rev_u - block_u, later_w[..., None, :] + rev_w - block_w)


def finish_forward(weights, values, q_feats, key_state, key_total):
    state_half = key_state
    numerator = product_of("...ij,...jd->...id", weights, values) + product_of(
        "...ir,...rd->...id", q_feats, state_half
    )
    denominator = (
        1.0
        + jnp.sum(weights.astype(jnp.float32), axis=-1)
        + precise_product("...ir,...r->...i", q_feats, key_total)
    )
    attended = (numerator / denominator[..., None]).astype(jnp.bfloat16)
    return (state_half, numerator, denominator, attended)


def backward_blocks(
    grad_in,
    numerator,
    denominator,
    scores,
    weights,
    values,
    q_normed,
    k_normed,
    q_feats,
    state_half,
    key_total,
):
    grad_float = grad_in.astype(jnp.float32)
    scaled_grad = (grad_float / denominator[..., None]).astype(jnp.bfloat16)
    den_grad = -jnp.sum(grad_float * numerator, axis=-1) / (denominator * denominator)
    weight_grad = product_of("...id,...jd->...ij", scaled_grad, values) + den_grad[..., None]
    score_grad = jnp.where(
        causal_mask(), 4.0 * scores**3 * weight_grad * DH ** (-0.5), 0.0
    ).astype(jnp.bfloat16)
    q_diag = product_of("...ij,...jd->...id", score_grad, k_normed)
    k_diag = product_of("...ij,...id->...jd", score_grad, q_normed)
    v_diag = product_of("...ij,...id->...jd", weights, scaled_grad)
    qf_grad = (
        product_of("...id,...rd->...ir", scaled_grad, state_half)
        + den_grad[..., None] * key_total[..., None, :]
    )
    block_u = product_of("...ir,...id->...rd", pick_pairs(q_feats), scaled_grad)
    block_w = precise_product("...ir,...i->...r", q_feats, den_grad)
    return (q_diag, k_diag, v_diag, qf_grad, block_u, block_w)


def finish_backward(values, k_feats, later_state, later_total, v_diag):
    later_half = later_state
    kf_grad = product_of("...jd,...rd->...jr", values, later_half) + later_total[..., None, :]
    v_grad = v_diag + product_of("...jr,...rd->...jd", k_feats, later_half)
    return (kf_grad, v_grad)


def normalize(raw, gain, total):
    scale = lax.rsqrt(total / (HEADS * DH) + EPSILON)[:, None]
    return (scale, (raw.astype(jnp.float32) * scale * gain).astype(jnp.bfloat16))


def norm_back(raw, gain, scale, normed_grad, dot_total):
    raw_float = raw.astype(jnp.float32)
    return (
        scale * gain * normed_grad - raw_float * scale**3 * dot_total[:, None] / (HEADS * DH)
    ).astype(jnp.bfloat16)


def on_device(queries, keys, values, out_grad, q_gain, k_gain, signs):
    tok_rows = queries.shape[0]
    heads_here = queries.shape[1] // DH
    block_count = tok_rows // BLOCK
    sign_pair = jnp.concatenate([2 * signs[0] - 1, 2 * signs[1] - 1], axis=1).astype(jnp.bfloat16)
    q_float = queries.astype(jnp.float32)
    k_float = keys.astype(jnp.float32)
    q_total, k_total = head_sum(
        (jnp.sum(q_float * q_float, axis=-1), jnp.sum(k_float * k_float, axis=-1)), "head"
    )
    q_scale, q_normed = normalize(queries, q_gain, q_total)
    k_scale, k_normed = normalize(keys, k_gain, k_total)

    def split_heads(array):
        return (
            array.reshape(tok_rows, heads_here, DH)
            .transpose(1, 0, 2)
            .reshape(heads_here, block_count, BLOCK, DH)
        )

    def join_heads(array):
        return (
            array.reshape(heads_here, tok_rows, DH)
            .transpose(1, 0, 2)
            .reshape(tok_rows, heads_here * DH)
        )

    q_heads = split_heads(q_normed)
    k_heads = split_heads(k_normed)
    v_heads = split_heads(values)
    g_heads = split_heads(out_grad)
    scores, weights, q_parts, k_parts, block_kv, block_keys = forward_blocks(
        q_heads, k_heads, v_heads, sign_pair
    )
    sum_kv = jnp.sum(block_kv, axis=1)
    sum_keys = jnp.sum(block_keys, axis=1)
    prior_kv, prior_keys = carried_in(sum_kv, sum_keys, "ctx", False)
    key_state, key_total = before_blocks(block_kv, block_keys, prior_kv, prior_keys)
    key_state = spread_pairs(key_state)
    state_half, numerator, denominator, attended = finish_forward(
        weights, v_heads, q_parts[0], key_state, key_total
    )
    q_diag, k_diag, v_diag, qf_grad, block_u, block_w = backward_blocks(
        g_heads,
        numerator,
        denominator,
        scores,
        weights,
        v_heads,
        q_heads,
        k_heads,
        q_parts[0],
        state_half,
        key_total,
    )
    later_u, later_w = carried_in(
        jnp.sum(block_u, axis=1), jnp.sum(block_w, axis=1), "ctx", True
    )
    later_state, later_total = after_blocks(block_u, block_w, later_u, later_w)
    later_state = spread_pairs(later_state)
    kf_grad, v_grad = finish_backward(v_heads, k_parts[0], later_state, later_total, v_diag)
    qn_grad = join_heads(
        q_diag + sketch_back(qf_grad, q_parts[1], q_parts[2], q_parts[3], sign_pair)
    )
    kn_grad = join_heads(
        k_diag + sketch_back(kf_grad, k_parts[1], k_parts[2], k_parts[3], sign_pair)
    )
    q_dot, k_dot = head_sum(
        (
            jnp.sum(q_float * q_gain * qn_grad, axis=-1),
            jnp.sum(k_float * k_gain * kn_grad, axis=-1),
        ),
        "head",
    )
    q_grad = norm_back(queries, q_gain, q_scale, qn_grad, q_dot)
    k_grad = norm_back(keys, k_gain, k_scale, kn_grad, k_dot)
    return (join_heads(attended), q_grad, k_grad, join_heads(v_grad).astype(jnp.bfloat16))


def solution(mesh):
    in_specs = (
        P("ctx", "head"),
        P("ctx", "head"),
        P("ctx", "head"),
        P("ctx", "head"),
        P("head"),
        P("head"),
        P(),
    )
    out_specs = (P("ctx", "head"), P("ctx", "head"), P("ctx", "head"), P("ctx", "head"))
    return jax.shard_map(
        on_device, mesh=mesh, in_specs=in_specs, out_specs=out_specs, check_vma=False
    )
```

```python
import numpy as np
import jax
import jax.numpy as jnp
from jax import lax
from jax.sharding import PartitionSpec as P

HEADS = 32
DH = 128
RS = 16
BLOCK = 256


EPSILON = 1e-06
HIGHEST_PREC = lax.Precision.HIGHEST


def shift_rows(rows, step, reverse):
    widths = [(0, 0)] * rows.ndim
    if reverse:
        widths[0] = (0, step)
        return jnp.pad(rows[step:], widths)
    widths[0] = (step, 0)
    return jnp.pad(rows[:-step], widths)


def carried_in(state, totals, axis, reverse, along=()):
    count = lax.axis_size(axis)
    heads_here, rows, lanes = state.shape
    total_rows = totals.shape[1] // lanes
    room = -(-(rows + total_rows) * heads_here // (count * 8)) * 8
    padded = room * count // heads_here
    stacked = jnp.concatenate(
        [
            state,
            totals.reshape(heads_here, total_rows, lanes),
            jnp.zeros((heads_here, padded - rows - total_rows, lanes), state.dtype),
        ],
        axis=1,
    ).reshape(count, room, lanes)
    stacked, along = lax.optimization_barrier((stacked, along))
    mine = lax.all_to_all(stacked, axis, 0, 0, tiled=True)
    shifted = shift_rows(mine, 1, reverse)
    step = 1
    while step < count:
        shifted = shifted + shift_rows(shifted, step, reverse)
        step *= 2
    back = lax.all_to_all(shifted, axis, 0, 0, tiled=True).reshape(heads_here, padded, lanes)
    return (back[:, :rows], back[:, rows : rows + total_rows].reshape(totals.shape), along)


def head_sum(parts, axis, along=()):
    count = lax.axis_size(axis)
    stacked, along = lax.optimization_barrier((jnp.stack(parts), along))
    spread = jnp.broadcast_to(stacked[None], (count,) + stacked.shape)
    gathered = lax.all_to_all(spread, axis, 0, 0, tiled=True)
    summed = jnp.sum(gathered, axis=0)
    return (tuple(summed[i] for i in range(len(parts))), along)


def product_of(spec, lhs, rhs):
    return jnp.einsum(spec, lhs, rhs, preferred_element_type=jnp.float32)


def precise_product(spec, lhs, rhs):
    return jnp.einsum(
        spec, lhs.astype(jnp.float32), rhs.astype(jnp.float32), precision=HIGHEST_PREC
    )


def causal_mask():
    row_ids = lax.broadcasted_iota(jnp.int32, (BLOCK, BLOCK), 0)
    col_ids = lax.broadcasted_iota(jnp.int32, (BLOCK, BLOCK), 1)
    return row_ids >= col_ids


def sketch(inputs, sign_pair):
    projected = product_of("...d,dr->...r", inputs, sign_pair)
    left_part = projected[..., :RS]
    right_part = projected[..., RS:]
    sketched = left_part * right_part * (RS * DH) ** (-0.5)
    outer_prod = sketched[..., :, None] * sketched[..., None, :]
    sketch_feats = outer_prod.reshape(sketched.shape[:-1] + (RS * RS,)).astype(jnp.bfloat16)
    return (sketch_feats, sketched, left_part, right_part)


def sketch_back(feat_grad, sketched, left_part, right_part, sign_pair):
    grid = feat_grad.reshape(feat_grad.shape[:-1] + (RS, RS))
    symmetric = grid + jnp.swapaxes(grid, -1, -2)
    sketch_grad = jnp.sum(symmetric * sketched[..., None, :], axis=-1)
    both_grad = jnp.concatenate([sketch_grad * right_part, sketch_grad * left_part], axis=-1) * (
        RS * DH
    ) ** (-0.5)
    return precise_product("...r,dr->...d", both_grad, sign_pair)


def pair_tables():
    upper = [r * RS + c for r in range(RS) for c in range(r, RS)]
    low = np.minimum.outer(np.arange(RS), np.arange(RS)).reshape(-1)
    high = np.maximum.outer(np.arange(RS), np.arange(RS)).reshape(-1)
    owner = np.array([upper.index(a * RS + b) for a, b in zip(low, high)])
    pick = np.zeros((RS * RS, len(upper)), np.float32)
    pick[upper, np.arange(len(upper))] = 1.0
    spread = np.zeros((RS * RS, len(upper)), np.float32)
    spread[np.arange(RS * RS), owner] = 1.0
    return pick, spread


def pick_pairs(feats):
    pick = jnp.asarray(pair_tables()[0], jnp.bfloat16)
    return lax.optimization_barrier(product_of("...f,fp->...p", feats, pick).astype(jnp.bfloat16))


def spread_pairs(half):
    spread = jnp.asarray(pair_tables()[1], jnp.bfloat16)
    return lax.optimization_barrier(
        product_of("...pd,fp->...fd", half.astype(jnp.bfloat16), spread).astype(jnp.bfloat16)
    )


def forward_blocks(q_normed, k_normed, values, sign_pair):
    scores = product_of("...id,...jd->...ij", q_normed, k_normed) * DH ** (-0.5)
    weights = jnp.where(causal_mask(), scores**4, 0.0).astype(jnp.bfloat16)
    q_parts = sketch(q_normed, sign_pair)
    k_parts = sketch(k_normed, sign_pair)
    block_kv = product_of("...jr,...jd->...rd", pick_pairs(k_parts[0]), values)
    block_keys = jnp.sum(k_parts[0].astype(jnp.float32), axis=-2)
    return (scores, weights, q_parts, k_parts, block_kv, block_keys)


def before_blocks(block_kv, block_keys, prior_kv, prior_keys):
    key_state = prior_kv[..., None, :, :] + jnp.cumsum(block_kv, axis=-3) - block_kv
    key_total = prior_keys[..., None, :] + jnp.cumsum(block_keys, axis=-2) - block_keys
    return (key_state, key_total)


def after_blocks(block_u, block_w, later_u, later_w):
    rev_u = jnp.flip(jnp.cumsum(jnp.flip(block_u, -3), axis=-3), -3)
    rev_w = jnp.flip(jnp.cumsum(jnp.flip(block_w, -2), axis=-2), -2)
    return (later_u[..., None, :, :] + rev_u - block_u, later_w[..., None, :] + rev_w - block_w)


def finish_forward(weights, values, q_feats, key_state, key_total):
    state_half = key_state
    numerator = product_of("...ij,...jd->...id", weights, values) + product_of(
        "...ir,...rd->...id", q_feats, state_half
    )
    denominator = (
        1.0
        + jnp.sum(weights.astype(jnp.float32), axis=-1)
        + precise_product("...ir,...r->...i", q_feats, key_total)
    )
    return (state_half, numerator, denominator)


def backward_states(grad_in, numerator, denominator, q_feats):
    grad_float = grad_in.astype(jnp.float32)
    scaled_grad = (grad_float / denominator[..., None]).astype(jnp.bfloat16)
    den_grad = -jnp.sum(grad_float * numerator, axis=-1) / (denominator * denominator)
    block_u = product_of("...ir,...id->...rd", pick_pairs(q_feats), scaled_grad)
    block_w = precise_product("...ir,...i->...r", q_feats, den_grad)
    return (scaled_grad, den_grad, block_u, block_w)


def backward_blocks(
    scaled_grad,
    den_grad,
    scores,
    weights,
    values,
    q_normed,
    k_normed,
    state_half,
    key_total,
):
    weight_grad = product_of("...id,...jd->...ij", scaled_grad, values) + den_grad[..., None]
    score_grad = jnp.where(
        causal_mask(), 4.0 * scores**3 * weight_grad * DH ** (-0.5), 0.0
    ).astype(jnp.bfloat16)
    q_diag = product_of("...ij,...jd->...id", score_grad, k_normed)
    k_diag = product_of("...ij,...id->...jd", score_grad, q_normed)
    v_diag = product_of("...ij,...id->...jd", weights, scaled_grad)
    qf_grad = (
        product_of("...id,...rd->...ir", scaled_grad, state_half)
        + den_grad[..., None] * key_total[..., None, :]
    )
    return (q_diag, k_diag, v_diag, qf_grad)


def finish_backward(values, k_feats, later_state, later_total, v_diag):
    later_half = later_state
    kf_grad = product_of("...jd,...rd->...jr", values, later_half) + later_total[..., None, :]
    v_grad = v_diag + product_of("...jr,...rd->...jd", k_feats, later_half)
    return (kf_grad, v_grad)


def normalize(raw, gain, total):
    scale = lax.rsqrt(total / (HEADS * DH) + EPSILON)[:, None]
    return (scale, (raw.astype(jnp.float32) * scale * gain).astype(jnp.bfloat16))


def norm_back(raw, gain, scale, normed_grad, dot_total):
    raw_float = raw.astype(jnp.float32)
    return (
        scale * gain * normed_grad - raw_float * scale**3 * dot_total[:, None] / (HEADS * DH)
    ).astype(jnp.bfloat16)


def on_device(queries, keys, values, out_grad, q_gain, k_gain, signs):
    tok_rows = queries.shape[0]
    heads_here = queries.shape[1] // DH
    block_count = tok_rows // BLOCK
    sign_pair = jnp.concatenate([2 * signs[0] - 1, 2 * signs[1] - 1], axis=1).astype(jnp.bfloat16)
    q_float = queries.astype(jnp.float32)
    k_float = keys.astype(jnp.float32)
    (q_total, k_total), _ = head_sum(
        (jnp.sum(q_float * q_float, axis=-1), jnp.sum(k_float * k_float, axis=-1)), "head"
    )
    q_scale, q_normed = normalize(queries, q_gain, q_total)
    k_scale, k_normed = normalize(keys, k_gain, k_total)

    def split_heads(array):
        return (
            array.reshape(tok_rows, heads_here, DH)
            .transpose(1, 0, 2)
            .reshape(heads_here, block_count, BLOCK, DH)
        )

    def join_heads(array):
        return (
            array.reshape(heads_here, tok_rows, DH)
            .transpose(1, 0, 2)
            .reshape(tok_rows, heads_here * DH)
        )

    q_heads = split_heads(q_normed)
    k_heads = split_heads(k_normed)
    v_heads = split_heads(values)
    g_heads = split_heads(out_grad)
    scores, weights, q_parts, k_parts, block_kv, block_keys = forward_blocks(
        q_heads, k_heads, v_heads, sign_pair
    )
    sum_kv = jnp.sum(block_kv, axis=1)
    sum_keys = jnp.sum(block_keys, axis=1)
    prior_kv, prior_keys, _ = carried_in(sum_kv, sum_keys, "ctx", False)
    key_state, key_total = before_blocks(block_kv, block_keys, prior_kv, prior_keys)
    key_state = spread_pairs(key_state)
    state_half, numerator, denominator = finish_forward(
        weights, v_heads, q_parts[0], key_state, key_total
    )
    scaled_grad, den_grad, block_u, block_w = backward_states(
        g_heads, numerator, denominator, q_parts[0]
    )
    later_u, later_w, (scaled_grad, den_grad, numerator, denominator) = carried_in(
        jnp.sum(block_u, axis=1),
        jnp.sum(block_w, axis=1),
        "ctx",
        True,
        (scaled_grad, den_grad, numerator, denominator),
    )
    attended = (numerator / denominator[..., None]).astype(jnp.bfloat16)
    q_diag, k_diag, v_diag, qf_grad = backward_blocks(
        scaled_grad,
        den_grad,
        scores,
        weights,
        v_heads,
        q_heads,
        k_heads,
        state_half,
        key_total,
    )
    later_state, later_total = after_blocks(block_u, block_w, later_u, later_w)
    later_state = spread_pairs(later_state)
    kf_grad, _ = finish_backward(v_heads, k_parts[0], later_state, later_total, v_diag)
    qn_grad = join_heads(
        q_diag + sketch_back(qf_grad, q_parts[1], q_parts[2], q_parts[3], sign_pair)
    )
    kn_grad = join_heads(
        k_diag + sketch_back(kf_grad, k_parts[1], k_parts[2], k_parts[3], sign_pair)
    )
    (q_dot, k_dot), (v_diag, later_state) = head_sum(
        (
            jnp.sum(q_float * q_gain * qn_grad, axis=-1),
            jnp.sum(k_float * k_gain * kn_grad, axis=-1),
        ),
        "head",
        (v_diag, later_state),
    )
    _, v_grad = finish_backward(v_heads, k_parts[0], later_state, later_total, v_diag)
    q_grad = norm_back(queries, q_gain, q_scale, qn_grad, q_dot)
    k_grad = norm_back(keys, k_gain, k_scale, kn_grad, k_dot)
    return (join_heads(attended), q_grad, k_grad, join_heads(v_grad).astype(jnp.bfloat16))


def solution(mesh):
    in_specs = (
        P("ctx", "head"),
        P("ctx", "head"),
        P("ctx", "head"),
        P("ctx", "head"),
        P("head"),
        P("head"),
        P(),
    )
    out_specs = (P("ctx", "head"), P("ctx", "head"), P("ctx", "head"), P("ctx", "head"))
    return jax.shard_map(
        on_device, mesh=mesh, in_specs=in_specs, out_specs=out_specs, check_vma=False
    )
```

```python
import numpy as np
import jax
import jax.numpy as jnp
from jax import lax
from jax.sharding import PartitionSpec as P

HEADS = 32
DH = 128
RS = 16
BLOCK = 256


EPSILON = 1e-06
HIGHEST_PREC = lax.Precision.HIGHEST


def shift_rows(rows, step, reverse):
    widths = [(0, 0)] * rows.ndim
    if reverse:
        widths[0] = (0, step)
        return jnp.pad(rows[step:], widths)
    widths[0] = (step, 0)
    return jnp.pad(rows[:-step], widths)


def carried_in(state, totals, axis, reverse, along=()):
    count = lax.axis_size(axis)
    heads_here, rows, lanes = state.shape
    total_rows = totals.shape[1] // lanes
    room = -(-(rows + total_rows) * heads_here // (count * 8)) * 8
    padded = room * count // heads_here
    stacked = jnp.concatenate(
        [
            state,
            totals.reshape(heads_here, total_rows, lanes),
            jnp.zeros((heads_here, padded - rows - total_rows, lanes), state.dtype),
        ],
        axis=1,
    ).reshape(count, room, lanes)
    stacked, along = lax.optimization_barrier((stacked, along))
    mine = lax.all_to_all(stacked, axis, 0, 0, tiled=True)
    shifted = shift_rows(mine, 1, reverse)
    step = 1
    while step < count:
        shifted = shifted + shift_rows(shifted, step, reverse)
        step *= 2
    back = lax.all_to_all(shifted, axis, 0, 0, tiled=True).reshape(heads_here, padded, lanes)
    return (back[:, :rows], back[:, rows : rows + total_rows].reshape(totals.shape), along)


def head_sum(parts, axis, along=()):
    count = lax.axis_size(axis)
    stacked, along = lax.optimization_barrier((jnp.stack(parts), along))
    spread = jnp.broadcast_to(stacked[None], (count,) + stacked.shape)
    gathered = lax.all_to_all(spread, axis, 0, 0, tiled=True)
    summed = jnp.sum(gathered, axis=0)
    return (tuple(summed[i] for i in range(len(parts))), along)


def product_of(spec, lhs, rhs):
    return jnp.einsum(spec, lhs, rhs, preferred_element_type=jnp.float32)


def precise_product(spec, lhs, rhs):
    return jnp.einsum(
        spec, lhs.astype(jnp.float32), rhs.astype(jnp.float32), precision=HIGHEST_PREC
    )


def causal_mask():
    row_ids = lax.broadcasted_iota(jnp.int32, (BLOCK, BLOCK), 0)
    col_ids = lax.broadcasted_iota(jnp.int32, (BLOCK, BLOCK), 1)
    return row_ids >= col_ids


def sketch(inputs, sign_pair):
    projected = product_of("...d,dr->...r", inputs, sign_pair)
    left_part = projected[..., :RS]
    right_part = projected[..., RS:]
    sketched = left_part * right_part * (RS * DH) ** (-0.5)
    outer_prod = sketched[..., :, None] * sketched[..., None, :]
    sketch_feats = outer_prod.reshape(sketched.shape[:-1] + (RS * RS,)).astype(jnp.bfloat16)
    return (sketch_feats, sketched, left_part, right_part)


def sketch_back(feat_grad, sketched, left_part, right_part, sign_pair):
    grid = feat_grad.reshape(feat_grad.shape[:-1] + (RS, RS))
    symmetric = grid + jnp.swapaxes(grid, -1, -2)
    sketch_grad = jnp.sum(symmetric * sketched[..., None, :], axis=-1)
    both_grad = jnp.concatenate([sketch_grad * right_part, sketch_grad * left_part], axis=-1) * (
        RS * DH
    ) ** (-0.5)
    return precise_product("...r,dr->...d", both_grad, sign_pair)


def pair_tables():
    upper = [r * RS + c for r in range(RS) for c in range(r, RS)]
    low = np.minimum.outer(np.arange(RS), np.arange(RS)).reshape(-1)
    high = np.maximum.outer(np.arange(RS), np.arange(RS)).reshape(-1)
    owner = np.array([upper.index(a * RS + b) for a, b in zip(low, high)])
    pick = np.zeros((RS * RS, len(upper)), np.float32)
    pick[upper, np.arange(len(upper))] = 1.0
    spread = np.zeros((RS * RS, len(upper)), np.float32)
    spread[np.arange(RS * RS), owner] = 1.0
    return pick, spread


def pick_pairs(feats):
    pick = jnp.asarray(pair_tables()[0], jnp.bfloat16)
    return lax.optimization_barrier(product_of("...f,fp->...p", feats, pick).astype(jnp.bfloat16))


def spread_pairs(half):
    spread = jnp.asarray(pair_tables()[1], jnp.bfloat16)
    return lax.optimization_barrier(
        product_of("...pd,fp->...fd", half.astype(jnp.bfloat16), spread).astype(jnp.bfloat16)
    )


def forward_blocks(q_normed, k_normed, values, sign_pair):
    scores = product_of("...id,...jd->...ij", q_normed, k_normed) * DH ** (-0.5)
    weights = jnp.where(causal_mask(), scores**4, 0.0).astype(jnp.bfloat16)
    q_parts = sketch(q_normed, sign_pair)
    k_parts = sketch(k_normed, sign_pair)
    block_kv = product_of("...jr,...jd->...rd", pick_pairs(k_parts[0]), values)
    block_keys = jnp.sum(k_parts[0].astype(jnp.float32), axis=-2)
    return (scores, weights, q_parts, k_parts, block_kv, block_keys)


def before_blocks(block_kv, block_keys, prior_kv, prior_keys):
    key_state = prior_kv[..., None, :, :] + jnp.cumsum(block_kv, axis=-3) - block_kv
    key_total = prior_keys[..., None, :] + jnp.cumsum(block_keys, axis=-2) - block_keys
    return (key_state, key_total)


def after_blocks(block_u, block_w, later_u, later_w):
    rev_u = jnp.flip(jnp.cumsum(jnp.flip(block_u, -3), axis=-3), -3)
    rev_w = jnp.flip(jnp.cumsum(jnp.flip(block_w, -2), axis=-2), -2)
    return (later_u[..., None, :, :] + rev_u - block_u, later_w[..., None, :] + rev_w - block_w)


def finish_forward(weights, values, q_feats, key_state, key_total):
    state_half = key_state
    numerator = product_of("...ij,...jd->...id", weights, values) + product_of(
        "...ir,...rd->...id", q_feats, state_half
    )
    denominator = (
        1.0
        + jnp.sum(weights.astype(jnp.float32), axis=-1)
        + precise_product("...ir,...r->...i", q_feats, key_total)
    )
    return (state_half, numerator, denominator)


def backward_states(grad_in, numerator, denominator, q_feats):
    grad_float = grad_in.astype(jnp.float32)
    scaled_grad = (grad_float / denominator[..., None]).astype(jnp.bfloat16)
    den_grad = -jnp.sum(grad_float * numerator, axis=-1) / (denominator * denominator)
    block_u = product_of("...ir,...id->...rd", pick_pairs(q_feats), scaled_grad)
    block_w = precise_product("...ir,...i->...r", q_feats, den_grad)
    return (scaled_grad, den_grad, block_u, block_w)


def backward_blocks(
    scaled_grad,
    den_grad,
    scores,
    weights,
    values,
    q_normed,
    k_normed,
    state_half,
    key_total,
):
    weight_grad = product_of("...id,...jd->...ij", scaled_grad, values) + den_grad[..., None]
    score_grad = jnp.where(
        causal_mask(), 4.0 * scores**3 * weight_grad * DH ** (-0.5), 0.0
    ).astype(jnp.bfloat16)
    q_diag = product_of("...ij,...jd->...id", score_grad, k_normed)
    k_diag = product_of("...ij,...id->...jd", score_grad, q_normed)
    v_diag = product_of("...ij,...id->...jd", weights, scaled_grad)
    qf_grad = (
        product_of("...id,...rd->...ir", scaled_grad, state_half)
        + den_grad[..., None] * key_total[..., None, :]
    )
    return (q_diag, k_diag, v_diag, qf_grad)


def finish_backward(values, k_feats, later_state, later_total, v_diag):
    later_half = later_state
    kf_grad = product_of("...jd,...rd->...jr", values, later_half) + later_total[..., None, :]
    v_grad = v_diag + product_of("...jr,...rd->...jd", k_feats, later_half)
    return (kf_grad, v_grad)


def normalize(raw, gain, total):
    scale = lax.rsqrt(total / (HEADS * DH) + EPSILON)[:, None]
    return (scale, (raw.astype(jnp.float32) * scale * gain).astype(jnp.bfloat16))


def norm_back(raw, gain, scale, normed_grad, dot_total):
    raw_float = raw.astype(jnp.float32)
    return (
        scale * gain * normed_grad - raw_float * scale**3 * dot_total[:, None] / (HEADS * DH)
    ).astype(jnp.bfloat16)


def on_device(queries, keys, values, out_grad, q_gain, k_gain, signs):
    tok_rows = queries.shape[0]
    heads_here = queries.shape[1] // DH
    block_count = tok_rows // BLOCK
    sign_pair = jnp.concatenate([2 * signs[0] - 1, 2 * signs[1] - 1], axis=1).astype(jnp.bfloat16)
    q_float = queries.astype(jnp.float32)
    k_float = keys.astype(jnp.float32)
    (q_total, k_total), _ = head_sum(
        (jnp.sum(q_float * q_float, axis=-1), jnp.sum(k_float * k_float, axis=-1)), "head"
    )
    q_scale, q_normed = normalize(queries, q_gain, q_total)
    k_scale, k_normed = normalize(keys, k_gain, k_total)

    def split_heads(array):
        return (
            array.reshape(tok_rows, heads_here, DH)
            .transpose(1, 0, 2)
            .reshape(heads_here, block_count, BLOCK, DH)
        )

    def join_heads(array):
        return (
            array.reshape(heads_here, tok_rows, DH)
            .transpose(1, 0, 2)
            .reshape(tok_rows, heads_here * DH)
        )

    q_heads = split_heads(q_normed)
    k_heads = split_heads(k_normed)
    v_heads = split_heads(values)
    g_heads = split_heads(out_grad)
    scores, weights, q_parts, k_parts, block_kv, block_keys = forward_blocks(
        q_heads, k_heads, v_heads, sign_pair
    )
    sum_kv = jnp.sum(block_kv, axis=1)
    sum_keys = jnp.sum(block_keys, axis=1)
    prior_kv, prior_keys, _ = carried_in(sum_kv, sum_keys, "ctx", False)
    key_state, key_total = before_blocks(block_kv, block_keys, prior_kv, prior_keys)
    key_state = spread_pairs(key_state)
    state_half, numerator, denominator = finish_forward(
        weights, v_heads, q_parts[0], key_state, key_total
    )
    scaled_grad, den_grad, block_u, block_w = backward_states(
        g_heads, numerator, denominator, q_parts[0]
    )
    later_u, later_w, (scaled_grad, den_grad) = carried_in(
        jnp.sum(block_u, axis=1),
        jnp.sum(block_w, axis=1),
        "ctx",
        True,
        (scaled_grad, den_grad),
    )
    q_diag, k_diag, v_diag, qf_grad = backward_blocks(
        scaled_grad,
        den_grad,
        scores,
        weights,
        v_heads,
        q_heads,
        k_heads,
        state_half,
        key_total,
    )
    later_state, later_total = after_blocks(block_u, block_w, later_u, later_w)
    later_state = spread_pairs(later_state)
    kf_grad, _ = finish_backward(v_heads, k_parts[0], later_state, later_total, v_diag)
    qn_grad = join_heads(
        q_diag + sketch_back(qf_grad, q_parts[1], q_parts[2], q_parts[3], sign_pair)
    )
    kn_grad = join_heads(
        k_diag + sketch_back(kf_grad, k_parts[1], k_parts[2], k_parts[3], sign_pair)
    )
    (q_dot, k_dot), (v_diag, later_state, numerator, denominator) = head_sum(
        (
            jnp.sum(q_float * q_gain * qn_grad, axis=-1),
            jnp.sum(k_float * k_gain * kn_grad, axis=-1),
        ),
        "head",
        (v_diag, later_state, numerator, denominator),
    )
    attended = (numerator / denominator[..., None]).astype(jnp.bfloat16)
    _, v_grad = finish_backward(v_heads, k_parts[0], later_state, later_total, v_diag)
    q_grad = norm_back(queries, q_gain, q_scale, qn_grad, q_dot)
    k_grad = norm_back(keys, k_gain, k_scale, kn_grad, k_dot)
    return (join_heads(attended), q_grad, k_grad, join_heads(v_grad).astype(jnp.bfloat16))


def solution(mesh):
    in_specs = (
        P("ctx", "head"),
        P("ctx", "head"),
        P("ctx", "head"),
        P("ctx", "head"),
        P("head"),
        P("head"),
        P(),
    )
    out_specs = (P("ctx", "head"), P("ctx", "head"), P("ctx", "head"), P("ctx", "head"))
    return jax.shard_map(
        on_device, mesh=mesh, in_specs=in_specs, out_specs=out_specs, check_vma=False
    )
```

```python
import numpy as np
import jax
import jax.numpy as jnp
from jax import lax
from jax.sharding import PartitionSpec as P

HEADS = 32
DH = 128
RS = 16
BLOCK = 256


EPSILON = 1e-06
HIGHEST_PREC = lax.Precision.HIGHEST


def shift_rows(rows, step, reverse):
    widths = [(0, 0)] * rows.ndim
    if reverse:
        widths[0] = (0, step)
        return jnp.pad(rows[step:], widths)
    widths[0] = (step, 0)
    return jnp.pad(rows[:-step], widths)


def carried_in(state, totals, axis, reverse, along=()):
    count = lax.axis_size(axis)
    heads_here, rows, lanes = state.shape
    total_rows = totals.shape[1] // lanes
    room = -(-(rows + total_rows) * heads_here // (count * 8)) * 8
    padded = room * count // heads_here
    stacked = jnp.concatenate(
        [
            state,
            totals.reshape(heads_here, total_rows, lanes),
            jnp.zeros((heads_here, padded - rows - total_rows, lanes), state.dtype),
        ],
        axis=1,
    ).reshape(count, room, lanes)
    stacked, along = lax.optimization_barrier((stacked, along))
    mine = lax.all_to_all(stacked, axis, 0, 0, tiled=True)
    shifted = shift_rows(mine, 1, reverse)
    step = 1
    while step < count:
        shifted = shifted + shift_rows(shifted, step, reverse)
        step *= 2
    back = lax.all_to_all(shifted, axis, 0, 0, tiled=True).reshape(heads_here, padded, lanes)
    return (back[:, :rows], back[:, rows : rows + total_rows].reshape(totals.shape), along)


def head_sum(parts, axis, along=()):
    count = lax.axis_size(axis)
    stacked, along = lax.optimization_barrier((jnp.stack(parts), along))
    spread = jnp.broadcast_to(stacked[None], (count,) + stacked.shape)
    gathered = lax.all_to_all(spread, axis, 0, 0, tiled=True)
    summed = jnp.sum(gathered, axis=0)
    return (tuple(summed[i] for i in range(len(parts))), along)


def product_of(spec, lhs, rhs):
    return jnp.einsum(spec, lhs, rhs, preferred_element_type=jnp.float32)


def precise_product(spec, lhs, rhs):
    return jnp.einsum(
        spec, lhs.astype(jnp.float32), rhs.astype(jnp.float32), precision=HIGHEST_PREC
    )


def causal_mask():
    row_ids = lax.broadcasted_iota(jnp.int32, (BLOCK, BLOCK), 0)
    col_ids = lax.broadcasted_iota(jnp.int32, (BLOCK, BLOCK), 1)
    return row_ids >= col_ids


def sketch(inputs, sign_pair):
    projected = product_of("...d,dr->...r", inputs, sign_pair)
    left_part = projected[..., :RS]
    right_part = projected[..., RS:]
    sketched = left_part * right_part * (RS * DH) ** (-0.5)
    outer_prod = sketched[..., :, None] * sketched[..., None, :]
    sketch_feats = outer_prod.reshape(sketched.shape[:-1] + (RS * RS,)).astype(jnp.bfloat16)
    return (sketch_feats, sketched, left_part, right_part)


def sketch_back(feat_grad, sketched, left_part, right_part, sign_pair):
    grid = feat_grad.reshape(feat_grad.shape[:-1] + (RS, RS))
    symmetric = grid + jnp.swapaxes(grid, -1, -2)
    sketch_grad = jnp.sum(symmetric * sketched[..., None, :], axis=-1)
    both_grad = jnp.concatenate([sketch_grad * right_part, sketch_grad * left_part], axis=-1) * (
        RS * DH
    ) ** (-0.5)
    return precise_product("...r,dr->...d", both_grad, sign_pair)


def pair_tables():
    upper = [r * RS + c for r in range(RS) for c in range(r, RS)]
    low = np.minimum.outer(np.arange(RS), np.arange(RS)).reshape(-1)
    high = np.maximum.outer(np.arange(RS), np.arange(RS)).reshape(-1)
    owner = np.array([upper.index(a * RS + b) for a, b in zip(low, high)])
    pick = np.zeros((RS * RS, len(upper)), np.float32)
    pick[upper, np.arange(len(upper))] = 1.0
    spread = np.zeros((RS * RS, len(upper)), np.float32)
    spread[np.arange(RS * RS), owner] = 1.0
    return pick, spread


def pick_pairs(feats):
    pick = jnp.asarray(pair_tables()[0], jnp.bfloat16)
    return lax.optimization_barrier(product_of("...f,fp->...p", feats, pick).astype(jnp.bfloat16))


def spread_pairs(half):
    spread = jnp.asarray(pair_tables()[1], jnp.bfloat16)
    return lax.optimization_barrier(
        product_of("...pd,fp->...fd", half.astype(jnp.bfloat16), spread).astype(jnp.bfloat16)
    )


def forward_blocks(q_normed, k_normed, values, sign_pair):
    scores = product_of("...id,...jd->...ij", q_normed, k_normed) * DH ** (-0.5)
    weights = jnp.where(causal_mask(), scores**4, 0.0).astype(jnp.bfloat16)
    q_parts = sketch(q_normed, sign_pair)
    k_parts = sketch(k_normed, sign_pair)
    block_kv = product_of("...jr,...jd->...rd", pick_pairs(k_parts[0]), values)
    block_keys = jnp.sum(k_parts[0].astype(jnp.float32), axis=-2)
    return (scores, weights, q_parts, k_parts, block_kv, block_keys)


def before_blocks(block_kv, block_keys, prior_kv, prior_keys):
    key_state = prior_kv[..., None, :, :] + jnp.cumsum(block_kv, axis=-3) - block_kv
    key_total = prior_keys[..., None, :] + jnp.cumsum(block_keys, axis=-2) - block_keys
    return (key_state, key_total)


def after_blocks(block_u, block_w, later_u, later_w):
    rev_u = jnp.flip(jnp.cumsum(jnp.flip(block_u, -3), axis=-3), -3)
    rev_w = jnp.flip(jnp.cumsum(jnp.flip(block_w, -2), axis=-2), -2)
    return (later_u[..., None, :, :] + rev_u - block_u, later_w[..., None, :] + rev_w - block_w)


def finish_forward(weights, values, q_feats, key_state, key_total):
    state_half = key_state
    numerator = product_of("...ij,...jd->...id", weights, values) + product_of(
        "...ir,...rd->...id", q_feats, state_half
    )
    denominator = (
        1.0
        + jnp.sum(weights.astype(jnp.float32), axis=-1)
        + precise_product("...ir,...r->...i", q_feats, key_total)
    )
    return (state_half, numerator, denominator)


def backward_states(grad_in, numerator, denominator, q_feats):
    grad_float = grad_in.astype(jnp.float32)
    scaled_grad = (grad_float / denominator[..., None]).astype(jnp.bfloat16)
    den_grad = -jnp.sum(grad_float * numerator, axis=-1) / (denominator * denominator)
    block_u = product_of("...ir,...id->...rd", pick_pairs(q_feats), scaled_grad)
    block_w = precise_product("...ir,...i->...r", q_feats, den_grad)
    return (scaled_grad, den_grad, block_u, block_w)


def backward_blocks(
    scaled_grad,
    den_grad,
    scores,
    weights,
    values,
    q_normed,
    k_normed,
    state_half,
    key_total,
):
    weight_grad = product_of("...id,...jd->...ij", scaled_grad, values) + den_grad[..., None]
    score_grad = jnp.where(
        causal_mask(), 4.0 * scores**3 * weight_grad * DH ** (-0.5), 0.0
    ).astype(jnp.bfloat16)
    q_diag = product_of("...ij,...jd->...id", score_grad, k_normed)
    k_diag = product_of("...ij,...id->...jd", score_grad, q_normed)
    v_diag = product_of("...ij,...id->...jd", weights, scaled_grad)
    qf_grad = (
        product_of("...id,...rd->...ir", scaled_grad, state_half)
        + den_grad[..., None] * key_total[..., None, :]
    )
    return (q_diag, k_diag, v_diag, qf_grad)


def finish_backward(values, k_feats, later_state, later_total, v_diag):
    later_half = later_state
    kf_grad = product_of("...jd,...rd->...jr", values, later_half) + later_total[..., None, :]
    v_grad = v_diag + product_of("...jr,...rd->...jd", k_feats, later_half)
    return (kf_grad, v_grad)


def normalize(raw, gain, total):
    scale = lax.rsqrt(total / (HEADS * DH) + EPSILON)[:, None]
    return (scale, (raw.astype(jnp.float32) * scale * gain).astype(jnp.bfloat16))


def norm_back(raw, gain, scale, normed_grad, dot_total):
    raw_float = raw.astype(jnp.float32)
    return (
        scale * gain * normed_grad - raw_float * scale**3 * dot_total[:, None] / (HEADS * DH)
    ).astype(jnp.bfloat16)


def on_device(queries, keys, values, out_grad, q_gain, k_gain, signs):
    tok_rows = queries.shape[0]
    heads_here = queries.shape[1] // DH
    block_count = tok_rows // BLOCK
    sign_pair = jnp.concatenate([2 * signs[0] - 1, 2 * signs[1] - 1], axis=1).astype(jnp.bfloat16)
    q_float = queries.astype(jnp.float32)
    k_float = keys.astype(jnp.float32)
    (q_total, k_total), _ = head_sum(
        (jnp.sum(q_float * q_float, axis=-1), jnp.sum(k_float * k_float, axis=-1)), "head"
    )
    q_scale, q_normed = normalize(queries, q_gain, q_total)
    k_scale, k_normed = normalize(keys, k_gain, k_total)

    def split_heads(array):
        return (
            array.reshape(tok_rows, heads_here, DH)
            .transpose(1, 0, 2)
            .reshape(heads_here, block_count, BLOCK, DH)
        )

    def join_heads(array):
        return (
            array.reshape(heads_here, tok_rows, DH)
            .transpose(1, 0, 2)
            .reshape(tok_rows, heads_here * DH)
        )

    q_heads = split_heads(q_normed)
    k_heads = split_heads(k_normed)
    v_heads = split_heads(values)
    g_heads = split_heads(out_grad)
    scores, weights, q_parts, k_parts, block_kv, block_keys = forward_blocks(
        q_heads, k_heads, v_heads, sign_pair
    )
    sum_kv = jnp.sum(block_kv, axis=1)
    sum_keys = jnp.sum(block_keys, axis=1)
    prior_kv, prior_keys, _ = carried_in(sum_kv, sum_keys, "ctx", False)
    key_state, key_total = before_blocks(block_kv, block_keys, prior_kv, prior_keys)
    key_state = spread_pairs(key_state)
    state_half, numerator, denominator = finish_forward(
        weights, v_heads, q_parts[0], key_state, key_total
    )
    scaled_grad, den_grad, block_u, block_w = backward_states(
        g_heads, numerator, denominator, q_parts[0]
    )
    attended = (numerator / denominator[..., None]).astype(jnp.bfloat16)
    later_u, later_w, (scaled_grad, den_grad) = carried_in(
        jnp.sum(block_u, axis=1),
        jnp.sum(block_w, axis=1),
        "ctx",
        True,
        (scaled_grad, den_grad),
    )
    q_diag, k_diag, v_diag, qf_grad = backward_blocks(
        scaled_grad,
        den_grad,
        scores,
        weights,
        v_heads,
        q_heads,
        k_heads,
        state_half,
        key_total,
    )
    later_state, later_total = after_blocks(block_u, block_w, later_u, later_w)
    later_state = spread_pairs(later_state)
    kf_grad, _ = finish_backward(v_heads, k_parts[0], later_state, later_total, v_diag)
    qn_grad = join_heads(
        q_diag + sketch_back(qf_grad, q_parts[1], q_parts[2], q_parts[3], sign_pair)
    )
    kn_grad = join_heads(
        k_diag + sketch_back(kf_grad, k_parts[1], k_parts[2], k_parts[3], sign_pair)
    )
    (q_dot, k_dot), (v_diag, later_state) = head_sum(
        (
            jnp.sum(q_float * q_gain * qn_grad, axis=-1),
            jnp.sum(k_float * k_gain * kn_grad, axis=-1),
        ),
        "head",
        (v_diag, later_state),
    )
    _, v_grad = finish_backward(v_heads, k_parts[0], later_state, later_total, v_diag)
    q_grad = norm_back(queries, q_gain, q_scale, qn_grad, q_dot)
    k_grad = norm_back(keys, k_gain, k_scale, kn_grad, k_dot)
    return (join_heads(attended), q_grad, k_grad, join_heads(v_grad).astype(jnp.bfloat16))


def solution(mesh):
    in_specs = (
        P("ctx", "head"),
        P("ctx", "head"),
        P("ctx", "head"),
        P("ctx", "head"),
        P("head"),
        P("head"),
        P(),
    )
    out_specs = (P("ctx", "head"), P("ctx", "head"), P("ctx", "head"), P("ctx", "head"))
    return jax.shard_map(
        on_device, mesh=mesh, in_specs=in_specs, out_specs=out_specs, check_vma=False
    )
```

```python
import numpy as np
import jax
import jax.numpy as jnp
from jax import lax
from jax.sharding import PartitionSpec as P

HEADS = 32
DH = 128
RS = 16
BLOCK = 256


EPSILON = 1e-06
HIGHEST_PREC = lax.Precision.HIGHEST


def shift_rows(rows, step, reverse):
    widths = [(0, 0)] * rows.ndim
    if reverse:
        widths[0] = (0, step)
        return jnp.pad(rows[step:], widths)
    widths[0] = (step, 0)
    return jnp.pad(rows[:-step], widths)


def carried_in(state, totals, axis, reverse, along=()):
    count = lax.axis_size(axis)
    heads_here, rows, lanes = state.shape
    total_rows = totals.shape[1] // lanes
    room = -(-(rows + total_rows) * heads_here // (count * 8)) * 8
    padded = room * count // heads_here
    stacked = jnp.concatenate(
        [
            state,
            totals.reshape(heads_here, total_rows, lanes),
            jnp.zeros((heads_here, padded - rows - total_rows, lanes), state.dtype),
        ],
        axis=1,
    ).reshape(count, room, lanes)
    stacked, along = lax.optimization_barrier((stacked, along))
    mine = lax.all_to_all(stacked, axis, 0, 0, tiled=True)
    shifted = shift_rows(mine, 1, reverse)
    step = 1
    while step < count:
        shifted = shifted + shift_rows(shifted, step, reverse)
        step *= 2
    back = lax.all_to_all(shifted, axis, 0, 0, tiled=True).reshape(heads_here, padded, lanes)
    return (back[:, :rows], back[:, rows : rows + total_rows].reshape(totals.shape), along)


def head_sum(parts, axis, along=()):
    count = lax.axis_size(axis)
    stacked, along = lax.optimization_barrier((jnp.stack(parts), along))
    spread = jnp.broadcast_to(stacked[None], (count,) + stacked.shape)
    gathered = lax.all_to_all(spread, axis, 0, 0, tiled=True)
    summed = jnp.sum(gathered, axis=0)
    return (tuple(summed[i] for i in range(len(parts))), along)


def product_of(spec, lhs, rhs):
    return jnp.einsum(spec, lhs, rhs, preferred_element_type=jnp.float32)


def precise_product(spec, lhs, rhs):
    return jnp.einsum(
        spec, lhs.astype(jnp.float32), rhs.astype(jnp.float32), precision=HIGHEST_PREC
    )


def causal_mask():
    row_ids = lax.broadcasted_iota(jnp.int32, (BLOCK, BLOCK), 0)
    col_ids = lax.broadcasted_iota(jnp.int32, (BLOCK, BLOCK), 1)
    return row_ids >= col_ids


def sketch(inputs, sign_pair):
    projected = product_of("...d,dr->...r", inputs, sign_pair)
    left_part = projected[..., :RS]
    right_part = projected[..., RS:]
    sketched = left_part * right_part * (RS * DH) ** (-0.5)
    outer_prod = sketched[..., :, None] * sketched[..., None, :]
    sketch_feats = outer_prod.reshape(sketched.shape[:-1] + (RS * RS,)).astype(jnp.bfloat16)
    return (sketch_feats, sketched, left_part, right_part)


def sketch_back(feat_grad, sketched, left_part, right_part, sign_pair):
    grid = feat_grad.reshape(feat_grad.shape[:-1] + (RS, RS))
    symmetric = grid + jnp.swapaxes(grid, -1, -2)
    sketch_grad = jnp.sum(symmetric * sketched[..., None, :], axis=-1)
    both_grad = jnp.concatenate([sketch_grad * right_part, sketch_grad * left_part], axis=-1) * (
        RS * DH
    ) ** (-0.5)
    return precise_product("...r,dr->...d", both_grad, sign_pair)


def pair_tables():
    upper = [r * RS + c for r in range(RS) for c in range(r, RS)]
    low = np.minimum.outer(np.arange(RS), np.arange(RS)).reshape(-1)
    high = np.maximum.outer(np.arange(RS), np.arange(RS)).reshape(-1)
    owner = np.array([upper.index(a * RS + b) for a, b in zip(low, high)])
    pick = np.zeros((RS * RS, len(upper)), np.float32)
    pick[upper, np.arange(len(upper))] = 1.0
    spread = np.zeros((RS * RS, len(upper)), np.float32)
    spread[np.arange(RS * RS), owner] = 1.0
    return pick, spread


def pick_pairs(feats):
    pick = jnp.asarray(pair_tables()[0], jnp.bfloat16)
    return lax.optimization_barrier(product_of("...f,fp->...p", feats, pick).astype(jnp.bfloat16))


def spread_pairs(half):
    spread = jnp.asarray(pair_tables()[1], jnp.bfloat16)
    return lax.optimization_barrier(
        product_of("...pd,fp->...fd", half.astype(jnp.bfloat16), spread).astype(jnp.bfloat16)
    )


def forward_blocks(q_normed, k_normed, values, sign_pair):
    scores = product_of("...id,...jd->...ij", q_normed, k_normed) * DH ** (-0.5)
    weights = jnp.where(causal_mask(), scores**4, 0.0).astype(jnp.bfloat16)
    q_parts = sketch(q_normed, sign_pair)
    k_parts = sketch(k_normed, sign_pair)
    block_kv = product_of("...jr,...jd->...rd", pick_pairs(k_parts[0]), values)
    block_keys = jnp.sum(k_parts[0].astype(jnp.float32), axis=-2)
    return (scores, weights, q_parts, k_parts, block_kv, block_keys)


def before_blocks(block_kv, block_keys, prior_kv, prior_keys):
    key_state = prior_kv[..., None, :, :] + jnp.cumsum(block_kv, axis=-3) - block_kv
    key_total = prior_keys[..., None, :] + jnp.cumsum(block_keys, axis=-2) - block_keys
    return (key_state, key_total)


def after_blocks(block_u, block_w, later_u, later_w):
    rev_u = jnp.flip(jnp.cumsum(jnp.flip(block_u, -3), axis=-3), -3)
    rev_w = jnp.flip(jnp.cumsum(jnp.flip(block_w, -2), axis=-2), -2)
    return (later_u[..., None, :, :] + rev_u - block_u, later_w[..., None, :] + rev_w - block_w)


def finish_forward(weights, values, q_feats, key_state, key_total):
    state_half = key_state
    numerator = product_of("...ij,...jd->...id", weights, values) + product_of(
        "...ir,...rd->...id", q_feats, state_half
    )
    denominator = (
        1.0
        + jnp.sum(weights.astype(jnp.float32), axis=-1)
        + precise_product("...ir,...r->...i", q_feats, key_total)
    )
    return (state_half, numerator, denominator)


def backward_states(grad_in, numerator, denominator, q_feats):
    grad_float = grad_in.astype(jnp.float32)
    scaled_grad = (grad_float / denominator[..., None]).astype(jnp.bfloat16)
    den_grad = -jnp.sum(grad_float * numerator, axis=-1) / (denominator * denominator)
    block_u = product_of("...ir,...id->...rd", pick_pairs(q_feats), scaled_grad)
    block_w = precise_product("...ir,...i->...r", q_feats, den_grad)
    return (scaled_grad, den_grad, block_u, block_w)


def backward_blocks(
    scaled_grad,
    den_grad,
    scores,
    weights,
    values,
    q_normed,
    k_normed,
    state_half,
    key_total,
):
    weight_grad = product_of("...id,...jd->...ij", scaled_grad, values) + den_grad[..., None]
    score_grad = jnp.where(
        causal_mask(), 4.0 * scores**3 * weight_grad * DH ** (-0.5), 0.0
    ).astype(jnp.bfloat16)
    q_diag = product_of("...ij,...jd->...id", score_grad, k_normed)
    k_diag = product_of("...ij,...id->...jd", score_grad, q_normed)
    v_diag = product_of("...ij,...id->...jd", weights, scaled_grad)
    qf_grad = (
        product_of("...id,...rd->...ir", scaled_grad, state_half)
        + den_grad[..., None] * key_total[..., None, :]
    )
    return (q_diag, k_diag, v_diag, qf_grad)


def finish_backward(values, k_feats, later_state, later_total, v_diag):
    later_half = later_state
    kf_grad = product_of("...jd,...rd->...jr", values, later_half) + later_total[..., None, :]
    v_grad = v_diag + product_of("...jr,...rd->...jd", k_feats, later_half)
    return (kf_grad, v_grad)


def normalize(raw, gain, total):
    scale = lax.rsqrt(total / (HEADS * DH) + EPSILON)[:, None]
    return (scale, (raw.astype(jnp.float32) * scale * gain).astype(jnp.bfloat16))


def norm_back(raw, gain, scale, normed_grad, dot_total):
    raw_float = raw.astype(jnp.float32)
    return (
        scale * gain * normed_grad - raw_float * scale**3 * dot_total[:, None] / (HEADS * DH)
    ).astype(jnp.bfloat16)


def on_device(queries, keys, values, out_grad, q_gain, k_gain, signs):
    tok_rows = queries.shape[0]
    heads_here = queries.shape[1] // DH
    block_count = tok_rows // BLOCK
    sign_pair = jnp.concatenate([2 * signs[0] - 1, 2 * signs[1] - 1], axis=1).astype(jnp.bfloat16)
    q_float = queries.astype(jnp.float32)
    k_float = keys.astype(jnp.float32)
    (q_total, k_total), _ = head_sum(
        (jnp.sum(q_float * q_float, axis=-1), jnp.sum(k_float * k_float, axis=-1)), "head"
    )
    q_scale, q_normed = normalize(queries, q_gain, q_total)
    k_scale, k_normed = normalize(keys, k_gain, k_total)

    def split_heads(array):
        return (
            array.reshape(tok_rows, heads_here, DH)
            .transpose(1, 0, 2)
            .reshape(heads_here, block_count, BLOCK, DH)
        )

    def join_heads(array):
        return (
            array.reshape(heads_here, tok_rows, DH)
            .transpose(1, 0, 2)
            .reshape(tok_rows, heads_here * DH)
        )

    q_heads = split_heads(q_normed)
    k_heads = split_heads(k_normed)
    v_heads = split_heads(values)
    g_heads = split_heads(out_grad)
    scores, weights, q_parts, k_parts, block_kv, block_keys = forward_blocks(
        q_heads, k_heads, v_heads, sign_pair
    )
    sum_kv = jnp.sum(block_kv, axis=1)
    sum_keys = jnp.sum(block_keys, axis=1)
    prior_kv, prior_keys, _ = carried_in(sum_kv, sum_keys, "ctx", False)
    key_state, key_total = before_blocks(block_kv, block_keys, prior_kv, prior_keys)
    key_state = spread_pairs(key_state)
    state_half, numerator, denominator = finish_forward(
        weights, v_heads, q_parts[0], key_state, key_total
    )
    scaled_grad, den_grad, block_u, block_w = backward_states(
        g_heads, numerator, denominator, q_parts[0]
    )
    later_u, later_w, (scaled_grad, den_grad, numerator, denominator) = carried_in(
        jnp.sum(block_u, axis=1),
        jnp.sum(block_w, axis=1),
        "ctx",
        True,
        (scaled_grad, den_grad, numerator, denominator),
    )
    spread_den = jnp.broadcast_to(
        denominator.reshape(heads_here, tok_rows)[..., None], (heads_here, tok_rows, DH)
    )
    attended = (join_heads(numerator) / join_heads(spread_den)).astype(jnp.bfloat16)
    q_diag, k_diag, v_diag, qf_grad = backward_blocks(
        scaled_grad,
        den_grad,
        scores,
        weights,
        v_heads,
        q_heads,
        k_heads,
        state_half,
        key_total,
    )
    later_state, later_total = after_blocks(block_u, block_w, later_u, later_w)
    later_state = spread_pairs(later_state)
    kf_grad, _ = finish_backward(v_heads, k_parts[0], later_state, later_total, v_diag)
    qn_grad = join_heads(
        q_diag + sketch_back(qf_grad, q_parts[1], q_parts[2], q_parts[3], sign_pair)
    )
    kn_grad = join_heads(
        k_diag + sketch_back(kf_grad, k_parts[1], k_parts[2], k_parts[3], sign_pair)
    )
    (q_dot, k_dot), (v_diag, later_state) = head_sum(
        (
            jnp.sum(q_float * q_gain * qn_grad, axis=-1),
            jnp.sum(k_float * k_gain * kn_grad, axis=-1),
        ),
        "head",
        (v_diag, later_state),
    )
    _, v_grad = finish_backward(v_heads, k_parts[0], later_state, later_total, v_diag)
    q_grad = norm_back(queries, q_gain, q_scale, qn_grad, q_dot)
    k_grad = norm_back(keys, k_gain, k_scale, kn_grad, k_dot)
    return (attended, q_grad, k_grad, join_heads(v_grad).astype(jnp.bfloat16))


def solution(mesh):
    in_specs = (
        P("ctx", "head"),
        P("ctx", "head"),
        P("ctx", "head"),
        P("ctx", "head"),
        P("head"),
        P("head"),
        P(),
    )
    out_specs = (P("ctx", "head"), P("ctx", "head"), P("ctx", "head"), P("ctx", "head"))
    return jax.shard_map(
        on_device, mesh=mesh, in_specs=in_specs, out_specs=out_specs, check_vma=False
    )
```

```python
import numpy as np
import jax
import jax.numpy as jnp
from jax import lax
from jax.sharding import PartitionSpec as P

HEADS = 32
DH = 128
RS = 16
BLOCK = 256


EPSILON = 1e-06
HIGHEST_PREC = lax.Precision.HIGHEST


def shift_rows(rows, step, reverse):
    widths = [(0, 0)] * rows.ndim
    if reverse:
        widths[0] = (0, step)
        return jnp.pad(rows[step:], widths)
    widths[0] = (step, 0)
    return jnp.pad(rows[:-step], widths)


def carried_in(state, totals, axis, reverse, along=()):
    count = lax.axis_size(axis)
    heads_here, rows, lanes = state.shape
    total_rows = totals.shape[1] // lanes
    room = -(-(rows + total_rows) * heads_here // (count * 8)) * 8
    padded = room * count // heads_here
    stacked = jnp.concatenate(
        [
            state,
            totals.reshape(heads_here, total_rows, lanes),
            jnp.zeros((heads_here, padded - rows - total_rows, lanes), state.dtype),
        ],
        axis=1,
    ).reshape(count, room, lanes)
    stacked, along = lax.optimization_barrier((stacked, along))
    mine = lax.all_to_all(stacked, axis, 0, 0, tiled=True)
    shifted = shift_rows(mine, 1, reverse)
    step = 1
    while step < count:
        shifted = shifted + shift_rows(shifted, step, reverse)
        step *= 2
    back = lax.all_to_all(shifted, axis, 0, 0, tiled=True).reshape(heads_here, padded, lanes)
    return (back[:, :rows], back[:, rows : rows + total_rows].reshape(totals.shape), along)


def head_sum(parts, axis, along=()):
    count = lax.axis_size(axis)
    stacked, along = lax.optimization_barrier((jnp.stack(parts), along))
    spread = jnp.broadcast_to(stacked[None], (count,) + stacked.shape)
    gathered = lax.all_to_all(spread, axis, 0, 0, tiled=True)
    summed = jnp.sum(gathered, axis=0)
    return (tuple(summed[i] for i in range(len(parts))), along)


def product_of(spec, lhs, rhs):
    return jnp.einsum(spec, lhs, rhs, preferred_element_type=jnp.float32)


def precise_product(spec, lhs, rhs):
    return jnp.einsum(
        spec, lhs.astype(jnp.float32), rhs.astype(jnp.float32), precision=HIGHEST_PREC
    )


def causal_mask():
    row_ids = lax.broadcasted_iota(jnp.int32, (BLOCK, BLOCK), 0)
    col_ids = lax.broadcasted_iota(jnp.int32, (BLOCK, BLOCK), 1)
    return row_ids >= col_ids


def sketch(inputs, sign_pair):
    projected = product_of("...d,dr->...r", inputs, sign_pair)
    left_part = projected[..., :RS]
    right_part = projected[..., RS:]
    sketched = left_part * right_part * (RS * DH) ** (-0.5)
    outer_prod = sketched[..., :, None] * sketched[..., None, :]
    sketch_feats = outer_prod.reshape(sketched.shape[:-1] + (RS * RS,)).astype(jnp.bfloat16)
    return (sketch_feats, sketched, left_part, right_part)


def sketch_back(feat_grad, sketched, left_part, right_part, sign_pair):
    grid = feat_grad.reshape(feat_grad.shape[:-1] + (RS, RS))
    symmetric = grid + jnp.swapaxes(grid, -1, -2)
    sketch_grad = jnp.sum(symmetric * sketched[..., None, :], axis=-1)
    both_grad = jnp.concatenate([sketch_grad * right_part, sketch_grad * left_part], axis=-1) * (
        RS * DH
    ) ** (-0.5)
    return precise_product("...r,dr->...d", both_grad, sign_pair)


def pair_tables():
    upper = [r * RS + c for r in range(RS) for c in range(r, RS)]
    low = np.minimum.outer(np.arange(RS), np.arange(RS)).reshape(-1)
    high = np.maximum.outer(np.arange(RS), np.arange(RS)).reshape(-1)
    owner = np.array([upper.index(a * RS + b) for a, b in zip(low, high)])
    pick = np.zeros((RS * RS, len(upper)), np.float32)
    pick[upper, np.arange(len(upper))] = 1.0
    spread = np.zeros((RS * RS, len(upper)), np.float32)
    spread[np.arange(RS * RS), owner] = 1.0
    return pick, spread


def pick_pairs(feats):
    pick = jnp.asarray(pair_tables()[0], jnp.bfloat16)
    return lax.optimization_barrier(product_of("...f,fp->...p", feats, pick).astype(jnp.bfloat16))


def spread_pairs(half):
    spread = jnp.asarray(pair_tables()[1], jnp.bfloat16)
    return lax.optimization_barrier(
        product_of("...pd,fp->...fd", half.astype(jnp.bfloat16), spread).astype(jnp.bfloat16)
    )


def forward_blocks(q_normed, k_normed, values, sign_pair):
    scores = product_of("...id,...jd->...ij", q_normed, k_normed) * DH ** (-0.5)
    weights = jnp.where(causal_mask(), scores**4, 0.0).astype(jnp.bfloat16)
    q_parts = sketch(q_normed, sign_pair)
    k_parts = sketch(k_normed, sign_pair)
    block_kv = product_of("...jr,...jd->...rd", pick_pairs(k_parts[0]), values)
    block_keys = jnp.sum(k_parts[0].astype(jnp.float32), axis=-2)
    return (scores, weights, q_parts, k_parts, block_kv, block_keys)


def before_blocks(block_kv, block_keys, prior_kv, prior_keys):
    key_state = prior_kv[..., None, :, :] + jnp.cumsum(block_kv, axis=-3) - block_kv
    key_total = prior_keys[..., None, :] + jnp.cumsum(block_keys, axis=-2) - block_keys
    return (key_state, key_total)


def after_blocks(block_u, block_w, later_u, later_w):
    rev_u = jnp.flip(jnp.cumsum(jnp.flip(block_u, -3), axis=-3), -3)
    rev_w = jnp.flip(jnp.cumsum(jnp.flip(block_w, -2), axis=-2), -2)
    return (later_u[..., None, :, :] + rev_u - block_u, later_w[..., None, :] + rev_w - block_w)


def finish_forward(weights, values, q_feats, key_state, key_total):
    state_half = key_state
    numerator = product_of("...ij,...jd->...id", weights, values) + product_of(
        "...ir,...rd->...id", q_feats, state_half
    )
    denominator = (
        1.0
        + jnp.sum(weights.astype(jnp.float32), axis=-1)
        + precise_product("...ir,...r->...i", q_feats, key_total)
    )
    return (state_half, numerator, denominator)


def backward_states(grad_in, numerator, denominator, q_feats):
    grad_float = grad_in.astype(jnp.float32)
    scaled_grad = (grad_float / denominator[..., None]).astype(jnp.bfloat16)
    den_grad = -jnp.sum(grad_float * numerator, axis=-1) / (denominator * denominator)
    block_u = product_of("...ir,...id->...rd", pick_pairs(q_feats), scaled_grad)
    block_w = precise_product("...ir,...i->...r", q_feats, den_grad)
    return (scaled_grad, den_grad, block_u, block_w)


def backward_blocks(
    scaled_grad,
    den_grad,
    scores,
    weights,
    values,
    q_normed,
    k_normed,
    state_half,
    key_total,
):
    weight_grad = product_of("...id,...jd->...ij", scaled_grad, values) + den_grad[..., None]
    score_grad = jnp.where(
        causal_mask(), 4.0 * scores**3 * weight_grad * DH ** (-0.5), 0.0
    ).astype(jnp.bfloat16)
    q_diag = product_of("...ij,...jd->...id", score_grad, k_normed)
    k_diag = product_of("...ij,...id->...jd", score_grad, q_normed)
    v_diag = product_of("...ij,...id->...jd", weights, scaled_grad)
    qf_grad = (
        product_of("...id,...rd->...ir", scaled_grad, state_half)
        + den_grad[..., None] * key_total[..., None, :]
    )
    return (q_diag, k_diag, v_diag, qf_grad)


def finish_backward(values, k_feats, later_state, later_total, v_diag):
    later_half = later_state
    kf_grad = product_of("...jd,...rd->...jr", values, later_half) + later_total[..., None, :]
    v_grad = v_diag + product_of("...jr,...rd->...jd", k_feats, later_half)
    return (kf_grad, v_grad)


def normalize(raw, gain, total):
    scale = lax.rsqrt(total / (HEADS * DH) + EPSILON)[:, None]
    return (scale, (raw.astype(jnp.float32) * scale * gain).astype(jnp.bfloat16))


def norm_terms(raw, gain, scale, normed_grad):
    return (scale * gain * normed_grad, raw.astype(jnp.float32) * scale**3)


def norm_back(terms, dot_total):
    direct, cross = terms
    return (direct - cross * dot_total[:, None] / (HEADS * DH)).astype(jnp.bfloat16)


def on_device(queries, keys, values, out_grad, q_gain, k_gain, signs):
    tok_rows = queries.shape[0]
    heads_here = queries.shape[1] // DH
    block_count = tok_rows // BLOCK
    sign_pair = jnp.concatenate([2 * signs[0] - 1, 2 * signs[1] - 1], axis=1).astype(jnp.bfloat16)
    q_float = queries.astype(jnp.float32)
    k_float = keys.astype(jnp.float32)
    (q_total, k_total), _ = head_sum(
        (jnp.sum(q_float * q_float, axis=-1), jnp.sum(k_float * k_float, axis=-1)), "head"
    )
    q_scale, q_normed = normalize(queries, q_gain, q_total)
    k_scale, k_normed = normalize(keys, k_gain, k_total)

    def split_heads(array):
        return (
            array.reshape(tok_rows, heads_here, DH)
            .transpose(1, 0, 2)
            .reshape(heads_here, block_count, BLOCK, DH)
        )

    def join_heads(array):
        return (
            array.reshape(heads_here, tok_rows, DH)
            .transpose(1, 0, 2)
            .reshape(tok_rows, heads_here * DH)
        )

    q_heads = split_heads(q_normed)
    k_heads = split_heads(k_normed)
    v_heads = split_heads(values)
    g_heads = split_heads(out_grad)
    scores, weights, q_parts, k_parts, block_kv, block_keys = forward_blocks(
        q_heads, k_heads, v_heads, sign_pair
    )
    sum_kv = jnp.sum(block_kv, axis=1)
    sum_keys = jnp.sum(block_keys, axis=1)
    prior_kv, prior_keys, _ = carried_in(sum_kv, sum_keys, "ctx", False)
    key_state, key_total = before_blocks(block_kv, block_keys, prior_kv, prior_keys)
    key_state = spread_pairs(key_state)
    state_half, numerator, denominator = finish_forward(
        weights, v_heads, q_parts[0], key_state, key_total
    )
    scaled_grad, den_grad, block_u, block_w = backward_states(
        g_heads, numerator, denominator, q_parts[0]
    )
    later_u, later_w, (scaled_grad, den_grad, numerator, denominator) = carried_in(
        jnp.sum(block_u, axis=1),
        jnp.sum(block_w, axis=1),
        "ctx",
        True,
        (scaled_grad, den_grad, numerator, denominator),
    )
    attended = (numerator / denominator[..., None]).astype(jnp.bfloat16)
    q_diag, k_diag, v_diag, qf_grad = backward_blocks(
        scaled_grad,
        den_grad,
        scores,
        weights,
        v_heads,
        q_heads,
        k_heads,
        state_half,
        key_total,
    )
    later_state, later_total = after_blocks(block_u, block_w, later_u, later_w)
    later_state = spread_pairs(later_state)
    kf_grad, _ = finish_backward(v_heads, k_parts[0], later_state, later_total, v_diag)
    qn_grad = join_heads(
        q_diag + sketch_back(qf_grad, q_parts[1], q_parts[2], q_parts[3], sign_pair)
    )
    kn_grad = join_heads(
        k_diag + sketch_back(kf_grad, k_parts[1], k_parts[2], k_parts[3], sign_pair)
    )
    q_terms = norm_terms(queries, q_gain, q_scale, qn_grad)
    k_terms = norm_terms(keys, k_gain, k_scale, kn_grad)
    (q_dot, k_dot), (v_diag, later_state, q_terms, k_terms) = head_sum(
        (
            jnp.sum(q_float * q_gain * qn_grad, axis=-1),
            jnp.sum(k_float * k_gain * kn_grad, axis=-1),
        ),
        "head",
        (v_diag, later_state, q_terms, k_terms),
    )
    _, v_grad = finish_backward(v_heads, k_parts[0], later_state, later_total, v_diag)
    q_grad = norm_back(q_terms, q_dot)
    k_grad = norm_back(k_terms, k_dot)
    return (join_heads(attended), q_grad, k_grad, join_heads(v_grad).astype(jnp.bfloat16))


def solution(mesh):
    in_specs = (
        P("ctx", "head"),
        P("ctx", "head"),
        P("ctx", "head"),
        P("ctx", "head"),
        P("head"),
        P("head"),
        P(),
    )
    out_specs = (P("ctx", "head"), P("ctx", "head"), P("ctx", "head"), P("ctx", "head"))
    return jax.shard_map(
        on_device, mesh=mesh, in_specs=in_specs, out_specs=out_specs, check_vma=False
    )
```

```python
import numpy as np
import jax
import jax.numpy as jnp
from jax import lax
from jax.sharding import PartitionSpec as P

HEADS = 32
DH = 128
RS = 16
BLOCK = 256


EPSILON = 1e-06
HIGHEST_PREC = lax.Precision.HIGHEST


def shift_rows(rows, step, reverse):
    widths = [(0, 0)] * rows.ndim
    if reverse:
        widths[0] = (0, step)
        return jnp.pad(rows[step:], widths)
    widths[0] = (step, 0)
    return jnp.pad(rows[:-step], widths)


def carried_in(state, totals, axis, reverse, along=()):
    count = lax.axis_size(axis)
    heads_here, rows, lanes = state.shape
    total_rows = totals.shape[1] // lanes
    room = -(-(rows + total_rows) * heads_here // (count * 8)) * 8
    padded = room * count // heads_here
    stacked = jnp.concatenate(
        [
            state,
            totals.reshape(heads_here, total_rows, lanes),
            jnp.zeros((heads_here, padded - rows - total_rows, lanes), state.dtype),
        ],
        axis=1,
    ).reshape(count, room, lanes)
    stacked, along = lax.optimization_barrier((stacked, along))
    mine = lax.all_to_all(stacked, axis, 0, 0, tiled=True)
    shifted = shift_rows(mine, 1, reverse)
    step = 1
    while step < count:
        shifted = shifted + shift_rows(shifted, step, reverse)
        step *= 2
    back = lax.all_to_all(shifted, axis, 0, 0, tiled=True).reshape(heads_here, padded, lanes)
    return (back[:, :rows], back[:, rows : rows + total_rows].reshape(totals.shape), along)


def head_sum(parts, axis, along=()):
    count = lax.axis_size(axis)
    stacked, along = lax.optimization_barrier((jnp.stack(parts), along))
    spread = jnp.broadcast_to(stacked[None], (count,) + stacked.shape)
    gathered = lax.all_to_all(spread, axis, 0, 0, tiled=True)
    summed = jnp.sum(gathered, axis=0)
    return (tuple(summed[i] for i in range(len(parts))), along)


def product_of(spec, lhs, rhs):
    return jnp.einsum(spec, lhs, rhs, preferred_element_type=jnp.float32)


def precise_product(spec, lhs, rhs):
    return jnp.einsum(
        spec, lhs.astype(jnp.float32), rhs.astype(jnp.float32), precision=HIGHEST_PREC
    )


def causal_mask():
    row_ids = lax.broadcasted_iota(jnp.int32, (BLOCK, BLOCK), 0)
    col_ids = lax.broadcasted_iota(jnp.int32, (BLOCK, BLOCK), 1)
    return row_ids >= col_ids


def sketch(inputs, sign_pair):
    projected = product_of("...d,dr->...r", inputs, sign_pair)
    left_part = projected[..., :RS]
    right_part = projected[..., RS:]
    sketched = left_part * right_part * (RS * DH) ** (-0.5)
    outer_prod = sketched[..., :, None] * sketched[..., None, :]
    sketch_feats = outer_prod.reshape(sketched.shape[:-1] + (RS * RS,)).astype(jnp.bfloat16)
    return (sketch_feats, sketched, left_part, right_part)


def sketch_back(feat_grad, sketched, left_part, right_part, sign_pair):
    grid = feat_grad.reshape(feat_grad.shape[:-1] + (RS, RS))
    symmetric = grid + jnp.swapaxes(grid, -1, -2)
    sketch_grad = jnp.sum(symmetric * sketched[..., None, :], axis=-1)
    both_grad = jnp.concatenate([sketch_grad * right_part, sketch_grad * left_part], axis=-1) * (
        RS * DH
    ) ** (-0.5)
    return precise_product("...r,dr->...d", both_grad, sign_pair)


def pair_tables():
    upper = [r * RS + c for r in range(RS) for c in range(r, RS)]
    low = np.minimum.outer(np.arange(RS), np.arange(RS)).reshape(-1)
    high = np.maximum.outer(np.arange(RS), np.arange(RS)).reshape(-1)
    owner = np.array([upper.index(a * RS + b) for a, b in zip(low, high)])
    pick = np.zeros((RS * RS, len(upper)), np.float32)
    pick[upper, np.arange(len(upper))] = 1.0
    spread = np.zeros((RS * RS, len(upper)), np.float32)
    spread[np.arange(RS * RS), owner] = 1.0
    return pick, spread


def pick_pairs(feats):
    pick = jnp.asarray(pair_tables()[0], jnp.bfloat16)
    return lax.optimization_barrier(product_of("...f,fp->...p", feats, pick).astype(jnp.bfloat16))


def spread_pairs(half):
    spread = jnp.asarray(pair_tables()[1], jnp.bfloat16)
    return lax.optimization_barrier(
        product_of("...pd,fp->...fd", half.astype(jnp.bfloat16), spread).astype(jnp.bfloat16)
    )


def forward_blocks(q_normed, k_normed, values, sign_pair):
    scores = product_of("...id,...jd->...ij", q_normed, k_normed) * DH ** (-0.5)
    weights = jnp.where(causal_mask(), scores**4, 0.0).astype(jnp.bfloat16)
    q_parts = sketch(q_normed, sign_pair)
    k_parts = sketch(k_normed, sign_pair)
    block_kv = product_of("...jr,...jd->...rd", pick_pairs(k_parts[0]), values)
    block_keys = jnp.sum(k_parts[0].astype(jnp.float32), axis=-2)
    return (scores, weights, q_parts, k_parts, block_kv, block_keys)


def before_blocks(block_kv, block_keys, prior_kv, prior_keys):
    key_state = prior_kv[..., None, :, :] + jnp.cumsum(block_kv, axis=-3) - block_kv
    key_total = prior_keys[..., None, :] + jnp.cumsum(block_keys, axis=-2) - block_keys
    return (key_state, key_total)


def after_blocks(block_u, block_w, later_u, later_w):
    rev_u = jnp.flip(jnp.cumsum(jnp.flip(block_u, -3), axis=-3), -3)
    rev_w = jnp.flip(jnp.cumsum(jnp.flip(block_w, -2), axis=-2), -2)
    return (later_u[..., None, :, :] + rev_u - block_u, later_w[..., None, :] + rev_w - block_w)


def finish_forward(weights, values, q_feats, key_state, key_total):
    state_half = key_state
    numerator = product_of("...ij,...jd->...id", weights, values) + product_of(
        "...ir,...rd->...id", q_feats, state_half
    )
    denominator = (
        1.0
        + jnp.sum(weights.astype(jnp.float32), axis=-1)
        + precise_product("...ir,...r->...i", q_feats, key_total)
    )
    return (state_half, numerator, denominator)


def backward_states(grad_in, numerator, denominator, q_feats):
    grad_float = grad_in.astype(jnp.float32)
    scaled_grad = (grad_float / denominator[..., None]).astype(jnp.bfloat16)
    den_grad = -jnp.sum(grad_float * numerator, axis=-1) / (denominator * denominator)
    block_u = product_of("...ir,...id->...rd", pick_pairs(q_feats), scaled_grad)
    block_w = precise_product("...ir,...i->...r", q_feats, den_grad)
    return (scaled_grad, den_grad, block_u, block_w)


def backward_blocks(
    scaled_grad,
    den_grad,
    scores,
    weights,
    values,
    q_normed,
    k_normed,
    state_half,
    key_total,
):
    weight_grad = product_of("...id,...jd->...ij", scaled_grad, values) + den_grad[..., None]
    score_grad = jnp.where(
        causal_mask(), 4.0 * scores**3 * weight_grad * DH ** (-0.5), 0.0
    ).astype(jnp.bfloat16)
    q_diag = product_of("...ij,...jd->...id", score_grad, k_normed)
    k_diag = product_of("...ij,...id->...jd", score_grad, q_normed)
    v_diag = product_of("...ij,...id->...jd", weights, scaled_grad)
    qf_grad = (
        product_of("...id,...rd->...ir", scaled_grad, state_half)
        + den_grad[..., None] * key_total[..., None, :]
    )
    return (q_diag, k_diag, v_diag, qf_grad)


def finish_backward(values, k_feats, later_state, later_total, v_diag):
    later_half = later_state
    kf_grad = product_of("...jd,...rd->...jr", values, later_half) + later_total[..., None, :]
    v_grad = v_diag + product_of("...jr,...rd->...jd", k_feats, later_half)
    return (kf_grad, v_grad)


def normalize(raw, gain, total):
    scale = lax.rsqrt(total / (HEADS * DH) + EPSILON)[:, None]
    return (scale, (raw.astype(jnp.float32) * scale * gain).astype(jnp.bfloat16))


def norm_back(raw, gain, scale, normed_grad, dot_total):
    raw_float = raw.astype(jnp.float32)
    return (
        scale * gain * normed_grad - raw_float * scale**3 * dot_total[:, None] / (HEADS * DH)
    ).astype(jnp.bfloat16)


def on_device(queries, keys, values, out_grad, q_gain, k_gain, signs):
    tok_rows = queries.shape[0]
    heads_here = queries.shape[1] // DH
    block_count = tok_rows // BLOCK
    sign_pair = jnp.concatenate([2 * signs[0] - 1, 2 * signs[1] - 1], axis=1).astype(jnp.bfloat16)
    q_float = queries.astype(jnp.float32)
    k_float = keys.astype(jnp.float32)
    both = jnp.stack([q_float, k_float])
    squares = jnp.sum(both * both, axis=-1)
    (q_total, k_total), _ = head_sum((squares[0], squares[1]), "head")
    q_scale, q_normed = normalize(queries, q_gain, q_total)
    k_scale, k_normed = normalize(keys, k_gain, k_total)

    def split_heads(array):
        return (
            array.reshape(tok_rows, heads_here, DH)
            .transpose(1, 0, 2)
            .reshape(heads_here, block_count, BLOCK, DH)
        )

    def join_heads(array):
        return (
            array.reshape(heads_here, tok_rows, DH)
            .transpose(1, 0, 2)
            .reshape(tok_rows, heads_here * DH)
        )

    q_heads = split_heads(q_normed)
    k_heads = split_heads(k_normed)
    v_heads = split_heads(values)
    g_heads = split_heads(out_grad)
    scores, weights, q_parts, k_parts, block_kv, block_keys = forward_blocks(
        q_heads, k_heads, v_heads, sign_pair
    )
    sum_kv = jnp.sum(block_kv, axis=1)
    sum_keys = jnp.sum(block_keys, axis=1)
    prior_kv, prior_keys, _ = carried_in(sum_kv, sum_keys, "ctx", False)
    key_state, key_total = before_blocks(block_kv, block_keys, prior_kv, prior_keys)
    key_state = spread_pairs(key_state)
    state_half, numerator, denominator = finish_forward(
        weights, v_heads, q_parts[0], key_state, key_total
    )
    scaled_grad, den_grad, block_u, block_w = backward_states(
        g_heads, numerator, denominator, q_parts[0]
    )
    later_u, later_w, (scaled_grad, den_grad, numerator, denominator) = carried_in(
        jnp.sum(block_u, axis=1),
        jnp.sum(block_w, axis=1),
        "ctx",
        True,
        (scaled_grad, den_grad, numerator, denominator),
    )
    attended = (numerator / denominator[..., None]).astype(jnp.bfloat16)
    q_diag, k_diag, v_diag, qf_grad = backward_blocks(
        scaled_grad,
        den_grad,
        scores,
        weights,
        v_heads,
        q_heads,
        k_heads,
        state_half,
        key_total,
    )
    later_state, later_total = after_blocks(block_u, block_w, later_u, later_w)
    later_state = spread_pairs(later_state)
    kf_grad, _ = finish_backward(v_heads, k_parts[0], later_state, later_total, v_diag)
    qn_grad = join_heads(
        q_diag + sketch_back(qf_grad, q_parts[1], q_parts[2], q_parts[3], sign_pair)
    )
    kn_grad = join_heads(
        k_diag + sketch_back(kf_grad, k_parts[1], k_parts[2], k_parts[3], sign_pair)
    )
    (q_dot, k_dot), (v_diag, later_state) = head_sum(
        (
            jnp.sum(q_float * q_gain * qn_grad, axis=-1),
            jnp.sum(k_float * k_gain * kn_grad, axis=-1),
        ),
        "head",
        (v_diag, later_state),
    )
    _, v_grad = finish_backward(v_heads, k_parts[0], later_state, later_total, v_diag)
    q_grad = norm_back(queries, q_gain, q_scale, qn_grad, q_dot)
    k_grad = norm_back(keys, k_gain, k_scale, kn_grad, k_dot)
    return (join_heads(attended), q_grad, k_grad, join_heads(v_grad).astype(jnp.bfloat16))


def solution(mesh):
    in_specs = (
        P("ctx", "head"),
        P("ctx", "head"),
        P("ctx", "head"),
        P("ctx", "head"),
        P("head"),
        P("head"),
        P(),
    )
    out_specs = (P("ctx", "head"), P("ctx", "head"), P("ctx", "head"), P("ctx", "head"))
    return jax.shard_map(
        on_device, mesh=mesh, in_specs=in_specs, out_specs=out_specs, check_vma=False
    )
```

```python
import numpy as np
import jax
import jax.numpy as jnp
from jax import lax
from jax.sharding import PartitionSpec as P

HEADS = 32
DH = 128
RS = 16
BLOCK = 256


EPSILON = 1e-06
HIGHEST_PREC = lax.Precision.HIGHEST


def shift_rows(rows, step, reverse):
    widths = [(0, 0)] * rows.ndim
    if reverse:
        widths[0] = (0, step)
        return jnp.pad(rows[step:], widths)
    widths[0] = (step, 0)
    return jnp.pad(rows[:-step], widths)


def carried_in(state, totals, axis, reverse, along=()):
    count = lax.axis_size(axis)
    heads_here, rows, lanes = state.shape
    total_rows = totals.shape[1] // lanes
    room = -(-(rows + total_rows) * heads_here // (count * 8)) * 8
    padded = room * count // heads_here
    stacked = jnp.concatenate(
        [
            state,
            totals.reshape(heads_here, total_rows, lanes),
            jnp.zeros((heads_here, padded - rows - total_rows, lanes), state.dtype),
        ],
        axis=1,
    ).reshape(count, room, lanes)
    stacked, along = lax.optimization_barrier((stacked, along))
    mine = lax.all_to_all(stacked, axis, 0, 0, tiled=True)
    shifted = shift_rows(mine, 1, reverse)
    step = 1
    while step < count:
        shifted = shifted + shift_rows(shifted, step, reverse)
        step *= 2
    back = lax.all_to_all(shifted, axis, 0, 0, tiled=True).reshape(heads_here, padded, lanes)
    return (back[:, :rows], back[:, rows : rows + total_rows].reshape(totals.shape), along)


def head_sum(parts, axis, along=()):
    count = lax.axis_size(axis)
    stacked, along = lax.optimization_barrier((jnp.stack(parts), along))
    spread = jnp.broadcast_to(stacked[None], (count,) + stacked.shape)
    gathered = lax.all_to_all(spread, axis, 0, 0, tiled=True)
    summed = jnp.sum(gathered, axis=0)
    return (tuple(summed[i] for i in range(len(parts))), along)


def product_of(spec, lhs, rhs):
    return jnp.einsum(spec, lhs, rhs, preferred_element_type=jnp.float32)


def precise_product(spec, lhs, rhs):
    return jnp.einsum(
        spec, lhs.astype(jnp.float32), rhs.astype(jnp.float32), precision=HIGHEST_PREC
    )


def causal_mask():
    row_ids = lax.broadcasted_iota(jnp.int32, (BLOCK, BLOCK), 0)
    col_ids = lax.broadcasted_iota(jnp.int32, (BLOCK, BLOCK), 1)
    return row_ids >= col_ids


def sketch(inputs, sign_pair):
    projected = product_of("...d,dr->...r", inputs, sign_pair)
    left_part = projected[..., :RS]
    right_part = projected[..., RS:]
    sketched = left_part * right_part * (RS * DH) ** (-0.5)
    outer_prod = sketched[..., :, None] * sketched[..., None, :]
    sketch_feats = outer_prod.reshape(sketched.shape[:-1] + (RS * RS,)).astype(jnp.bfloat16)
    return (sketch_feats, sketched, left_part, right_part)


def sketch_back(feat_grad, sketched, left_part, right_part, sign_pair):
    grid = feat_grad.reshape(feat_grad.shape[:-1] + (RS, RS))
    symmetric = grid + jnp.swapaxes(grid, -1, -2)
    sketch_grad = jnp.sum(symmetric * sketched[..., None, :], axis=-1)
    both_grad = jnp.concatenate([sketch_grad * right_part, sketch_grad * left_part], axis=-1) * (
        RS * DH
    ) ** (-0.5)
    return precise_product("...r,dr->...d", both_grad, sign_pair)


def pair_tables():
    upper = [r * RS + c for r in range(RS) for c in range(r, RS)]
    low = np.minimum.outer(np.arange(RS), np.arange(RS)).reshape(-1)
    high = np.maximum.outer(np.arange(RS), np.arange(RS)).reshape(-1)
    owner = np.array([upper.index(a * RS + b) for a, b in zip(low, high)])
    pick = np.zeros((RS * RS, len(upper)), np.float32)
    pick[upper, np.arange(len(upper))] = 1.0
    spread = np.zeros((RS * RS, len(upper)), np.float32)
    spread[np.arange(RS * RS), owner] = 1.0
    return pick, spread


def pick_pairs(feats):
    pick = jnp.asarray(pair_tables()[0], jnp.bfloat16)
    return lax.optimization_barrier(product_of("...f,fp->...p", feats, pick).astype(jnp.bfloat16))


def spread_pairs(half):
    spread = jnp.asarray(pair_tables()[1], jnp.bfloat16)
    return lax.optimization_barrier(
        product_of("...pd,fp->...fd", half.astype(jnp.bfloat16), spread).astype(jnp.bfloat16)
    )


def forward_blocks(q_normed, k_normed, values, sign_pair):
    scores = product_of("...id,...jd->...ij", q_normed, k_normed) * DH ** (-0.5)
    weights = jnp.where(causal_mask(), scores**4, 0.0).astype(jnp.bfloat16)
    q_parts = sketch(q_normed, sign_pair)
    k_parts = sketch(k_normed, sign_pair)
    block_kv = product_of("...jr,...jd->...rd", pick_pairs(k_parts[0]), values)
    block_keys = jnp.sum(k_parts[0].astype(jnp.float32), axis=-2)
    return (scores, weights, q_parts, k_parts, block_kv, block_keys)


def before_blocks(block_kv, block_keys, prior_kv, prior_keys):
    key_state = prior_kv[..., None, :, :] + jnp.cumsum(block_kv, axis=-3) - block_kv
    key_total = prior_keys[..., None, :] + jnp.cumsum(block_keys, axis=-2) - block_keys
    return (key_state, key_total)


def after_blocks(block_u, block_w, later_u, later_w):
    rev_u = jnp.flip(jnp.cumsum(jnp.flip(block_u, -3), axis=-3), -3)
    rev_w = jnp.flip(jnp.cumsum(jnp.flip(block_w, -2), axis=-2), -2)
    return (later_u[..., None, :, :] + rev_u - block_u, later_w[..., None, :] + rev_w - block_w)


def finish_forward(weights, values, q_feats, key_state, key_total):
    state_half = key_state
    numerator = product_of("...ij,...jd->...id", weights, values) + product_of(
        "...ir,...rd->...id", q_feats, state_half
    )
    denominator = (
        1.0
        + jnp.sum(weights.astype(jnp.float32), axis=-1)
        + precise_product("...ir,...r->...i", q_feats, key_total)
    )
    return (state_half, numerator, denominator)


def backward_states(grad_in, numerator, denominator, q_feats):
    grad_float = grad_in.astype(jnp.float32)
    scaled_grad = (grad_float / denominator[..., None]).astype(jnp.bfloat16)
    den_grad = -jnp.sum(grad_float * numerator, axis=-1) / (denominator * denominator)
    block_u = product_of("...ir,...id->...rd", pick_pairs(q_feats), scaled_grad)
    block_w = precise_product("...ir,...i->...r", q_feats, den_grad)
    return (scaled_grad, den_grad, block_u, block_w)


def backward_blocks(
    scaled_grad,
    den_grad,
    scores,
    weights,
    values,
    q_normed,
    k_normed,
    state_half,
    key_total,
):
    weight_grad = product_of("...id,...jd->...ij", scaled_grad, values) + den_grad[..., None]
    score_grad = jnp.where(
        causal_mask(), 4.0 * scores**3 * weight_grad * DH ** (-0.5), 0.0
    ).astype(jnp.bfloat16)
    q_diag = product_of("...ij,...jd->...id", score_grad, k_normed)
    k_diag = product_of("...ij,...id->...jd", score_grad, q_normed)
    v_diag = product_of("...ij,...id->...jd", weights, scaled_grad)
    qf_grad = (
        product_of("...id,...rd->...ir", scaled_grad, state_half)
        + den_grad[..., None] * key_total[..., None, :]
    )
    return (q_diag, k_diag, v_diag, qf_grad)


def finish_backward(values, k_feats, later_state, later_total, v_diag):
    later_half = later_state
    kf_grad = product_of("...jd,...rd->...jr", values, later_half) + later_total[..., None, :]
    v_grad = v_diag + product_of("...jr,...rd->...jd", k_feats, later_half)
    return (kf_grad, v_grad)


def normalize(raw, gain, total):
    scale = lax.rsqrt(total / (HEADS * DH) + EPSILON)[:, None]
    return (scale, (raw.astype(jnp.float32) * scale * gain).astype(jnp.bfloat16))


def norm_back(raw, gain, scale, normed_grad, dot_total):
    raw_float = raw.astype(jnp.float32)
    return (
        scale * gain * normed_grad - raw_float * scale**3 * dot_total[:, None] / (HEADS * DH)
    ).astype(jnp.bfloat16)


def on_device(queries, keys, values, out_grad, q_gain, k_gain, signs):
    tok_rows = queries.shape[0]
    heads_here = queries.shape[1] // DH
    block_count = tok_rows // BLOCK
    sign_pair = jnp.concatenate([2 * signs[0] - 1, 2 * signs[1] - 1], axis=1).astype(jnp.bfloat16)
    q_float = queries.astype(jnp.float32)
    k_float = keys.astype(jnp.float32)
    both = jnp.stack([q_float, k_float])
    squares = jnp.sum(both * both, axis=-1)
    (q_total, k_total), _ = head_sum((squares[0], squares[1]), "head")
    q_scale, q_normed = normalize(queries, q_gain, q_total)
    k_scale, k_normed = normalize(keys, k_gain, k_total)

    def split_heads(array):
        return (
            array.reshape(tok_rows, heads_here, DH)
            .transpose(1, 0, 2)
            .reshape(heads_here, block_count, BLOCK, DH)
        )

    def join_heads(array):
        return (
            array.reshape(heads_here, tok_rows, DH)
            .transpose(1, 0, 2)
            .reshape(tok_rows, heads_here * DH)
        )

    q_heads = split_heads(q_normed)
    k_heads = split_heads(k_normed)
    v_heads = split_heads(values)
    g_heads = split_heads(out_grad)
    scores, weights, q_parts, k_parts, block_kv, block_keys = forward_blocks(
        q_heads, k_heads, v_heads, sign_pair
    )
    sum_kv = jnp.sum(block_kv, axis=1)
    sum_keys = jnp.sum(block_keys, axis=1)
    prior_kv, prior_keys, _ = carried_in(sum_kv, sum_keys, "ctx", False)
    key_state, key_total = before_blocks(block_kv, block_keys, prior_kv, prior_keys)
    key_state = spread_pairs(key_state)
    state_half, numerator, denominator = finish_forward(
        weights, v_heads, q_parts[0], key_state, key_total
    )
    scaled_grad, den_grad, block_u, block_w = backward_states(
        g_heads, numerator, denominator, q_parts[0]
    )
    later_u, later_w, (scaled_grad, den_grad, numerator, denominator) = carried_in(
        jnp.sum(block_u, axis=1),
        jnp.sum(block_w, axis=1),
        "ctx",
        True,
        (scaled_grad, den_grad, numerator, denominator),
    )
    attended = (numerator / denominator[..., None]).astype(jnp.bfloat16)
    q_diag, k_diag, v_diag, qf_grad = backward_blocks(
        scaled_grad,
        den_grad,
        scores,
        weights,
        v_heads,
        q_heads,
        k_heads,
        state_half,
        key_total,
    )
    later_state, later_total = after_blocks(block_u, block_w, later_u, later_w)
    later_state = spread_pairs(later_state)
    kf_grad, _ = finish_backward(v_heads, k_parts[0], later_state, later_total, v_diag)
    qn_grad = join_heads(
        q_diag + sketch_back(qf_grad, q_parts[1], q_parts[2], q_parts[3], sign_pair)
    )
    kn_grad = join_heads(
        k_diag + sketch_back(kf_grad, k_parts[1], k_parts[2], k_parts[3], sign_pair)
    )
    dots = jnp.sum(
        jnp.stack([q_float * q_gain * qn_grad, k_float * k_gain * kn_grad]), axis=-1
    )
    (q_dot, k_dot), (v_diag, later_state) = head_sum(
        (dots[0], dots[1]),
        "head",
        (v_diag, later_state),
    )
    _, v_grad = finish_backward(v_heads, k_parts[0], later_state, later_total, v_diag)
    q_grad = norm_back(queries, q_gain, q_scale, qn_grad, q_dot)
    k_grad = norm_back(keys, k_gain, k_scale, kn_grad, k_dot)
    return (join_heads(attended), q_grad, k_grad, join_heads(v_grad).astype(jnp.bfloat16))


def solution(mesh):
    in_specs = (
        P("ctx", "head"),
        P("ctx", "head"),
        P("ctx", "head"),
        P("ctx", "head"),
        P("head"),
        P("head"),
        P(),
    )
    out_specs = (P("ctx", "head"), P("ctx", "head"), P("ctx", "head"), P("ctx", "head"))
    return jax.shard_map(
        on_device, mesh=mesh, in_specs=in_specs, out_specs=out_specs, check_vma=False
    )
```

```python
import numpy as np
import jax
import jax.numpy as jnp
from jax import lax
from jax.sharding import PartitionSpec as P

HEADS = 32
DH = 128
RS = 16
BLOCK = 256


EPSILON = 1e-06
HIGHEST_PREC = lax.Precision.HIGHEST


def shift_rows(rows, step, reverse):
    widths = [(0, 0)] * rows.ndim
    if reverse:
        widths[0] = (0, step)
        return jnp.pad(rows[step:], widths)
    widths[0] = (step, 0)
    return jnp.pad(rows[:-step], widths)


def carried_in(state, totals, axis, reverse, along=()):
    count = lax.axis_size(axis)
    heads_here, rows, lanes = state.shape
    total_rows = totals.shape[1] // lanes
    room = -(-(rows + total_rows) * heads_here // (count * 8)) * 8
    padded = room * count // heads_here
    stacked = jnp.concatenate(
        [
            state,
            totals.reshape(heads_here, total_rows, lanes),
            jnp.zeros((heads_here, padded - rows - total_rows, lanes), state.dtype),
        ],
        axis=1,
    ).reshape(count, room, lanes)
    stacked, along = lax.optimization_barrier((stacked, along))
    mine = lax.all_to_all(stacked, axis, 0, 0, tiled=True)
    shifted = shift_rows(mine, 1, reverse)
    step = 1
    while step < count:
        shifted = shifted + shift_rows(shifted, step, reverse)
        step *= 2
    back = lax.all_to_all(shifted, axis, 0, 0, tiled=True).reshape(heads_here, padded, lanes)
    return (back[:, :rows], back[:, rows : rows + total_rows].reshape(totals.shape), along)


def head_sum(parts, axis, along=()):
    count = lax.axis_size(axis)
    stacked, along = lax.optimization_barrier((jnp.stack(parts), along))
    spread = jnp.broadcast_to(stacked[None], (count,) + stacked.shape)
    gathered = lax.all_to_all(spread, axis, 0, 0, tiled=True)
    summed = jnp.sum(gathered, axis=0)
    return (tuple(summed[i] for i in range(len(parts))), along)


def product_of(spec, lhs, rhs):
    return jnp.einsum(spec, lhs, rhs, preferred_element_type=jnp.float32)


def precise_product(spec, lhs, rhs):
    return jnp.einsum(
        spec, lhs.astype(jnp.float32), rhs.astype(jnp.float32), precision=HIGHEST_PREC
    )


def causal_mask():
    row_ids = lax.broadcasted_iota(jnp.int32, (BLOCK, BLOCK), 0)
    col_ids = lax.broadcasted_iota(jnp.int32, (BLOCK, BLOCK), 1)
    return row_ids >= col_ids


def sketch(inputs, sign_pair):
    projected = product_of("...d,dr->...r", inputs, sign_pair)
    left_part = projected[..., :RS]
    right_part = projected[..., RS:]
    sketched = left_part * right_part * (RS * DH) ** (-0.5)
    outer_prod = sketched[..., :, None] * sketched[..., None, :]
    sketch_feats = outer_prod.reshape(sketched.shape[:-1] + (RS * RS,)).astype(jnp.bfloat16)
    return (sketch_feats, sketched, left_part, right_part)


def sketch_back(feat_grad, sketched, left_part, right_part, sign_pair):
    grid = feat_grad.reshape(feat_grad.shape[:-1] + (RS, RS))
    symmetric = grid + jnp.swapaxes(grid, -1, -2)
    sketch_grad = jnp.sum(symmetric * sketched[..., None, :], axis=-1)
    both_grad = jnp.concatenate([sketch_grad * right_part, sketch_grad * left_part], axis=-1) * (
        RS * DH
    ) ** (-0.5)
    return precise_product("...r,dr->...d", both_grad, sign_pair)


def pair_tables():
    upper = [r * RS + c for r in range(RS) for c in range(r, RS)]
    low = np.minimum.outer(np.arange(RS), np.arange(RS)).reshape(-1)
    high = np.maximum.outer(np.arange(RS), np.arange(RS)).reshape(-1)
    owner = np.array([upper.index(a * RS + b) for a, b in zip(low, high)])
    pick = np.zeros((RS * RS, len(upper)), np.float32)
    pick[upper, np.arange(len(upper))] = 1.0
    spread = np.zeros((RS * RS, len(upper)), np.float32)
    spread[np.arange(RS * RS), owner] = 1.0
    return pick, spread


def pick_pairs(feats):
    pick = jnp.asarray(pair_tables()[0], jnp.bfloat16)
    return lax.optimization_barrier(product_of("...f,fp->...p", feats, pick).astype(jnp.bfloat16))


def spread_pairs(half):
    spread = jnp.asarray(pair_tables()[1], jnp.bfloat16)
    return lax.optimization_barrier(
        product_of("...pd,fp->...fd", half.astype(jnp.bfloat16), spread).astype(jnp.bfloat16)
    )


def forward_blocks(q_normed, k_normed, values, sign_pair):
    scores = product_of("...id,...jd->...ij", q_normed, k_normed) * DH ** (-0.5)
    weights = jnp.where(causal_mask(), scores**4, 0.0).astype(jnp.bfloat16)
    q_parts = sketch(q_normed, sign_pair)
    k_parts = sketch(k_normed, sign_pair)
    block_kv = product_of("...jr,...jd->...rd", pick_pairs(k_parts[0]), values)
    block_keys = jnp.sum(k_parts[0].astype(jnp.float32), axis=-2)
    return (scores, weights, q_parts, k_parts, block_kv, block_keys)


def before_blocks(block_kv, block_keys, prior_kv, prior_keys):
    key_state = prior_kv[..., None, :, :] + jnp.cumsum(block_kv, axis=-3) - block_kv
    key_total = prior_keys[..., None, :] + jnp.cumsum(block_keys, axis=-2) - block_keys
    return (key_state, key_total)


def after_blocks(block_u, block_w, later_u, later_w):
    rev_u = jnp.flip(jnp.cumsum(jnp.flip(block_u, -3), axis=-3), -3)
    rev_w = jnp.flip(jnp.cumsum(jnp.flip(block_w, -2), axis=-2), -2)
    return (later_u[..., None, :, :] + rev_u - block_u, later_w[..., None, :] + rev_w - block_w)


def finish_forward(weights, values, q_feats, key_state, key_total):
    state_half = key_state
    numerator = product_of("...ij,...jd->...id", weights, values) + product_of(
        "...ir,...rd->...id", q_feats, state_half
    )
    denominator = (
        1.0
        + jnp.sum(weights.astype(jnp.float32), axis=-1)
        + precise_product("...ir,...r->...i", q_feats, key_total)
    )
    return (state_half, numerator, denominator)


def backward_states(grad_in, numerator, denominator, q_feats):
    grad_float = grad_in.astype(jnp.float32)
    scaled_grad = (grad_float / denominator[..., None]).astype(jnp.bfloat16)
    den_grad = -jnp.sum(grad_float * numerator, axis=-1) / (denominator * denominator)
    block_u = product_of("...ir,...id->...rd", pick_pairs(q_feats), scaled_grad)
    block_w = precise_product("...ir,...i->...r", q_feats, den_grad)
    return (scaled_grad, den_grad, block_u, block_w)


def backward_blocks(
    scaled_grad,
    den_grad,
    scores,
    weights,
    values,
    q_normed,
    k_normed,
    state_half,
    key_total,
):
    weight_grad = product_of("...id,...jd->...ij", scaled_grad, values) + den_grad[..., None]
    score_grad = jnp.where(
        causal_mask(), 4.0 * scores**3 * weight_grad * DH ** (-0.5), 0.0
    ).astype(jnp.bfloat16)
    q_diag = product_of("...ij,...jd->...id", score_grad, k_normed)
    k_diag = product_of("...ij,...id->...jd", score_grad, q_normed)
    v_diag = product_of("...ij,...id->...jd", weights, scaled_grad)
    qf_grad = (
        product_of("...id,...rd->...ir", scaled_grad, state_half)
        + den_grad[..., None] * key_total[..., None, :]
    )
    return (q_diag, k_diag, v_diag, qf_grad)


def finish_backward(values, k_feats, later_state, later_total, v_diag):
    later_half = later_state
    kf_grad = product_of("...jd,...rd->...jr", values, later_half) + later_total[..., None, :]
    v_grad = v_diag + product_of("...jr,...rd->...jd", k_feats, later_half)
    return (kf_grad, v_grad)


def normalize(raw, gain, total):
    scale = lax.rsqrt(total / (HEADS * DH) + EPSILON)[:, None]
    return (scale, (raw.astype(jnp.float32) * scale * gain).astype(jnp.bfloat16))


def norm_back(raw, gain, scale, normed_grad, dot_total):
    raw_float = raw.astype(jnp.float32)
    return (
        scale * gain * normed_grad - raw_float * scale**3 * dot_total[:, None] / (HEADS * DH)
    ).astype(jnp.bfloat16)


def on_device(queries, keys, values, out_grad, q_gain, k_gain, signs):
    tok_rows = queries.shape[0]
    heads_here = queries.shape[1] // DH
    block_count = tok_rows // BLOCK
    sign_pair = jnp.concatenate([2 * signs[0] - 1, 2 * signs[1] - 1], axis=1).astype(jnp.bfloat16)
    both = jnp.stack([queries, keys]).astype(jnp.float32)
    q_float = both[0]
    k_float = both[1]
    squares = jnp.sum(both * both, axis=-1)
    (q_total, k_total), _ = head_sum((squares[0], squares[1]), "head")
    q_scale, q_normed = normalize(queries, q_gain, q_total)
    k_scale, k_normed = normalize(keys, k_gain, k_total)

    def split_heads(array):
        return (
            array.reshape(tok_rows, heads_here, DH)
            .transpose(1, 0, 2)
            .reshape(heads_here, block_count, BLOCK, DH)
        )

    def join_heads(array):
        return (
            array.reshape(heads_here, tok_rows, DH)
            .transpose(1, 0, 2)
            .reshape(tok_rows, heads_here * DH)
        )

    q_heads = split_heads(q_normed)
    k_heads = split_heads(k_normed)
    v_heads = split_heads(values)
    g_heads = split_heads(out_grad)
    scores, weights, q_parts, k_parts, block_kv, block_keys = forward_blocks(
        q_heads, k_heads, v_heads, sign_pair
    )
    sum_kv = jnp.sum(block_kv, axis=1)
    sum_keys = jnp.sum(block_keys, axis=1)
    prior_kv, prior_keys, _ = carried_in(sum_kv, sum_keys, "ctx", False)
    key_state, key_total = before_blocks(block_kv, block_keys, prior_kv, prior_keys)
    key_state = spread_pairs(key_state)
    state_half, numerator, denominator = finish_forward(
        weights, v_heads, q_parts[0], key_state, key_total
    )
    scaled_grad, den_grad, block_u, block_w = backward_states(
        g_heads, numerator, denominator, q_parts[0]
    )
    later_u, later_w, (scaled_grad, den_grad, numerator, denominator) = carried_in(
        jnp.sum(block_u, axis=1),
        jnp.sum(block_w, axis=1),
        "ctx",
        True,
        (scaled_grad, den_grad, numerator, denominator),
    )
    attended = (numerator / denominator[..., None]).astype(jnp.bfloat16)
    q_diag, k_diag, v_diag, qf_grad = backward_blocks(
        scaled_grad,
        den_grad,
        scores,
        weights,
        v_heads,
        q_heads,
        k_heads,
        state_half,
        key_total,
    )
    later_state, later_total = after_blocks(block_u, block_w, later_u, later_w)
    later_state = spread_pairs(later_state)
    kf_grad, _ = finish_backward(v_heads, k_parts[0], later_state, later_total, v_diag)
    qn_grad = join_heads(
        q_diag + sketch_back(qf_grad, q_parts[1], q_parts[2], q_parts[3], sign_pair)
    )
    kn_grad = join_heads(
        k_diag + sketch_back(kf_grad, k_parts[1], k_parts[2], k_parts[3], sign_pair)
    )
    (q_dot, k_dot), (v_diag, later_state) = head_sum(
        (
            jnp.sum(q_float * q_gain * qn_grad, axis=-1),
            jnp.sum(k_float * k_gain * kn_grad, axis=-1),
        ),
        "head",
        (v_diag, later_state),
    )
    _, v_grad = finish_backward(v_heads, k_parts[0], later_state, later_total, v_diag)
    q_grad = norm_back(queries, q_gain, q_scale, qn_grad, q_dot)
    k_grad = norm_back(keys, k_gain, k_scale, kn_grad, k_dot)
    return (join_heads(attended), q_grad, k_grad, join_heads(v_grad).astype(jnp.bfloat16))


def solution(mesh):
    in_specs = (
        P("ctx", "head"),
        P("ctx", "head"),
        P("ctx", "head"),
        P("ctx", "head"),
        P("head"),
        P("head"),
        P(),
    )
    out_specs = (P("ctx", "head"), P("ctx", "head"), P("ctx", "head"), P("ctx", "head"))
    return jax.shard_map(
        on_device, mesh=mesh, in_specs=in_specs, out_specs=out_specs, check_vma=False
    )
```
